32 devices in a mesh: gx: 4 (over x, core), gy: 8 (over z, y).
Axes of the slice: x: 2, y: 2, z: 4, core: 2. Of those that a mesh axis runs over, the one named last changes fastest.
Arguments:
- flow_state: float32 [6, 128, 16384], P(None, 'gx', 'gy'), may hold values from -6 to 6
- drag_coefficient: float32 [128, 16384], P('gx', 'gy'), may hold values from 0.05 to 0.5
- wet_mask: int32 [128, 16384], P('gx', 'gy'), may hold values 0 or 1
- target_elem: int32 [128, 16384], P('gx', 'gy'), may hold values from 0 to 8191, as said below
- target_node: int32 [128, 16384], P('gx', 'gy'), may hold values from 0 to 24
- displacement: float32 [3, 5, 5, 5, 2, 8, 1024], P(None, None, None, None, None, 'gx', 'gy'), as said below
- previous: float32 [3, 5, 5, 5, 2, 8, 1024], P(None, None, None, None, None, 'gx', 'gy'), as said below
- density: float32 [2, 8, 1024], P(None, 'gx', 'gy'), may hold values from 1 to 3
- lame_first: float32 [2, 8, 1024], P(None, 'gx', 'gy'), may hold values from 1 to 4
- shear_modulus: float32 [2, 8, 1024], P(None, 'gx', 'gy'), may hold values from 0.5 to 2
Outputs:
- flow_final: float32 [6, 128, 16384], P(None, 'gx', 'gy')
- displacement_next: float32 [3, 5, 5, 5, 2, 8, 1024], P(None, None, None, None, None, 'gx', 'gy')
- displacement_last: float32 [3, 5, 5, 5, 2, 8, 1024], P(None, None, None, None, None, 'gx', 'gy')
The draws below stay inside these ranges and needn't reach their ends.
Inputs may be any that keep to these rules, and one draw needn't show every extreme that they name: `target_elem`: each cell's element lies at most one element row and one element column outside the 2 x 128 block of elements that shares the cell's device; the value is element row times 1024 plus element column. `displacement`: a grid point shared by adjacent elements holds the same value in every copy. `previous`: a grid point shared by adjacent elements holds the same value in every copy.
All inputs are finite; a program needn't handle non-finite values. No bound on the sum of `wet_mask` on one device may be relied on, other than what follows from the above.
Results may differ from the reference program's by a relative error of at most 0.00021.
Values sent between devices are 32-bit elements; how exact they have to be, the bound alone decides.
No kernel may reach another device: no remote copies, remote signals or barrier semaphores. Data moves between devices by JAX's collectives and lax.ppermute only.
A program may use at most 192 MiB of HBM per device.

```python
import math
import jax
import jax.numpy as jnp
import numpy as np
from jax import lax

ELZ = 2
CPE = 16
FLOW_STEPS = 4
SOLID_STEPS = 2
EXG = 8
EYG = 1024
SR = 128
SC = 16384


def element_view(grid):
    x_index = jnp.arange(5).reshape(5, 1, 1, 1, 1, 1) + 4 * jnp.arange(EXG).reshape(1, 1, 1, 1, EXG, 1)
    y_index = jnp.arange(5).reshape(1, 5, 1, 1, 1, 1) + 4 * jnp.arange(EYG).reshape(1, 1, 1, 1, 1, EYG)
    z_index = jnp.arange(5).reshape(1, 1, 5, 1, 1, 1) + 4 * jnp.arange(ELZ).reshape(1, 1, 1, ELZ, 1, 1)
    return grid[:, x_index, y_index, z_index]


def consistent_field(key):
    shape = (3, 4 * EXG + 1, 4 * EYG + 1, 4 * ELZ + 1)
    grid = jax.random.normal(key, shape, jnp.float32)
    return element_view(grid).astype(jnp.float32)


def draw_displacement(key, part):
    return consistent_field(jax.random.fold_in(key, 11))


def draw_previous(key, part):
    return consistent_field(jax.random.fold_in(key, 23))


def draw_target_elem(key, part):
    elem_rows = (jnp.arange(SR, dtype=jnp.int32) // CPE)[:, None]
    elem_cols = (jnp.arange(SC, dtype=jnp.int32) // CPE)[None, :]
    jitter_rows = jax.random.randint(jax.random.fold_in(key, 5), (SR, SC), -1, 2)
    jitter_cols = jax.random.randint(jax.random.fold_in(key, 7), (SR, SC), -1, 2)
    rows_hit = jnp.clip(elem_rows + jitter_rows, 0, EXG - 1)
    cols_hit = jnp.clip(elem_cols + jitter_cols, 0, EYG - 1)
    return (rows_hit * EYG + cols_hit).astype(jnp.int32)


def set_ends(entries, rng, least, top_value):
    shape = entries.shape
    index_at = [jax.random.randint(jax.random.fold_in(rng, axis), (), 0, shape[axis]) for axis in range(len(shape))]
    entries = entries.at[tuple(index_at)].set(least)
    longest = shape.index(max(shape))
    index_at[longest] = (index_at[longest] + 1) % shape[longest]
    return entries.at[tuple(index_at)].set(top_value)


def shard_levels(stream_key, shape, cuts, low, top_value):
    factor_of = 1.0
    for dim, parts in cuts:
        heights = jax.random.uniform(jax.random.fold_in(jax.random.fold_in(stream_key, 6), dim), (parts,), jnp.float32, low / len(cuts), top_value / len(cuts))
        factor_of = factor_of * jnp.repeat(jnp.exp(heights), shape[dim] // parts).reshape((-1,) + (1,) * (len(shape) - 1 - dim))
    return factor_of


def gaussian(stream_key, shape, scale, most, shards=(), kind=jnp.bfloat16):
    loudness = shard_levels(stream_key, shape, shards, -0.22, 0.18) if shards else 1.0
    values = jax.random.normal(stream_key, shape, jnp.float32) * scale * loudness
    return jnp.minimum(jnp.maximum(values, -most), most).astype(kind)


def setup_inputs(seed: int = 0) -> dict:
    seeds = jax.random.split(jax.random.key(seed), 11)
    return {
        "flow_state": gaussian(seeds[0], (6, SR, SC), 1.0, 6.0, ((1, 4), (2, 8)), jnp.float32),
        "drag_coefficient": jnp.clip(jnp.exp(math.log(0.5) - 2.3025851 * jax.random.uniform(seeds[1], (SR, SC), jnp.float32) ** shard_levels(seeds[1], (SR, SC), ((0, 4), (1, 8)), -0.2, 0.2)), 0.05, 0.5),
        "wet_mask": set_ends((jax.random.randint(seeds[2], (SR, SC), 0, 2) < 1).astype(jnp.int32), jax.random.fold_in(seeds[2], 1), 0, 1),
        "target_elem": draw_target_elem(jax.random.fold_in(seeds[10], 71), 0),
        "target_node": set_ends(jax.random.randint(seeds[4], (SR, SC), 0, 25), jax.random.fold_in(seeds[4], 1), 0, 24).astype(jnp.int32),
        "displacement": draw_displacement(jax.random.fold_in(seeds[10], 71), 0),
        "previous": draw_previous(jax.random.fold_in(seeds[10], 71), 0),
        "density": jnp.clip(jnp.exp(math.log(3.0) - 1.0986123 * jax.random.uniform(seeds[7], (ELZ, EXG, EYG), jnp.float32) ** shard_levels(seeds[7], (ELZ, EXG, EYG), ((1, 4), (2, 8)), -0.2, 0.2)), 1.0, 3.0),
        "lame_first": jnp.clip(jnp.exp(math.log(4.0) - 1.3862944 * jax.random.uniform(seeds[8], (ELZ, EXG, EYG), jnp.float32) ** shard_levels(seeds[8], (ELZ, EXG, EYG), ((1, 4), (2, 8)), -0.2, 0.2)), 1.0, 4.0),
        "shear_modulus": jnp.clip(jnp.exp(math.log(2.0) - 1.3862944 * jax.random.uniform(seeds[9], (ELZ, EXG, EYG), jnp.float32) ** shard_levels(seeds[9], (ELZ, EXG, EYG), ((1, 4), (2, 8)), -0.2, 0.2)), 0.5, 2.0),
    }


gll_points = np.array([-1.0, -np.sqrt(3.0 / 7.0), 0.0, np.sqrt(3.0 / 7.0), 1.0])
gll_weights = np.array([0.1, 49.0 / 90.0, 32.0 / 45.0, 49.0 / 90.0, 0.1])
flow_dt = 0.4
diffusion = 0.2
coupling = 0.5
upper_gravity = 0.8
density_ratio = 0.7
speed_floor = 0.0001
load_factor = 4.0
solid_dt = 0.04

def legendre_four(x):
    return (35.0 * x ** 4 - 30.0 * x ** 2 + 3.0) / 8.0

def derivative_table():
    result = np.zeros((5, 5))
    for i in range(5):
        for j in range(5):
            if i != j:
                result[i, j] = legendre_four(gll_points[i]) / legendre_four(gll_points[j]) / (gll_points[i] - gll_points[j])
    result[0, 0] = -5.0
    result[4, 4] = 5.0
    return result

def pressures(fields, buoyancy):
    press_one = buoyancy * (fields[0] + fields[1])
    press_two = upper_gravity * (density_ratio * fields[0] + fields[1])
    return jnp.concatenate([fields, press_one[None], press_two[None]], axis=0)

def advance(center, padded, drag_coefficient):
    ahead_x = padded[:, 2:, 1:-1]
    behind_x = padded[:, :-2, 1:-1]
    ahead_y = padded[:, 1:-1, 2:]
    behind_y = padded[:, 1:-1, :-2]
    slope_x = 0.5 * (ahead_x - behind_x)
    slope_y = 0.5 * (ahead_y - behind_y)
    spread = ahead_x + behind_x + ahead_y + behind_y - 4.0 * center
    flow_speed = jnp.sqrt(center[2] * center[2] + center[3] * center[3] + speed_floor)
    dense_depth = center[0] - flow_dt * (slope_x[2] + slope_y[3]) + diffusion * spread[0]
    light_depth = center[1] - flow_dt * (slope_x[4] + slope_y[5]) + diffusion * spread[1]
    dense_xmom = center[2] - flow_dt * (slope_x[6] + drag_coefficient * flow_speed * center[2] + coupling * (center[2] - center[4])) + diffusion * spread[2]
    dense_ymom = center[3] - flow_dt * (slope_y[6] + drag_coefficient * flow_speed * center[3] + coupling * (center[3] - center[5])) + diffusion * spread[3]
    light_xmom = center[4] - flow_dt * (slope_x[7] + coupling * (center[4] - center[2])) + diffusion * spread[4]
    light_ymom = center[5] - flow_dt * (slope_y[7] + coupling * (center[5] - center[3])) + diffusion * spread[5]
    return jnp.stack([dense_depth, light_depth, dense_xmom, dense_ymom, light_xmom, light_ymom])

def basal_traction(fields, buoyancy, drag_coefficient):
    flow_speed = jnp.sqrt(fields[2] * fields[2] + fields[3] * fields[3] + speed_floor)
    press_one = buoyancy * (fields[0] + fields[1])
    rubbing = load_factor * drag_coefficient * flow_speed
    return jnp.stack([rubbing * fields[2], rubbing * fields[3], -load_factor * press_one]).reshape(3, -1)

def weights_cube():
    cube = gll_weights.reshape(5, 1, 1) * gll_weights.reshape(1, 5, 1) * gll_weights.reshape(1, 1, 5)
    return jnp.asarray(cube.reshape(5, 5, 5, 1, 1, 1), jnp.float32)

def internal_force(values, lame_first, shear_modulus):
    highest = lax.Precision.HIGHEST
    table = jnp.asarray(derivative_table(), jnp.float32)
    weights_3d = weights_cube()
    gradients = [jnp.einsum('pa,iabczxy->ipbczxy', table, values, precision=highest), jnp.einsum('pb,iabczxy->iapczxy', table, values, precision=highest), jnp.einsum('pc,iabczxy->iabpzxy', table, values, precision=highest)]
    divergence = gradients[0][0] + gradients[1][1] + gradients[2][2]
    forces = []
    for i in range(3):
        weighted = []
        for j in range(3):
            stress = shear_modulus * (gradients[j][i] + gradients[i][j])
            if i == j:
                stress = stress + lame_first * divergence
            weighted.append(weights_3d * stress)
        pulled = jnp.einsum('pa,pbczxy->abczxy', table, weighted[0], precision=highest)
        pulled = pulled + jnp.einsum('pb,apczxy->abczxy', table, weighted[1], precision=highest)
        pulled = pulled + jnp.einsum('pc,abpzxy->abczxy', table, weighted[2], precision=highest)
        forces.append(-pulled)
    return jnp.stack(forces)

def assemble(values):
    summed = values[:, 4, :, :, :, :-1, :] + values[:, 0, :, :, :, 1:, :]
    values = values.at[:, 4, :, :, :, :-1, :].set(summed).at[:, 0, :, :, :, 1:, :].set(summed)
    summed = values[:, :, 4, :, :, :, :-1] + values[:, :, 0, :, :, :, 1:]
    values = values.at[:, :, 4, :, :, :, :-1].set(summed).at[:, :, 0, :, :, :, 1:].set(summed)
    summed = values[:, :, :, 4, :-1] + values[:, :, :, 0, 1:]
    values = values.at[:, :, :, 4, :-1].set(summed).at[:, :, :, 0, 1:].set(summed)
    return values

def reference(flow_state, drag_coefficient, wet_mask, target_elem, target_node, displacement, previous, density, lame_first, shear_modulus):
    buoyancy = 1.0 - 0.6 * wet_mask.astype(jnp.float32)
    fields = flow_state
    for counter in range(FLOW_STEPS):
        stacked = pressures(fields, buoyancy)
        padded = jnp.pad(stacked, ((0, 0), (1, 1), (1, 1)))
        fields = advance(stacked, padded, drag_coefficient)
    traction = basal_traction(fields, buoyancy, drag_coefficient)
    slot_index = (target_node.reshape(-1) * (EXG * EYG) + target_elem.reshape(-1)).astype(jnp.int32)
    surface_load = jnp.zeros((3, 25 * EXG * EYG), jnp.float32).at[:, slot_index].add(traction)
    surface_load = surface_load.reshape(3, 5, 5, EXG, EYG)
    masses = assemble(density[None, None, None, None] * weights_cube()[None])
    current = displacement
    for counter in range(SOLID_STEPS):
        force = internal_force(current, lame_first, shear_modulus)
        force = force.at[:, :, :, 0, 0].add(surface_load)
        acceleration = assemble(force) / masses
        advanced = 2.0 * current - previous + solid_dt * solid_dt * acceleration
        previous = current
        current = advanced
    return (fields, current, previous)
```

```python
import jax
import jax.numpy as jnp
import numpy as np
from jax import lax
from jax.experimental import pallas as pl
from jax.experimental.pallas import tpu as pltpu
from jax.sharding import PartitionSpec as P

FLOW_STEPS = 4
SOLID_STEPS = 2


gll_points = np.array([-1.0, -np.sqrt(3.0 / 7.0), 0.0, np.sqrt(3.0 / 7.0), 1.0])
gll_weights = np.array([0.1, 49.0 / 90.0, 32.0 / 45.0, 49.0 / 90.0, 0.1])
flow_dt = 0.4
diffusion = 0.2
coupling = 0.5
upper_gravity = 0.8
density_ratio = 0.7
speed_floor = 0.0001
load_factor = 4.0
solid_dt = 0.04

NODE_PAD = 32
CHUNK = 1024
ROW_BLOCK = 8


def extended(block, sides, width):
    for axis, dim in sides:
        count = lax.axis_size(axis)
        forward = [(i, i + 1) for i in range(count - 1)]
        backward = [(target, source) for source, target in forward]
        low = lax.ppermute(
            lax.slice_in_dim(block, block.shape[dim] - width, None, axis=dim), axis, forward
        )
        high = lax.ppermute(lax.slice_in_dim(block, 0, width, axis=dim), axis, backward)
        block = jnp.concatenate([low, block, high], axis=dim)
    return block


def legendre_four(x):
    return (35.0 * x**4 - 30.0 * x**2 + 3.0) / 8.0


def derivative_table():
    result = np.zeros((5, 5))
    for i in range(5):
        for j in range(5):
            if i != j:
                result[i, j] = (
                    legendre_four(gll_points[i])
                    / legendre_four(gll_points[j])
                    / (gll_points[i] - gll_points[j])
                )
    result[0, 0] = -5.0
    result[4, 4] = 5.0
    return result


TABLE = derivative_table().astype(np.float32)


def pressures(fields, buoyancy):
    press_one = buoyancy * (fields[0] + fields[1])
    press_two = upper_gravity * (density_ratio * fields[0] + fields[1])
    return jnp.concatenate([fields, press_one[None], press_two[None]], axis=0)


def advance(center, padded, drag_coefficient):
    ahead_x = padded[:, 2:, 1:-1]
    behind_x = padded[:, :-2, 1:-1]
    ahead_y = padded[:, 1:-1, 2:]
    behind_y = padded[:, 1:-1, :-2]
    slope_x = 0.5 * (ahead_x - behind_x)
    slope_y = 0.5 * (ahead_y - behind_y)
    spread = ahead_x + behind_x + ahead_y + behind_y - 4.0 * center
    flow_speed = jnp.sqrt(center[2] * center[2] + center[3] * center[3] + speed_floor)
    dense_depth = center[0] - flow_dt * (slope_x[2] + slope_y[3]) + diffusion * spread[0]
    light_depth = center[1] - flow_dt * (slope_x[4] + slope_y[5]) + diffusion * spread[1]
    dense_xmom = (
        center[2]
        - flow_dt
        * (
            slope_x[6]
            + drag_coefficient * flow_speed * center[2]
            + coupling * (center[2] - center[4])
        )
        + diffusion * spread[2]
    )
    dense_ymom = (
        center[3]
        - flow_dt
        * (
            slope_y[6]
            + drag_coefficient * flow_speed * center[3]
            + coupling * (center[3] - center[5])
        )
        + diffusion * spread[3]
    )
    light_xmom = (
        center[4]
        - flow_dt * (slope_x[7] + coupling * (center[4] - center[2]))
        + diffusion * spread[4]
    )
    light_ymom = (
        center[5]
        - flow_dt * (slope_y[7] + coupling * (center[5] - center[3]))
        + diffusion * spread[5]
    )
    return jnp.stack([dense_depth, light_depth, dense_xmom, dense_ymom, light_xmom, light_ymom])


def basal_traction(fields, buoyancy, drag_coefficient):
    flow_speed = jnp.sqrt(fields[2] * fields[2] + fields[3] * fields[3] + speed_floor)
    press_one = buoyancy * (fields[0] + fields[1])
    rubbing = load_factor * drag_coefficient * flow_speed
    return jnp.stack([rubbing * fields[2], rubbing * fields[3], -load_factor * press_one])


def weights_cube():
    cube = (
        gll_weights.reshape(5, 1, 1) * gll_weights.reshape(1, 5, 1) * gll_weights.reshape(1, 1, 5)
    )
    return jnp.asarray(cube.reshape(5, 5, 5, 1, 1, 1), jnp.float32)


def load_kernel(trac_ref, node_ref, slot_ref, out_ref):
    slots = out_ref.shape[0]

    @pl.when(pl.program_id(0) == 0)
    def _():
        out_ref[...] = jnp.zeros(out_ref.shape, out_ref.dtype)

    def row_body(r, carry):
        for c0 in range(0, node_ref.shape[1], CHUNK):
            node = node_ref[pl.ds(r, 1), pl.ds(c0, CHUNK)]
            slot = slot_ref[pl.ds(r, 1), pl.ds(c0, CHUNK)]
            hit = lax.broadcasted_iota(jnp.int32, (NODE_PAD, CHUNK), 0) == node
            pieces = []
            for k in range(3):
                value = trac_ref[k, pl.ds(r, 1), pl.ds(c0, CHUNK)]
                high = value.astype(jnp.bfloat16).astype(jnp.float32)
                low = value - high
                pieces.append(jnp.where(hit, high, 0.0))
                pieces.append(jnp.where(hit, low, 0.0))
            weighted = jnp.concatenate(pieces, axis=0).astype(jnp.bfloat16)
            onehot = (
                lax.broadcasted_iota(jnp.int32, (slots, CHUNK), 0) == slot
            ).astype(jnp.bfloat16)
            out_ref[...] += lax.dot_general(
                onehot,
                weighted,
                (((1,), (1,)), ((), ())),
                preferred_element_type=jnp.float32,
            )
        return carry

    lax.fori_loop(0, ROW_BLOCK, row_body, 0)


def load_table(trac, node, slot, slots):
    rows, cols = node.shape
    return pl.pallas_call(
        load_kernel,
        grid=(rows // ROW_BLOCK,),
        in_specs=[
            pl.BlockSpec((3, ROW_BLOCK, cols), lambda g: (0, g, 0)),
            pl.BlockSpec((ROW_BLOCK, cols), lambda g: (g, 0)),
            pl.BlockSpec((ROW_BLOCK, cols), lambda g: (g, 0)),
        ],
        out_specs=pl.BlockSpec((slots, 6 * NODE_PAD), lambda g: (0, 0)),
        out_shape=jax.ShapeDtypeStruct((slots, 6 * NODE_PAD), jnp.float32),
        compiler_params=pltpu.CompilerParams(dimension_semantics=("arbitrary",)),
    )(trac, node, slot)


def along(x, axis, transpose):
    parts = [lax.index_in_dim(x, a, axis, keepdims=False) for a in range(5)]
    outs = []
    for p in range(5):
        total = None
        for a in range(5):
            coef = float(TABLE[a, p]) if transpose else float(TABLE[p, a])
            if coef == 0.0:
                continue
            term = coef * parts[a]
            total = term if total is None else total + term
        outs.append(total)
    return jnp.stack(outs, axis=axis)


def internal_force(values, lame_first, shear_modulus):
    weights_3d = weights_cube()
    gradients = [[along(values[i], j, False) for i in range(3)] for j in range(3)]
    divergence = gradients[0][0] + gradients[1][1] + gradients[2][2]
    forces = []
    for i in range(3):
        pulled = None
        for j in range(3):
            stress = shear_modulus * (gradients[j][i] + gradients[i][j])
            if i == j:
                stress = stress + lame_first * divergence
            term = along(weights_3d * stress, j, True)
            pulled = term if pulled is None else pulled + term
        forces.append(-pulled)
    return jnp.stack(forces)


def shift_faces(low_face, high_face, dim, axis):
    count = lax.axis_size(axis)
    forward = [(i, i + 1) for i in range(count - 1)]
    backward = [(target, source) for source, target in forward]
    size = low_face.shape[dim]
    from_prev = lax.ppermute(lax.slice_in_dim(high_face, size - 1, size, axis=dim), axis, forward)
    from_next = lax.ppermute(lax.slice_in_dim(low_face, 0, 1, axis=dim), axis, backward)
    before = jnp.concatenate([from_prev, lax.slice_in_dim(high_face, 0, size - 1, axis=dim)], axis=dim)
    after = jnp.concatenate([lax.slice_in_dim(low_face, 1, size, axis=dim), from_next], axis=dim)
    return before, after


def assemble_dim(values, node_dim, elem_dim, axis):
    low_face = lax.index_in_dim(values, 0, node_dim, keepdims=False)
    high_face = lax.index_in_dim(values, 4, node_dim, keepdims=False)
    face_elem_dim = elem_dim - 1
    if axis is None:
        size = low_face.shape[face_elem_dim]
        zero = jnp.zeros_like(lax.slice_in_dim(low_face, 0, 1, axis=face_elem_dim))
        before = jnp.concatenate(
            [zero, lax.slice_in_dim(high_face, 0, size - 1, axis=face_elem_dim)], axis=face_elem_dim
        )
        after = jnp.concatenate(
            [lax.slice_in_dim(low_face, 1, size, axis=face_elem_dim), zero], axis=face_elem_dim
        )
    else:
        before, after = shift_faces(low_face, high_face, face_elem_dim, axis)
    new_low = jnp.expand_dims(low_face + before, node_dim)
    new_high = jnp.expand_dims(high_face + after, node_dim)
    middle = lax.slice_in_dim(values, 1, 4, axis=node_dim)
    return jnp.concatenate([new_low, middle, new_high], axis=node_dim)


def assemble(values):
    values = assemble_dim(values, 1, 5, "gx")
    values = assemble_dim(values, 2, 6, "gy")
    values = assemble_dim(values, 3, 4, None)
    return values


def per_device(
    flow_state,
    drag_coefficient,
    wet_mask,
    target_elem,
    target_node,
    displacement,
    previous,
    density,
    lame_first,
    shear_modulus,
):
    buoyancy = 1.0 - 0.6 * wet_mask.astype(jnp.float32)
    fields = flow_state
    depth = FLOW_STEPS
    cell_rows = fields.shape[1]
    cell_cols = fields.shape[2]
    bundle = jnp.concatenate([fields, buoyancy[None], drag_coefficient[None]], axis=0)
    widened = extended(bundle, (("gx", 1), ("gy", 2)), depth)
    row_ids = lax.axis_index("gx") * cell_rows + jnp.arange(cell_rows + 2 * depth) - depth
    col_ids = lax.axis_index("gy") * cell_cols + jnp.arange(cell_cols + 2 * depth) - depth
    row_inside = (row_ids >= 0) & (row_ids < cell_rows * lax.axis_size("gx"))
    col_inside = (col_ids >= 0) & (col_ids < cell_cols * lax.axis_size("gy"))
    inside = (row_inside[:, None] & col_inside[None, :]).astype(jnp.float32)
    wide_fields = widened[:6]
    wide_buoyancy = widened[6]
    wide_drag = widened[7]
    for counter in range(FLOW_STEPS):
        stacked = pressures(wide_fields, wide_buoyancy)
        padded = jnp.pad(stacked, ((0, 0), (1, 1), (1, 1)))
        wide_fields = advance(stacked, padded, wide_drag) * inside[None]
    fields = wide_fields[:, depth : depth + cell_rows, depth : depth + cell_cols]
    traction = basal_traction(fields, buoyancy, drag_coefficient)
    block_rows = displacement.shape[5]
    block_cols = displacement.shape[6]
    devices_y = lax.axis_size("gy")
    surface_cols = block_cols * devices_y
    elem_row = target_elem // surface_cols
    elem_col = target_elem % surface_cols
    local_x = elem_row - block_rows * lax.axis_index("gx") + 1
    local_y = elem_col - block_cols * lax.axis_index("gy") + 1
    slot_index = local_x * (block_cols + 2) + local_y
    wide_slots = (block_rows + 2) * (block_cols + 2)
    slots = -(-wide_slots // 16) * 16
    table = load_table(traction, target_node, slot_index, slots)
    table = table[:wide_slots].reshape(wide_slots, 3, 2, NODE_PAD)
    table = (table[:, :, 0] + table[:, :, 1])[:, :, :25]
    table = jnp.transpose(table, (1, 2, 0)).reshape(3, 25, block_rows + 2, block_cols + 2)
    beyond = extended(table, (("gx", 2), ("gy", 3)), 1)
    rows_folded = (
        beyond[:, :, 2 : 2 + block_rows]
        + jnp.pad(beyond[:, :, 0:1], ((0, 0), (0, 0), (0, block_rows - 1), (0, 0)))
        + jnp.pad(beyond[:, :, -1:], ((0, 0), (0, 0), (block_rows - 1, 0), (0, 0)))
    )
    own_loads = (
        rows_folded[:, :, :, 2 : 2 + block_cols]
        + jnp.pad(rows_folded[:, :, :, 0:1], ((0, 0), (0, 0), (0, 0), (0, block_cols - 1)))
        + jnp.pad(rows_folded[:, :, :, -1:], ((0, 0), (0, 0), (0, 0), (block_cols - 1, 0)))
    )
    surface_load = own_loads.reshape(3, 5, 5, 1, 1, block_rows, block_cols)
    layers = displacement.shape[4]
    load_padded = jnp.pad(
        surface_load,
        ((0, 0), (0, 0), (0, 0), (0, 4), (0, layers - 1), (0, 0), (0, 0)),
    )
    masses = assemble(density[None, None, None, None] * weights_cube()[None])
    current = displacement
    for counter in range(SOLID_STEPS):
        force = internal_force(current, lame_first, shear_modulus) + load_padded
        acceleration = assemble(force) / masses
        advanced = 2.0 * current - previous + solid_dt * solid_dt * acceleration
        previous = current
        current = advanced
    return (fields, current, previous)


def solution(mesh):
    return jax.shard_map(
        per_device,
        mesh=mesh,
        in_specs=(
            P(None, "gx", "gy"),
            P("gx", "gy"),
            P("gx", "gy"),
            P("gx", "gy"),
            P("gx", "gy"),
            P(None, None, None, None, None, "gx", "gy"),
            P(None, None, None, None, None, "gx", "gy"),
            P(None, "gx", "gy"),
            P(None, "gx", "gy"),
            P(None, "gx", "gy"),
        ),
        out_specs=(
            P(None, "gx", "gy"),
            P(None, None, None, None, None, "gx", "gy"),
            P(None, None, None, None, None, "gx", "gy"),
        ),
        check_vma=False,
    )
```

```python
import jax
import jax.numpy as jnp
import numpy as np
from jax import lax
from jax.experimental import pallas as pl
from jax.experimental.pallas import tpu as pltpu
from jax.sharding import PartitionSpec as P

FLOW_STEPS = 4
SOLID_STEPS = 2


gll_points = np.array([-1.0, -np.sqrt(3.0 / 7.0), 0.0, np.sqrt(3.0 / 7.0), 1.0])
gll_weights = np.array([0.1, 49.0 / 90.0, 32.0 / 45.0, 49.0 / 90.0, 0.1])
flow_dt = 0.4
diffusion = 0.2
coupling = 0.5
upper_gravity = 0.8
density_ratio = 0.7
speed_floor = 0.0001
load_factor = 4.0
solid_dt = 0.04

NODE_PAD = 32
CHUNK = 1024
ROW_BLOCK = 8


def extended(block, sides, width):
    for axis, dim in sides:
        count = lax.axis_size(axis)
        forward = [(i, i + 1) for i in range(count - 1)]
        backward = [(target, source) for source, target in forward]
        low = lax.ppermute(
            lax.slice_in_dim(block, block.shape[dim] - width, None, axis=dim), axis, forward
        )
        high = lax.ppermute(lax.slice_in_dim(block, 0, width, axis=dim), axis, backward)
        block = jnp.concatenate([low, block, high], axis=dim)
    return block


def legendre_four(x):
    return (35.0 * x**4 - 30.0 * x**2 + 3.0) / 8.0


def derivative_table():
    result = np.zeros((5, 5))
    for i in range(5):
        for j in range(5):
            if i != j:
                result[i, j] = (
                    legendre_four(gll_points[i])
                    / legendre_four(gll_points[j])
                    / (gll_points[i] - gll_points[j])
                )
    result[0, 0] = -5.0
    result[4, 4] = 5.0
    return result


TABLE = derivative_table().astype(np.float32)


def pressures(fields, buoyancy):
    press_one = buoyancy * (fields[0] + fields[1])
    press_two = upper_gravity * (density_ratio * fields[0] + fields[1])
    return jnp.concatenate([fields, press_one[None], press_two[None]], axis=0)


def advance(center, padded, drag_coefficient):
    ahead_x = padded[:, 2:, 1:-1]
    behind_x = padded[:, :-2, 1:-1]
    ahead_y = padded[:, 1:-1, 2:]
    behind_y = padded[:, 1:-1, :-2]
    slope_x = 0.5 * (ahead_x - behind_x)
    slope_y = 0.5 * (ahead_y - behind_y)
    spread = ahead_x + behind_x + ahead_y + behind_y - 4.0 * center
    flow_speed = jnp.sqrt(center[2] * center[2] + center[3] * center[3] + speed_floor)
    dense_depth = center[0] - flow_dt * (slope_x[2] + slope_y[3]) + diffusion * spread[0]
    light_depth = center[1] - flow_dt * (slope_x[4] + slope_y[5]) + diffusion * spread[1]
    dense_xmom = (
        center[2]
        - flow_dt
        * (
            slope_x[6]
            + drag_coefficient * flow_speed * center[2]
            + coupling * (center[2] - center[4])
        )
        + diffusion * spread[2]
    )
    dense_ymom = (
        center[3]
        - flow_dt
        * (
            slope_y[6]
            + drag_coefficient * flow_speed * center[3]
            + coupling * (center[3] - center[5])
        )
        + diffusion * spread[3]
    )
    light_xmom = (
        center[4]
        - flow_dt * (slope_x[7] + coupling * (center[4] - center[2]))
        + diffusion * spread[4]
    )
    light_ymom = (
        center[5]
        - flow_dt * (slope_y[7] + coupling * (center[5] - center[3]))
        + diffusion * spread[5]
    )
    return jnp.stack([dense_depth, light_depth, dense_xmom, dense_ymom, light_xmom, light_ymom])


def basal_traction(fields, buoyancy, drag_coefficient):
    flow_speed = jnp.sqrt(fields[2] * fields[2] + fields[3] * fields[3] + speed_floor)
    press_one = buoyancy * (fields[0] + fields[1])
    rubbing = load_factor * drag_coefficient * flow_speed
    return jnp.stack([rubbing * fields[2], rubbing * fields[3], -load_factor * press_one])


def weights_cube():
    cube = (
        gll_weights.reshape(5, 1, 1) * gll_weights.reshape(1, 5, 1) * gll_weights.reshape(1, 1, 5)
    )
    return jnp.asarray(cube.reshape(5, 5, 5, 1, 1, 1), jnp.float32)


def load_kernel(trac_ref, node_ref, slot_ref, out_ref):
    slots = out_ref.shape[0]

    @pl.when(pl.program_id(0) == 0)
    def _():
        out_ref[...] = jnp.zeros(out_ref.shape, out_ref.dtype)

    def row_body(r, carry):
        for c0 in range(0, node_ref.shape[1], CHUNK):
            node = node_ref[pl.ds(r, 1), pl.ds(c0, CHUNK)]
            slot = slot_ref[pl.ds(r, 1), pl.ds(c0, CHUNK)]
            hit = lax.broadcasted_iota(jnp.int32, (NODE_PAD, CHUNK), 0) == node
            pieces = []
            for k in range(3):
                value = trac_ref[k, pl.ds(r, 1), pl.ds(c0, CHUNK)]
                high = value.astype(jnp.bfloat16).astype(jnp.float32)
                low = value - high
                pieces.append(jnp.where(hit, high, 0.0))
                pieces.append(jnp.where(hit, low, 0.0))
            weighted = jnp.concatenate(pieces, axis=0).astype(jnp.bfloat16)
            onehot = (
                lax.broadcasted_iota(jnp.int32, (slots, CHUNK), 0) == slot
            ).astype(jnp.bfloat16)
            out_ref[...] += lax.dot_general(
                onehot,
                weighted,
                (((1,), (1,)), ((), ())),
                preferred_element_type=jnp.float32,
            )
        return carry

    lax.fori_loop(0, ROW_BLOCK, row_body, 0)


def load_table(trac, node, slot, slots):
    rows, cols = node.shape
    return pl.pallas_call(
        load_kernel,
        grid=(rows // ROW_BLOCK,),
        in_specs=[
            pl.BlockSpec((3, ROW_BLOCK, cols), lambda g: (0, g, 0)),
            pl.BlockSpec((ROW_BLOCK, cols), lambda g: (g, 0)),
            pl.BlockSpec((ROW_BLOCK, cols), lambda g: (g, 0)),
        ],
        out_specs=pl.BlockSpec((slots, 6 * NODE_PAD), lambda g: (0, 0)),
        out_shape=jax.ShapeDtypeStruct((slots, 6 * NODE_PAD), jnp.float32),
        compiler_params=pltpu.CompilerParams(dimension_semantics=("arbitrary",)),
    )(trac, node, slot)


def along(x, axis, transpose):
    table = TABLE.T if transpose else TABLE
    shape = [1] * (x.ndim + 1)
    shape[axis] = 5
    shape[axis + 1] = 5
    coefs = jnp.asarray(table.reshape(shape))
    return jnp.sum(coefs * jnp.expand_dims(x, axis), axis=axis + 1)


def internal_force(values, lame_first, shear_modulus):
    weights_3d = weights_cube()
    gradients = [[along(values[i], j, False) for i in range(3)] for j in range(3)]
    divergence = gradients[0][0] + gradients[1][1] + gradients[2][2]
    forces = []
    for i in range(3):
        pulled = None
        for j in range(3):
            stress = shear_modulus * (gradients[j][i] + gradients[i][j])
            if i == j:
                stress = stress + lame_first * divergence
            term = along(weights_3d * stress, j, True)
            pulled = term if pulled is None else pulled + term
        forces.append(-pulled)
    return jnp.stack(forces)


def shift_faces(low_face, high_face, dim, axis):
    count = lax.axis_size(axis)
    forward = [(i, i + 1) for i in range(count - 1)]
    backward = [(target, source) for source, target in forward]
    size = low_face.shape[dim]
    from_prev = lax.ppermute(lax.slice_in_dim(high_face, size - 1, size, axis=dim), axis, forward)
    from_next = lax.ppermute(lax.slice_in_dim(low_face, 0, 1, axis=dim), axis, backward)
    before = jnp.concatenate([from_prev, lax.slice_in_dim(high_face, 0, size - 1, axis=dim)], axis=dim)
    after = jnp.concatenate([lax.slice_in_dim(low_face, 1, size, axis=dim), from_next], axis=dim)
    return before, after


def assemble_dim(values, node_dim, elem_dim, axis):
    low_face = lax.index_in_dim(values, 0, node_dim, keepdims=False)
    high_face = lax.index_in_dim(values, 4, node_dim, keepdims=False)
    face_elem_dim = elem_dim - 1
    if axis is None:
        size = low_face.shape[face_elem_dim]
        zero = jnp.zeros_like(lax.slice_in_dim(low_face, 0, 1, axis=face_elem_dim))
        before = jnp.concatenate(
            [zero, lax.slice_in_dim(high_face, 0, size - 1, axis=face_elem_dim)], axis=face_elem_dim
        )
        after = jnp.concatenate(
            [lax.slice_in_dim(low_face, 1, size, axis=face_elem_dim), zero], axis=face_elem_dim
        )
    else:
        before, after = shift_faces(low_face, high_face, face_elem_dim, axis)
    new_low = jnp.expand_dims(low_face + before, node_dim)
    new_high = jnp.expand_dims(high_face + after, node_dim)
    middle = lax.slice_in_dim(values, 1, 4, axis=node_dim)
    return jnp.concatenate([new_low, middle, new_high], axis=node_dim)


def assemble(values):
    values = assemble_dim(values, 1, 5, "gx")
    values = assemble_dim(values, 2, 6, "gy")
    values = assemble_dim(values, 3, 4, None)
    return values


def per_device(
    flow_state,
    drag_coefficient,
    wet_mask,
    target_elem,
    target_node,
    displacement,
    previous,
    density,
    lame_first,
    shear_modulus,
):
    buoyancy = 1.0 - 0.6 * wet_mask.astype(jnp.float32)
    fields = flow_state
    depth = FLOW_STEPS
    cell_rows = fields.shape[1]
    cell_cols = fields.shape[2]
    bundle = jnp.concatenate([fields, buoyancy[None], drag_coefficient[None]], axis=0)
    widened = extended(bundle, (("gx", 1), ("gy", 2)), depth)
    row_ids = lax.axis_index("gx") * cell_rows + jnp.arange(cell_rows + 2 * depth) - depth
    col_ids = lax.axis_index("gy") * cell_cols + jnp.arange(cell_cols + 2 * depth) - depth
    row_inside = (row_ids >= 0) & (row_ids < cell_rows * lax.axis_size("gx"))
    col_inside = (col_ids >= 0) & (col_ids < cell_cols * lax.axis_size("gy"))
    inside = (row_inside[:, None] & col_inside[None, :]).astype(jnp.float32)
    wide_fields = widened[:6]
    wide_buoyancy = widened[6]
    wide_drag = widened[7]
    for counter in range(FLOW_STEPS):
        stacked = pressures(wide_fields, wide_buoyancy)
        padded = jnp.pad(stacked, ((0, 0), (1, 1), (1, 1)))
        wide_fields = advance(stacked, padded, wide_drag) * inside[None]
    fields = wide_fields[:, depth : depth + cell_rows, depth : depth + cell_cols]
    traction = basal_traction(fields, buoyancy, drag_coefficient)
    block_rows = displacement.shape[5]
    block_cols = displacement.shape[6]
    devices_y = lax.axis_size("gy")
    surface_cols = block_cols * devices_y
    elem_row = target_elem // surface_cols
    elem_col = target_elem % surface_cols
    local_x = elem_row - block_rows * lax.axis_index("gx") + 1
    local_y = elem_col - block_cols * lax.axis_index("gy") + 1
    slot_index = local_x * (block_cols + 2) + local_y
    wide_slots = (block_rows + 2) * (block_cols + 2)
    slots = -(-wide_slots // 16) * 16
    table = load_table(traction, target_node, slot_index, slots)
    table = table[:wide_slots].reshape(wide_slots, 3, 2, NODE_PAD)
    table = (table[:, :, 0] + table[:, :, 1])[:, :, :25]
    table = jnp.transpose(table, (1, 2, 0)).reshape(3, 25, block_rows + 2, block_cols + 2)
    beyond = extended(table, (("gx", 2), ("gy", 3)), 1)
    rows_folded = (
        beyond[:, :, 2 : 2 + block_rows]
        + jnp.pad(beyond[:, :, 0:1], ((0, 0), (0, 0), (0, block_rows - 1), (0, 0)))
        + jnp.pad(beyond[:, :, -1:], ((0, 0), (0, 0), (block_rows - 1, 0), (0, 0)))
    )
    own_loads = (
        rows_folded[:, :, :, 2 : 2 + block_cols]
        + jnp.pad(rows_folded[:, :, :, 0:1], ((0, 0), (0, 0), (0, 0), (0, block_cols - 1)))
        + jnp.pad(rows_folded[:, :, :, -1:], ((0, 0), (0, 0), (0, 0), (block_cols - 1, 0)))
    )
    surface_load = own_loads.reshape(3, 5, 5, 1, 1, block_rows, block_cols)
    layers = displacement.shape[4]
    load_padded = jnp.pad(
        surface_load,
        ((0, 0), (0, 0), (0, 0), (0, 4), (0, layers - 1), (0, 0), (0, 0)),
    )
    masses = assemble(density[None, None, None, None] * weights_cube()[None])
    current = displacement
    for counter in range(SOLID_STEPS):
        force = internal_force(current, lame_first, shear_modulus) + load_padded
        acceleration = assemble(force) / masses
        advanced = 2.0 * current - previous + solid_dt * solid_dt * acceleration
        previous = current
        current = advanced
    return (fields, current, previous)


def solution(mesh):
    return jax.shard_map(
        per_device,
        mesh=mesh,
        in_specs=(
            P(None, "gx", "gy"),
            P("gx", "gy"),
            P("gx", "gy"),
            P("gx", "gy"),
            P("gx", "gy"),
            P(None, None, None, None, None, "gx", "gy"),
            P(None, None, None, None, None, "gx", "gy"),
            P(None, "gx", "gy"),
            P(None, "gx", "gy"),
            P(None, "gx", "gy"),
        ),
        out_specs=(
            P(None, "gx", "gy"),
            P(None, None, None, None, None, "gx", "gy"),
            P(None, None, None, None, None, "gx", "gy"),
        ),
        check_vma=False,
    )
```

```python
import jax
import jax.numpy as jnp
import numpy as np
from jax import lax
from jax.experimental import pallas as pl
from jax.experimental.pallas import tpu as pltpu
from jax.sharding import PartitionSpec as P

FLOW_STEPS = 4
SOLID_STEPS = 2


gll_points = np.array([-1.0, -np.sqrt(3.0 / 7.0), 0.0, np.sqrt(3.0 / 7.0), 1.0])
gll_weights = np.array([0.1, 49.0 / 90.0, 32.0 / 45.0, 49.0 / 90.0, 0.1])
flow_dt = 0.4
diffusion = 0.2
coupling = 0.5
upper_gravity = 0.8
density_ratio = 0.7
speed_floor = 0.0001
load_factor = 4.0
solid_dt = 0.04

NODE_PAD = 32
CHUNK = 1024
ROW_BLOCK = 8


def send(block, axes, offsets):
    sizes = [lax.axis_size(axis) for axis in axes]
    pairs = []
    for source in np.ndindex(*sizes):
        target = tuple(s + o for s, o in zip(source, offsets))
        if all(0 <= t < n for t, n in zip(target, sizes)):
            pairs.append((int(np.ravel_multi_index(source, sizes)), int(np.ravel_multi_index(target, sizes))))
    count = block.size
    lanes = -(-count // 1024) * 1024
    flat = jnp.pad(block.reshape(-1), (0, lanes - count)).reshape(lanes // 128, 128)
    moved = lax.ppermute(flat, tuple(axes) if len(axes) > 1 else axes[0], pairs)
    return moved.reshape(-1)[:count].reshape(block.shape)


def halo(block, width):
    rows = block.shape[-2]
    cols = block.shape[-1]
    both = ("gx", "gy")
    top = lax.slice_in_dim(block, 0, width, axis=-2)
    bottom = lax.slice_in_dim(block, rows - width, rows, axis=-2)
    left = lax.slice_in_dim(block, 0, width, axis=-1)
    right = lax.slice_in_dim(block, cols - width, cols, axis=-1)
    from_up = send(bottom, ("gx",), (1,))
    from_down = send(top, ("gx",), (-1,))
    from_left = send(right, ("gy",), (1,))
    from_right = send(left, ("gy",), (-1,))
    corner_ul = send(lax.slice_in_dim(bottom, cols - width, cols, axis=-1), both, (1, 1))
    corner_ur = send(lax.slice_in_dim(bottom, 0, width, axis=-1), both, (1, -1))
    corner_dl = send(lax.slice_in_dim(top, cols - width, cols, axis=-1), both, (-1, 1))
    corner_dr = send(lax.slice_in_dim(top, 0, width, axis=-1), both, (-1, -1))
    return jnp.concatenate(
        [
            jnp.concatenate([corner_ul, from_up, corner_ur], axis=-1),
            jnp.concatenate([from_left, block, from_right], axis=-1),
            jnp.concatenate([corner_dl, from_down, corner_dr], axis=-1),
        ],
        axis=-2,
    )


def legendre_four(x):
    return (35.0 * x**4 - 30.0 * x**2 + 3.0) / 8.0


def derivative_table():
    result = np.zeros((5, 5))
    for i in range(5):
        for j in range(5):
            if i != j:
                result[i, j] = (
                    legendre_four(gll_points[i])
                    / legendre_four(gll_points[j])
                    / (gll_points[i] - gll_points[j])
                )
    result[0, 0] = -5.0
    result[4, 4] = 5.0
    return result


TABLE = derivative_table().astype(np.float32)


def pressures(fields, buoyancy):
    press_one = buoyancy * (fields[0] + fields[1])
    press_two = upper_gravity * (density_ratio * fields[0] + fields[1])
    return jnp.concatenate([fields, press_one[None], press_two[None]], axis=0)


def advance(center, padded, drag_coefficient):
    ahead_x = padded[:, 2:, 1:-1]
    behind_x = padded[:, :-2, 1:-1]
    ahead_y = padded[:, 1:-1, 2:]
    behind_y = padded[:, 1:-1, :-2]
    slope_x = 0.5 * (ahead_x - behind_x)
    slope_y = 0.5 * (ahead_y - behind_y)
    spread = ahead_x + behind_x + ahead_y + behind_y - 4.0 * center
    flow_speed = jnp.sqrt(center[2] * center[2] + center[3] * center[3] + speed_floor)
    dense_depth = center[0] - flow_dt * (slope_x[2] + slope_y[3]) + diffusion * spread[0]
    light_depth = center[1] - flow_dt * (slope_x[4] + slope_y[5]) + diffusion * spread[1]
    dense_xmom = (
        center[2]
        - flow_dt
        * (
            slope_x[6]
            + drag_coefficient * flow_speed * center[2]
            + coupling * (center[2] - center[4])
        )
        + diffusion * spread[2]
    )
    dense_ymom = (
        center[3]
        - flow_dt
        * (
            slope_y[6]
            + drag_coefficient * flow_speed * center[3]
            + coupling * (center[3] - center[5])
        )
        + diffusion * spread[3]
    )
    light_xmom = (
        center[4]
        - flow_dt * (slope_x[7] + coupling * (center[4] - center[2]))
        + diffusion * spread[4]
    )
    light_ymom = (
        center[5]
        - flow_dt * (slope_y[7] + coupling * (center[5] - center[3]))
        + diffusion * spread[5]
    )
    return jnp.stack([dense_depth, light_depth, dense_xmom, dense_ymom, light_xmom, light_ymom])


def basal_traction(fields, buoyancy, drag_coefficient):
    flow_speed = jnp.sqrt(fields[2] * fields[2] + fields[3] * fields[3] + speed_floor)
    press_one = buoyancy * (fields[0] + fields[1])
    rubbing = load_factor * drag_coefficient * flow_speed
    return jnp.stack([rubbing * fields[2], rubbing * fields[3], -load_factor * press_one])


def weights_cube():
    cube = (
        gll_weights.reshape(5, 1, 1) * gll_weights.reshape(1, 5, 1) * gll_weights.reshape(1, 1, 5)
    )
    return jnp.asarray(cube.reshape(5, 5, 5, 1, 1, 1), jnp.float32)


def load_kernel(trac_ref, node_ref, slot_ref, out_ref):
    slots = out_ref.shape[0]

    @pl.when(pl.program_id(0) == 0)
    def _():
        out_ref[...] = jnp.zeros(out_ref.shape, out_ref.dtype)

    def row_body(r, carry):
        for c0 in range(0, node_ref.shape[1], CHUNK):
            node = node_ref[pl.ds(r, 1), pl.ds(c0, CHUNK)]
            slot = slot_ref[pl.ds(r, 1), pl.ds(c0, CHUNK)]
            hit = lax.broadcasted_iota(jnp.int32, (NODE_PAD, CHUNK), 0) == node
            pieces = []
            for k in range(3):
                value = trac_ref[k, pl.ds(r, 1), pl.ds(c0, CHUNK)]
                high = value.astype(jnp.bfloat16).astype(jnp.float32)
                low = value - high
                pieces.append(jnp.where(hit, high, 0.0))
                pieces.append(jnp.where(hit, low, 0.0))
            weighted = jnp.concatenate(pieces, axis=0).astype(jnp.bfloat16)
            onehot = (
                lax.broadcasted_iota(jnp.int32, (slots, CHUNK), 0) == slot
            ).astype(jnp.bfloat16)
            out_ref[...] += lax.dot_general(
                onehot,
                weighted,
                (((1,), (1,)), ((), ())),
                preferred_element_type=jnp.float32,
            )
        return carry

    lax.fori_loop(0, ROW_BLOCK, row_body, 0)


def load_table(trac, node, slot, slots):
    rows, cols = node.shape
    return pl.pallas_call(
        load_kernel,
        grid=(rows // ROW_BLOCK,),
        in_specs=[
            pl.BlockSpec((3, ROW_BLOCK, cols), lambda g: (0, g, 0)),
            pl.BlockSpec((ROW_BLOCK, cols), lambda g: (g, 0)),
            pl.BlockSpec((ROW_BLOCK, cols), lambda g: (g, 0)),
        ],
        out_specs=pl.BlockSpec((slots, 6 * NODE_PAD), lambda g: (0, 0)),
        out_shape=jax.ShapeDtypeStruct((slots, 6 * NODE_PAD), jnp.float32),
        compiler_params=pltpu.CompilerParams(dimension_semantics=("arbitrary",)),
    )(trac, node, slot)


def along(x, axis, transpose):
    table = TABLE.T if transpose else TABLE
    shape = [1] * (x.ndim + 1)
    shape[axis] = 5
    shape[axis + 1] = 5
    coefs = jnp.asarray(table.reshape(shape))
    return jnp.sum(coefs * jnp.expand_dims(x, axis), axis=axis + 1)


def internal_force(values, lame_first, shear_modulus):
    weights_3d = weights_cube()
    gradients = [[along(values[i], j, False) for i in range(3)] for j in range(3)]
    divergence = gradients[0][0] + gradients[1][1] + gradients[2][2]
    forces = []
    for i in range(3):
        pulled = None
        for j in range(3):
            stress = shear_modulus * (gradients[j][i] + gradients[i][j])
            if i == j:
                stress = stress + lame_first * divergence
            term = along(weights_3d * stress, j, True)
            pulled = term if pulled is None else pulled + term
        forces.append(-pulled)
    return jnp.stack(forces)


def shift_faces(low_face, high_face, dim, axis):
    size = low_face.shape[dim]
    from_prev = send(lax.slice_in_dim(high_face, size - 1, size, axis=dim), (axis,), (1,))
    from_next = send(lax.slice_in_dim(low_face, 0, 1, axis=dim), (axis,), (-1,))
    before = jnp.concatenate([from_prev, lax.slice_in_dim(high_face, 0, size - 1, axis=dim)], axis=dim)
    after = jnp.concatenate([lax.slice_in_dim(low_face, 1, size, axis=dim), from_next], axis=dim)
    return before, after


def assemble_dim(values, node_dim, elem_dim, axis):
    low_face = lax.index_in_dim(values, 0, node_dim, keepdims=False)
    high_face = lax.index_in_dim(values, 4, node_dim, keepdims=False)
    face_elem_dim = elem_dim - 1
    if axis is None:
        size = low_face.shape[face_elem_dim]
        zero = jnp.zeros_like(lax.slice_in_dim(low_face, 0, 1, axis=face_elem_dim))
        before = jnp.concatenate(
            [zero, lax.slice_in_dim(high_face, 0, size - 1, axis=face_elem_dim)], axis=face_elem_dim
        )
        after = jnp.concatenate(
            [lax.slice_in_dim(low_face, 1, size, axis=face_elem_dim), zero], axis=face_elem_dim
        )
    else:
        before, after = shift_faces(low_face, high_face, face_elem_dim, axis)
    new_low = jnp.expand_dims(low_face + before, node_dim)
    new_high = jnp.expand_dims(high_face + after, node_dim)
    middle = lax.slice_in_dim(values, 1, 4, axis=node_dim)
    return jnp.concatenate([new_low, middle, new_high], axis=node_dim)


def assemble(values):
    values = assemble_dim(values, 1, 5, "gx")
    values = assemble_dim(values, 2, 6, "gy")
    values = assemble_dim(values, 3, 4, None)
    return values


def per_device(
    flow_state,
    drag_coefficient,
    wet_mask,
    target_elem,
    target_node,
    displacement,
    previous,
    density,
    lame_first,
    shear_modulus,
):
    buoyancy = 1.0 - 0.6 * wet_mask.astype(jnp.float32)
    fields = flow_state
    depth = FLOW_STEPS
    cell_rows = fields.shape[1]
    cell_cols = fields.shape[2]
    bundle = jnp.concatenate([fields, buoyancy[None], drag_coefficient[None]], axis=0)
    widened = halo(bundle, depth)
    row_ids = lax.axis_index("gx") * cell_rows + jnp.arange(cell_rows + 2 * depth) - depth
    col_ids = lax.axis_index("gy") * cell_cols + jnp.arange(cell_cols + 2 * depth) - depth
    row_inside = (row_ids >= 0) & (row_ids < cell_rows * lax.axis_size("gx"))
    col_inside = (col_ids >= 0) & (col_ids < cell_cols * lax.axis_size("gy"))
    inside = (row_inside[:, None] & col_inside[None, :]).astype(jnp.float32)
    wide_fields = widened[:6]
    wide_buoyancy = widened[6]
    wide_drag = widened[7]
    for counter in range(FLOW_STEPS):
        stacked = pressures(wide_fields, wide_buoyancy)
        padded = jnp.pad(stacked, ((0, 0), (1, 1), (1, 1)))
        wide_fields = advance(stacked, padded, wide_drag) * inside[None]
    fields = wide_fields[:, depth : depth + cell_rows, depth : depth + cell_cols]
    traction = basal_traction(fields, buoyancy, drag_coefficient)
    block_rows = displacement.shape[5]
    block_cols = displacement.shape[6]
    devices_y = lax.axis_size("gy")
    surface_cols = block_cols * devices_y
    elem_row = target_elem // surface_cols
    elem_col = target_elem % surface_cols
    local_x = elem_row - block_rows * lax.axis_index("gx") + 1
    local_y = elem_col - block_cols * lax.axis_index("gy") + 1
    slot_index = local_x * (block_cols + 2) + local_y
    wide_slots = (block_rows + 2) * (block_cols + 2)
    slots = -(-wide_slots // 16) * 16
    table = load_table(traction, target_node, slot_index, slots)
    table = table[:wide_slots].reshape(wide_slots, 3, 2, NODE_PAD)
    table = (table[:, :, 0] + table[:, :, 1])[:, :, :25]
    table = jnp.transpose(table, (1, 2, 0)).reshape(3, 25, block_rows + 2, block_cols + 2)
    both = ("gx", "gy")
    inner = table[:, :, 1 : 1 + block_rows, 1 : 1 + block_cols]
    row_low = send(table[:, :, block_rows + 1 : block_rows + 2, 1 : 1 + block_cols], ("gx",), (1,))
    row_high = send(table[:, :, 0:1, 1 : 1 + block_cols], ("gx",), (-1,))
    col_low = send(table[:, :, 1 : 1 + block_rows, block_cols + 1 :], ("gy",), (1,))
    col_high = send(table[:, :, 1 : 1 + block_rows, 0:1], ("gy",), (-1,))
    corner_ll = send(table[:, :, block_rows + 1 :, block_cols + 1 :], both, (1, 1))
    corner_lh = send(table[:, :, block_rows + 1 :, 0:1], both, (1, -1))
    corner_hl = send(table[:, :, 0:1, block_cols + 1 :], both, (-1, 1))
    corner_hh = send(table[:, :, 0:1, 0:1], both, (-1, -1))

    def place(piece, row_at, col_at):
        pads = [(0, 0), (0, 0)]
        pads.append((0, block_rows - 1) if row_at == 0 else (block_rows - 1, 0))
        pads.append((0, block_cols - 1) if col_at == 0 else (block_cols - 1, 0))
        return jnp.pad(piece, pads)

    own_loads = (
        inner
        + jnp.pad(row_low, ((0, 0), (0, 0), (0, block_rows - 1), (0, 0)))
        + jnp.pad(row_high, ((0, 0), (0, 0), (block_rows - 1, 0), (0, 0)))
        + jnp.pad(col_low, ((0, 0), (0, 0), (0, 0), (0, block_cols - 1)))
        + jnp.pad(col_high, ((0, 0), (0, 0), (0, 0), (block_cols - 1, 0)))
        + place(corner_ll, 0, 0)
        + place(corner_lh, 0, 1)
        + place(corner_hl, 1, 0)
        + place(corner_hh, 1, 1)
    )
    surface_load = own_loads.reshape(3, 5, 5, 1, 1, block_rows, block_cols)
    layers = displacement.shape[4]
    load_padded = jnp.pad(
        surface_load,
        ((0, 0), (0, 0), (0, 0), (0, 4), (0, layers - 1), (0, 0), (0, 0)),
    )
    masses = assemble(density[None, None, None, None] * weights_cube()[None])
    current = displacement
    for counter in range(SOLID_STEPS):
        force = internal_force(current, lame_first, shear_modulus) + load_padded
        acceleration = assemble(force) / masses
        advanced = 2.0 * current - previous + solid_dt * solid_dt * acceleration
        previous = current
        current = advanced
    return (fields, current, previous)


def solution(mesh):
    return jax.shard_map(
        per_device,
        mesh=mesh,
        in_specs=(
            P(None, "gx", "gy"),
            P("gx", "gy"),
            P("gx", "gy"),
            P("gx", "gy"),
            P("gx", "gy"),
            P(None, None, None, None, None, "gx", "gy"),
            P(None, None, None, None, None, "gx", "gy"),
            P(None, "gx", "gy"),
            P(None, "gx", "gy"),
            P(None, "gx", "gy"),
        ),
        out_specs=(
            P(None, "gx", "gy"),
            P(None, None, None, None, None, "gx", "gy"),
            P(None, None, None, None, None, "gx", "gy"),
        ),
        check_vma=False,
    )
```

```python
import jax
import jax.numpy as jnp
import numpy as np
from jax import lax
from jax.experimental import pallas as pl
from jax.experimental.pallas import tpu as pltpu
from jax.sharding import PartitionSpec as P

FLOW_STEPS = 4
SOLID_STEPS = 2


gll_points = np.array([-1.0, -np.sqrt(3.0 / 7.0), 0.0, np.sqrt(3.0 / 7.0), 1.0])
gll_weights = np.array([0.1, 49.0 / 90.0, 32.0 / 45.0, 49.0 / 90.0, 0.1])
flow_dt = 0.4
diffusion = 0.2
coupling = 0.5
upper_gravity = 0.8
density_ratio = 0.7
speed_floor = 0.0001
load_factor = 4.0
solid_dt = 0.04

NODE_PAD = 32
CHUNK = 1024
ROW_BLOCK = 8


def extended(block, sides, width):
    for axis, dim in sides:
        count = lax.axis_size(axis)
        forward = [(i, i + 1) for i in range(count - 1)]
        backward = [(target, source) for source, target in forward]
        low = lax.ppermute(
            lax.slice_in_dim(block, block.shape[dim] - width, None, axis=dim), axis, forward
        )
        high = lax.ppermute(lax.slice_in_dim(block, 0, width, axis=dim), axis, backward)
        block = jnp.concatenate([low, block, high], axis=dim)
    return block


def legendre_four(x):
    return (35.0 * x**4 - 30.0 * x**2 + 3.0) / 8.0


def derivative_table():
    result = np.zeros((5, 5))
    for i in range(5):
        for j in range(5):
            if i != j:
                result[i, j] = (
                    legendre_four(gll_points[i])
                    / legendre_four(gll_points[j])
                    / (gll_points[i] - gll_points[j])
                )
    result[0, 0] = -5.0
    result[4, 4] = 5.0
    return result


TABLE = derivative_table().astype(np.float32)


def pressures(fields, buoyancy):
    press_one = buoyancy * (fields[0] + fields[1])
    press_two = upper_gravity * (density_ratio * fields[0] + fields[1])
    return jnp.concatenate([fields, press_one[None], press_two[None]], axis=0)


def advance(center, padded, drag_coefficient):
    ahead_x = padded[:, 2:, 1:-1]
    behind_x = padded[:, :-2, 1:-1]
    ahead_y = padded[:, 1:-1, 2:]
    behind_y = padded[:, 1:-1, :-2]
    slope_x = 0.5 * (ahead_x - behind_x)
    slope_y = 0.5 * (ahead_y - behind_y)
    spread = ahead_x + behind_x + ahead_y + behind_y - 4.0 * center
    flow_speed = jnp.sqrt(center[2] * center[2] + center[3] * center[3] + speed_floor)
    dense_depth = center[0] - flow_dt * (slope_x[2] + slope_y[3]) + diffusion * spread[0]
    light_depth = center[1] - flow_dt * (slope_x[4] + slope_y[5]) + diffusion * spread[1]
    dense_xmom = (
        center[2]
        - flow_dt
        * (
            slope_x[6]
            + drag_coefficient * flow_speed * center[2]
            + coupling * (center[2] - center[4])
        )
        + diffusion * spread[2]
    )
    dense_ymom = (
        center[3]
        - flow_dt
        * (
            slope_y[6]
            + drag_coefficient * flow_speed * center[3]
            + coupling * (center[3] - center[5])
        )
        + diffusion * spread[3]
    )
    light_xmom = (
        center[4]
        - flow_dt * (slope_x[7] + coupling * (center[4] - center[2]))
        + diffusion * spread[4]
    )
    light_ymom = (
        center[5]
        - flow_dt * (slope_y[7] + coupling * (center[5] - center[3]))
        + diffusion * spread[5]
    )
    return jnp.stack([dense_depth, light_depth, dense_xmom, dense_ymom, light_xmom, light_ymom])


def basal_traction(fields, buoyancy, drag_coefficient):
    flow_speed = jnp.sqrt(fields[2] * fields[2] + fields[3] * fields[3] + speed_floor)
    press_one = buoyancy * (fields[0] + fields[1])
    rubbing = load_factor * drag_coefficient * flow_speed
    return jnp.stack([rubbing * fields[2], rubbing * fields[3], -load_factor * press_one])


def weights_cube():
    cube = (
        gll_weights.reshape(5, 1, 1) * gll_weights.reshape(1, 5, 1) * gll_weights.reshape(1, 1, 5)
    )
    return jnp.asarray(cube.reshape(5, 5, 5, 1, 1, 1), jnp.float32)


def load_kernel(trac_ref, node_ref, slot_ref, out_ref):
    slots = out_ref.shape[0]

    @pl.when(pl.program_id(0) == 0)
    def _():
        out_ref[...] = jnp.zeros(out_ref.shape, out_ref.dtype)

    def row_body(r, carry):
        for c0 in range(0, node_ref.shape[1], CHUNK):
            node = node_ref[pl.ds(r, 1), pl.ds(c0, CHUNK)]
            slot = slot_ref[pl.ds(r, 1), pl.ds(c0, CHUNK)]
            hit = lax.broadcasted_iota(jnp.int32, (NODE_PAD, CHUNK), 0) == node
            pieces = []
            for k in range(3):
                value = trac_ref[k, pl.ds(r, 1), pl.ds(c0, CHUNK)]
                high = value.astype(jnp.bfloat16).astype(jnp.float32)
                low = value - high
                pieces.append(jnp.where(hit, high, 0.0))
                pieces.append(jnp.where(hit, low, 0.0))
            weighted = jnp.concatenate(pieces, axis=0).astype(jnp.bfloat16)
            onehot = (
                lax.broadcasted_iota(jnp.int32, (slots, CHUNK), 0) == slot
            ).astype(jnp.bfloat16)
            out_ref[...] += lax.dot_general(
                onehot,
                weighted,
                (((1,), (1,)), ((), ())),
                preferred_element_type=jnp.float32,
            )
        return carry

    lax.fori_loop(0, ROW_BLOCK, row_body, 0)


def load_table(trac, node, slot, slots):
    rows, cols = node.shape
    return pl.pallas_call(
        load_kernel,
        grid=(rows // ROW_BLOCK,),
        in_specs=[
            pl.BlockSpec((3, ROW_BLOCK, cols), lambda g: (0, g, 0)),
            pl.BlockSpec((ROW_BLOCK, cols), lambda g: (g, 0)),
            pl.BlockSpec((ROW_BLOCK, cols), lambda g: (g, 0)),
        ],
        out_specs=pl.BlockSpec((slots, 6 * NODE_PAD), lambda g: (0, 0)),
        out_shape=jax.ShapeDtypeStruct((slots, 6 * NODE_PAD), jnp.float32),
        compiler_params=pltpu.CompilerParams(dimension_semantics=("arbitrary",)),
    )(trac, node, slot)


def along(x, axis, transpose):
    table = TABLE.T if transpose else TABLE
    shape = [1] * (x.ndim + 1)
    shape[axis] = 5
    shape[axis + 1] = 5
    coefs = jnp.asarray(table.reshape(shape))
    return jnp.sum(coefs * jnp.expand_dims(x, axis), axis=axis + 1)


def internal_force(values, lame_first, shear_modulus):
    weights_3d = weights_cube()
    gradients = [[along(values[i], j, False) for i in range(3)] for j in range(3)]
    divergence = gradients[0][0] + gradients[1][1] + gradients[2][2]
    forces = []
    for i in range(3):
        pulled = None
        for j in range(3):
            stress = shear_modulus * (gradients[j][i] + gradients[i][j])
            if i == j:
                stress = stress + lame_first * divergence
            term = along(weights_3d * stress, j, True)
            pulled = term if pulled is None else pulled + term
        forces.append(-pulled)
    return jnp.stack(forces)


def shift_block(block, axis, forward):
    count = lax.axis_size(axis)
    pairs = [(i, i + 1) for i in range(count - 1)]
    if not forward:
        pairs = [(target, source) for source, target in pairs]
    return lax.ppermute(block, axis, pairs)


def shift_faces(low_face, high_face, dim, axis):
    count = lax.axis_size(axis)
    forward = [(i, i + 1) for i in range(count - 1)]
    backward = [(target, source) for source, target in forward]
    size = low_face.shape[dim]
    from_prev = lax.ppermute(lax.slice_in_dim(high_face, size - 1, size, axis=dim), axis, forward)
    from_next = lax.ppermute(lax.slice_in_dim(low_face, 0, 1, axis=dim), axis, backward)
    before = jnp.concatenate([from_prev, lax.slice_in_dim(high_face, 0, size - 1, axis=dim)], axis=dim)
    after = jnp.concatenate([lax.slice_in_dim(low_face, 1, size, axis=dim), from_next], axis=dim)
    return before, after


def assemble_dim(values, node_dim, elem_dim, axis):
    low_face = lax.index_in_dim(values, 0, node_dim, keepdims=False)
    high_face = lax.index_in_dim(values, 4, node_dim, keepdims=False)
    face_elem_dim = elem_dim - 1
    if axis is None:
        size = low_face.shape[face_elem_dim]
        zero = jnp.zeros_like(lax.slice_in_dim(low_face, 0, 1, axis=face_elem_dim))
        before = jnp.concatenate(
            [zero, lax.slice_in_dim(high_face, 0, size - 1, axis=face_elem_dim)], axis=face_elem_dim
        )
        after = jnp.concatenate(
            [lax.slice_in_dim(low_face, 1, size, axis=face_elem_dim), zero], axis=face_elem_dim
        )
    else:
        before, after = shift_faces(low_face, high_face, face_elem_dim, axis)
    new_low = jnp.expand_dims(low_face + before, node_dim)
    new_high = jnp.expand_dims(high_face + after, node_dim)
    middle = lax.slice_in_dim(values, 1, 4, axis=node_dim)
    return jnp.concatenate([new_low, middle, new_high], axis=node_dim)


def assemble(values):
    values = assemble_dim(values, 1, 5, "gx")
    values = assemble_dim(values, 2, 6, "gy")
    values = assemble_dim(values, 3, 4, None)
    return values


def per_device(
    flow_state,
    drag_coefficient,
    wet_mask,
    target_elem,
    target_node,
    displacement,
    previous,
    density,
    lame_first,
    shear_modulus,
):
    buoyancy = 1.0 - 0.6 * wet_mask.astype(jnp.float32)
    fields = flow_state
    depth = FLOW_STEPS
    cell_rows = fields.shape[1]
    cell_cols = fields.shape[2]
    bundle = jnp.concatenate([fields, buoyancy[None], drag_coefficient[None]], axis=0)
    widened = extended(bundle, (("gx", 1), ("gy", 2)), depth)
    row_ids = lax.axis_index("gx") * cell_rows + jnp.arange(cell_rows + 2 * depth) - depth
    col_ids = lax.axis_index("gy") * cell_cols + jnp.arange(cell_cols + 2 * depth) - depth
    row_inside = (row_ids >= 0) & (row_ids < cell_rows * lax.axis_size("gx"))
    col_inside = (col_ids >= 0) & (col_ids < cell_cols * lax.axis_size("gy"))
    inside = (row_inside[:, None] & col_inside[None, :]).astype(jnp.float32)
    wide_fields = widened[:6]
    wide_buoyancy = widened[6]
    wide_drag = widened[7]
    for counter in range(FLOW_STEPS):
        stacked = pressures(wide_fields, wide_buoyancy)
        padded = jnp.pad(stacked, ((0, 0), (1, 1), (1, 1)))
        wide_fields = advance(stacked, padded, wide_drag) * inside[None]
    fields = wide_fields[:, depth : depth + cell_rows, depth : depth + cell_cols]
    traction = basal_traction(fields, buoyancy, drag_coefficient)
    block_rows = displacement.shape[5]
    block_cols = displacement.shape[6]
    devices_y = lax.axis_size("gy")
    surface_cols = block_cols * devices_y
    elem_row = target_elem // surface_cols
    elem_col = target_elem % surface_cols
    local_x = elem_row - block_rows * lax.axis_index("gx") + 1
    local_y = elem_col - block_cols * lax.axis_index("gy") + 1
    slot_index = local_x * (block_cols + 2) + local_y
    wide_slots = (block_rows + 2) * (block_cols + 2)
    slots = -(-wide_slots // 16) * 16
    table = load_table(traction, target_node, slot_index, slots)
    table = table[:wide_slots].reshape(wide_slots, 3, 2, NODE_PAD)
    table = (table[:, :, 0] + table[:, :, 1])[:, :, :25]
    table = jnp.transpose(table, (1, 2, 0)).reshape(3, 25, block_rows + 2, block_cols + 2)
    table = table.reshape(3, 5, 5, block_rows + 2, block_cols + 2)
    grid = None
    for a in range(5):
        for b in range(5):
            piece = lax.pad(table[:, a, b], 0.0, ((0, 0, 0), (a, 4 - a, 3), (b, 4 - b, 3)))
            grid = piece if grid is None else grid + piece
    point_rows = grid.shape[1]
    point_cols = grid.shape[2]
    span_x = 4 * block_rows
    span_y = 4 * block_cols
    from_next = shift_block(grid[:, : point_rows - span_x], "gx", False)
    from_prev = shift_block(grid[:, span_x:], "gx", True)
    grid = (
        grid
        + jnp.pad(from_next, ((0, 0), (span_x, 0), (0, 0)))
        + jnp.pad(from_prev, ((0, 0), (0, span_x), (0, 0)))
    )
    from_next = shift_block(grid[:, :, : point_cols - span_y], "gy", False)
    from_prev = shift_block(grid[:, :, span_y:], "gy", True)
    grid = (
        grid
        + jnp.pad(from_next, ((0, 0), (0, 0), (span_y, 0)))
        + jnp.pad(from_prev, ((0, 0), (0, 0), (0, span_y)))
    )
    by_row = jnp.stack(
        [lax.slice_in_dim(grid, 4 + a, 4 + a + span_x - 3, 4, axis=1) for a in range(5)], axis=1
    )
    surface_load = jnp.stack(
        [lax.slice_in_dim(by_row, 4 + b, 4 + b + span_y - 3, 4, axis=3) for b in range(5)], axis=2
    )
    surface_load = surface_load.reshape(3, 5, 5, 1, 1, block_rows, block_cols)
    layers = displacement.shape[4]
    load_padded = jnp.pad(
        surface_load,
        ((0, 0), (0, 0), (0, 0), (0, 4), (0, layers - 1), (0, 0), (0, 0)),
    )
    masses = assemble(density[None, None, None, None] * weights_cube()[None])
    current = displacement
    for counter in range(SOLID_STEPS):
        force = assemble(internal_force(current, lame_first, shear_modulus)) + load_padded
        acceleration = force / masses
        advanced = 2.0 * current - previous + solid_dt * solid_dt * acceleration
        previous = current
        current = advanced
    return (fields, current, previous)


def solution(mesh):
    return jax.shard_map(
        per_device,
        mesh=mesh,
        in_specs=(
            P(None, "gx", "gy"),
            P("gx", "gy"),
            P("gx", "gy"),
            P("gx", "gy"),
            P("gx", "gy"),
            P(None, None, None, None, None, "gx", "gy"),
            P(None, None, None, None, None, "gx", "gy"),
            P(None, "gx", "gy"),
            P(None, "gx", "gy"),
            P(None, "gx", "gy"),
        ),
        out_specs=(
            P(None, "gx", "gy"),
            P(None, None, None, None, None, "gx", "gy"),
            P(None, None, None, None, None, "gx", "gy"),
        ),
        check_vma=False,
    )
```

```python
import jax
import jax.numpy as jnp
import numpy as np
from jax import lax
from jax.experimental import pallas as pl
from jax.experimental.pallas import tpu as pltpu
from jax.sharding import PartitionSpec as P

FLOW_STEPS = 4
SOLID_STEPS = 2


gll_points = np.array([-1.0, -np.sqrt(3.0 / 7.0), 0.0, np.sqrt(3.0 / 7.0), 1.0])
gll_weights = np.array([0.1, 49.0 / 90.0, 32.0 / 45.0, 49.0 / 90.0, 0.1])
flow_dt = 0.4
diffusion = 0.2
coupling = 0.5
upper_gravity = 0.8
density_ratio = 0.7
speed_floor = 0.0001
load_factor = 4.0
solid_dt = 0.04

ROW_PAD = 24
CHUNK = 1024
ROW_BLOCK = 8


def extended(block, sides, width):
    for axis, dim in sides:
        count = lax.axis_size(axis)
        forward = [(i, i + 1) for i in range(count - 1)]
        backward = [(target, source) for source, target in forward]
        low = lax.ppermute(
            lax.slice_in_dim(block, block.shape[dim] - width, None, axis=dim), axis, forward
        )
        high = lax.ppermute(lax.slice_in_dim(block, 0, width, axis=dim), axis, backward)
        block = jnp.concatenate([low, block, high], axis=dim)
    return block


def legendre_four(x):
    return (35.0 * x**4 - 30.0 * x**2 + 3.0) / 8.0


def derivative_table():
    result = np.zeros((5, 5))
    for i in range(5):
        for j in range(5):
            if i != j:
                result[i, j] = (
                    legendre_four(gll_points[i])
                    / legendre_four(gll_points[j])
                    / (gll_points[i] - gll_points[j])
                )
    result[0, 0] = -5.0
    result[4, 4] = 5.0
    return result


TABLE = derivative_table().astype(np.float32)


def pressures(fields, buoyancy):
    press_one = buoyancy * (fields[0] + fields[1])
    press_two = upper_gravity * (density_ratio * fields[0] + fields[1])
    return jnp.concatenate([fields, press_one[None], press_two[None]], axis=0)


def advance(center, padded, drag_coefficient):
    ahead_x = padded[:, 2:, 1:-1]
    behind_x = padded[:, :-2, 1:-1]
    ahead_y = padded[:, 1:-1, 2:]
    behind_y = padded[:, 1:-1, :-2]
    slope_x = 0.5 * (ahead_x - behind_x)
    slope_y = 0.5 * (ahead_y - behind_y)
    spread = ahead_x + behind_x + ahead_y + behind_y - 4.0 * center
    flow_speed = jnp.sqrt(center[2] * center[2] + center[3] * center[3] + speed_floor)
    dense_depth = center[0] - flow_dt * (slope_x[2] + slope_y[3]) + diffusion * spread[0]
    light_depth = center[1] - flow_dt * (slope_x[4] + slope_y[5]) + diffusion * spread[1]
    dense_xmom = (
        center[2]
        - flow_dt
        * (
            slope_x[6]
            + drag_coefficient * flow_speed * center[2]
            + coupling * (center[2] - center[4])
        )
        + diffusion * spread[2]
    )
    dense_ymom = (
        center[3]
        - flow_dt
        * (
            slope_y[6]
            + drag_coefficient * flow_speed * center[3]
            + coupling * (center[3] - center[5])
        )
        + diffusion * spread[3]
    )
    light_xmom = (
        center[4]
        - flow_dt * (slope_x[7] + coupling * (center[4] - center[2]))
        + diffusion * spread[4]
    )
    light_ymom = (
        center[5]
        - flow_dt * (slope_y[7] + coupling * (center[5] - center[3]))
        + diffusion * spread[5]
    )
    return jnp.stack([dense_depth, light_depth, dense_xmom, dense_ymom, light_xmom, light_ymom])


def basal_traction(fields, buoyancy, drag_coefficient):
    flow_speed = jnp.sqrt(fields[2] * fields[2] + fields[3] * fields[3] + speed_floor)
    press_one = buoyancy * (fields[0] + fields[1])
    rubbing = load_factor * drag_coefficient * flow_speed
    return jnp.stack([rubbing * fields[2], rubbing * fields[3], -load_factor * press_one])


def weights_cube():
    cube = (
        gll_weights.reshape(5, 1, 1) * gll_weights.reshape(1, 5, 1) * gll_weights.reshape(1, 1, 5)
    )
    return jnp.asarray(cube.reshape(5, 5, 5, 1, 1, 1), jnp.float32)


def load_kernel(trac_ref, row_ref, col_ref, out_ref):
    slots = out_ref.shape[0]

    @pl.when(pl.program_id(0) == 0)
    def _():
        out_ref[...] = jnp.zeros(out_ref.shape, out_ref.dtype)

    def row_body(r, carry):
        for c0 in range(0, row_ref.shape[1], CHUNK):
            point_row = row_ref[pl.ds(r, 1), pl.ds(c0, CHUNK)]
            point_col = col_ref[pl.ds(r, 1), pl.ds(c0, CHUNK)]
            hit = lax.broadcasted_iota(jnp.int32, (ROW_PAD, CHUNK), 0) == point_row
            pieces = []
            for k in range(3):
                value = trac_ref[k, pl.ds(r, 1), pl.ds(c0, CHUNK)]
                high = value.astype(jnp.bfloat16).astype(jnp.float32)
                low = value - high
                pieces.append(jnp.where(hit, high, 0.0))
                pieces.append(jnp.where(hit, low, 0.0))
            weighted = jnp.concatenate(pieces, axis=0).astype(jnp.bfloat16)
            onehot = (
                lax.broadcasted_iota(jnp.int32, (slots, CHUNK), 0) == point_col
            ).astype(jnp.bfloat16)
            out_ref[...] += lax.dot_general(
                onehot,
                weighted,
                (((1,), (1,)), ((), ())),
                preferred_element_type=jnp.float32,
            )
        return carry

    lax.fori_loop(0, ROW_BLOCK, row_body, 0)


def load_table(trac, point_row, point_col, slots):
    rows, cols = point_row.shape
    return pl.pallas_call(
        load_kernel,
        grid=(rows // ROW_BLOCK,),
        in_specs=[
            pl.BlockSpec((3, ROW_BLOCK, cols), lambda g: (0, g, 0)),
            pl.BlockSpec((ROW_BLOCK, cols), lambda g: (g, 0)),
            pl.BlockSpec((ROW_BLOCK, cols), lambda g: (g, 0)),
        ],
        out_specs=pl.BlockSpec((slots, 6 * ROW_PAD), lambda g: (0, 0)),
        out_shape=jax.ShapeDtypeStruct((slots, 6 * ROW_PAD), jnp.float32),
        compiler_params=pltpu.CompilerParams(dimension_semantics=("arbitrary",)),
    )(trac, point_row, point_col)


def along(x, axis, transpose):
    table = TABLE.T if transpose else TABLE
    shape = [1] * (x.ndim + 1)
    shape[axis] = 5
    shape[axis + 1] = 5
    coefs = jnp.asarray(table.reshape(shape))
    return jnp.sum(coefs * jnp.expand_dims(x, axis), axis=axis + 1)


def internal_force(values, lame_first, shear_modulus):
    weights_3d = weights_cube()
    gradients = [[along(values[i], j, False) for i in range(3)] for j in range(3)]
    divergence = gradients[0][0] + gradients[1][1] + gradients[2][2]
    forces = []
    for i in range(3):
        pulled = None
        for j in range(3):
            stress = shear_modulus * (gradients[j][i] + gradients[i][j])
            if i == j:
                stress = stress + lame_first * divergence
            term = along(weights_3d * stress, j, True)
            pulled = term if pulled is None else pulled + term
        forces.append(-pulled)
    return jnp.stack(forces)


def shift_block(block, axis, forward):
    count = lax.axis_size(axis)
    pairs = [(i, i + 1) for i in range(count - 1)]
    if not forward:
        pairs = [(target, source) for source, target in pairs]
    return lax.ppermute(block, axis, pairs)


def shift_faces(low_face, high_face, dim, axis):
    count = lax.axis_size(axis)
    forward = [(i, i + 1) for i in range(count - 1)]
    backward = [(target, source) for source, target in forward]
    size = low_face.shape[dim]
    from_prev = lax.ppermute(lax.slice_in_dim(high_face, size - 1, size, axis=dim), axis, forward)
    from_next = lax.ppermute(lax.slice_in_dim(low_face, 0, 1, axis=dim), axis, backward)
    before = jnp.concatenate([from_prev, lax.slice_in_dim(high_face, 0, size - 1, axis=dim)], axis=dim)
    after = jnp.concatenate([lax.slice_in_dim(low_face, 1, size, axis=dim), from_next], axis=dim)
    return before, after


def assemble_dim(values, node_dim, elem_dim, axis):
    low_face = lax.index_in_dim(values, 0, node_dim, keepdims=False)
    high_face = lax.index_in_dim(values, 4, node_dim, keepdims=False)
    face_elem_dim = elem_dim - 1
    if axis is None:
        size = low_face.shape[face_elem_dim]
        zero = jnp.zeros_like(lax.slice_in_dim(low_face, 0, 1, axis=face_elem_dim))
        before = jnp.concatenate(
            [zero, lax.slice_in_dim(high_face, 0, size - 1, axis=face_elem_dim)], axis=face_elem_dim
        )
        after = jnp.concatenate(
            [lax.slice_in_dim(low_face, 1, size, axis=face_elem_dim), zero], axis=face_elem_dim
        )
    else:
        before, after = shift_faces(low_face, high_face, face_elem_dim, axis)
    new_low = jnp.expand_dims(low_face + before, node_dim)
    new_high = jnp.expand_dims(high_face + after, node_dim)
    middle = lax.slice_in_dim(values, 1, 4, axis=node_dim)
    return jnp.concatenate([new_low, middle, new_high], axis=node_dim)


def assemble(values):
    values = assemble_dim(values, 1, 5, "gx")
    values = assemble_dim(values, 2, 6, "gy")
    values = assemble_dim(values, 3, 4, None)
    return values


def per_device(
    flow_state,
    drag_coefficient,
    wet_mask,
    target_elem,
    target_node,
    displacement,
    previous,
    density,
    lame_first,
    shear_modulus,
):
    buoyancy = 1.0 - 0.6 * wet_mask.astype(jnp.float32)
    fields = flow_state
    depth = FLOW_STEPS
    cell_rows = fields.shape[1]
    cell_cols = fields.shape[2]
    bundle = jnp.concatenate([fields, buoyancy[None], drag_coefficient[None]], axis=0)
    widened = extended(bundle, (("gx", 1), ("gy", 2)), depth)
    row_ids = lax.axis_index("gx") * cell_rows + jnp.arange(cell_rows + 2 * depth) - depth
    col_ids = lax.axis_index("gy") * cell_cols + jnp.arange(cell_cols + 2 * depth) - depth
    row_inside = (row_ids >= 0) & (row_ids < cell_rows * lax.axis_size("gx"))
    col_inside = (col_ids >= 0) & (col_ids < cell_cols * lax.axis_size("gy"))
    inside = (row_inside[:, None] & col_inside[None, :]).astype(jnp.float32)
    wide_fields = widened[:6]
    wide_buoyancy = widened[6]
    wide_drag = widened[7]
    for counter in range(FLOW_STEPS):
        stacked = pressures(wide_fields, wide_buoyancy)
        padded = jnp.pad(stacked, ((0, 0), (1, 1), (1, 1)))
        wide_fields = advance(stacked, padded, wide_drag) * inside[None]
    fields = wide_fields[:, depth : depth + cell_rows, depth : depth + cell_cols]
    traction = basal_traction(fields, buoyancy, drag_coefficient)
    block_rows = displacement.shape[5]
    block_cols = displacement.shape[6]
    devices_y = lax.axis_size("gy")
    surface_cols = block_cols * devices_y
    elem_row = target_elem // surface_cols
    elem_col = target_elem % surface_cols
    local_x = elem_row - block_rows * lax.axis_index("gx") + 1
    local_y = elem_col - block_cols * lax.axis_index("gy") + 1
    point_rows = 4 * (block_rows + 2) + 1
    point_cols = 4 * (block_cols + 2) + 1
    span_x = 4 * block_rows
    span_y = 4 * block_cols
    point_row = 4 * local_x + target_node // 5
    point_col = 4 * local_y + target_node % 5
    slots = -(-point_cols // 16) * 16
    grid = load_table(traction, point_row, point_col, slots)
    grid = grid.reshape(slots, 3, 2, ROW_PAD)
    grid = grid[:, :, 0] + grid[:, :, 1]
    overlap_x = point_rows - span_x
    overlap_y = point_cols - span_y
    from_next = shift_block(grid[:, :, :overlap_x], "gx", False)
    from_prev = shift_block(grid[:, :, span_x:point_rows], "gx", True)
    grid = (
        grid
        + jnp.pad(from_next, ((0, 0), (0, 0), (span_x, ROW_PAD - point_rows)))
        + jnp.pad(from_prev, ((0, 0), (0, 0), (0, ROW_PAD - overlap_x)))
    )
    from_next = shift_block(grid[:overlap_y], "gy", False)
    from_prev = shift_block(grid[span_y:point_cols], "gy", True)
    grid = (
        grid
        + jnp.pad(from_next, ((span_y, slots - point_cols), (0, 0), (0, 0)))
        + jnp.pad(from_prev, ((0, slots - overlap_y), (0, 0), (0, 0)))
    )
    by_col = jnp.concatenate(
        [
            grid[4 : 4 + span_y].reshape(block_cols, 4, 3, ROW_PAD),
            grid[8 : 8 + span_y].reshape(block_cols, 4, 3, ROW_PAD)[:, 0:1],
        ],
        axis=1,
    )
    by_row = jnp.concatenate(
        [
            by_col[..., 4 : 4 + span_x].reshape(block_cols, 5, 3, block_rows, 4),
            by_col[..., 8 : 8 + span_x].reshape(block_cols, 5, 3, block_rows, 4)[..., 0:1],
        ],
        axis=-1,
    )
    surface_load = jnp.transpose(by_row, (2, 4, 1, 3, 0))
    surface_load = surface_load.reshape(3, 5, 5, 1, 1, block_rows, block_cols)
    layers = displacement.shape[4]
    load_padded = jnp.pad(
        surface_load,
        ((0, 0), (0, 0), (0, 0), (0, 4), (0, layers - 1), (0, 0), (0, 0)),
    )
    masses = assemble(density[None, None, None, None] * weights_cube()[None])
    current = displacement
    for counter in range(SOLID_STEPS):
        force = assemble(internal_force(current, lame_first, shear_modulus)) + load_padded
        acceleration = force / masses
        advanced = 2.0 * current - previous + solid_dt * solid_dt * acceleration
        previous = current
        current = advanced
    return (fields, current, previous)


def solution(mesh):
    return jax.shard_map(
        per_device,
        mesh=mesh,
        in_specs=(
            P(None, "gx", "gy"),
            P("gx", "gy"),
            P("gx", "gy"),
            P("gx", "gy"),
            P("gx", "gy"),
            P(None, None, None, None, None, "gx", "gy"),
            P(None, None, None, None, None, "gx", "gy"),
            P(None, "gx", "gy"),
            P(None, "gx", "gy"),
            P(None, "gx", "gy"),
        ),
        out_specs=(
            P(None, "gx", "gy"),
            P(None, None, None, None, None, "gx", "gy"),
            P(None, None, None, None, None, "gx", "gy"),
        ),
        check_vma=False,
    )
```

```python
import jax
import jax.numpy as jnp
import numpy as np
from jax import lax
from jax.experimental import pallas as pl
from jax.experimental.pallas import tpu as pltpu
from jax.sharding import PartitionSpec as P

FLOW_STEPS = 4
SOLID_STEPS = 2


gll_points = np.array([-1.0, -np.sqrt(3.0 / 7.0), 0.0, np.sqrt(3.0 / 7.0), 1.0])
gll_weights = np.array([0.1, 49.0 / 90.0, 32.0 / 45.0, 49.0 / 90.0, 0.1])
flow_dt = 0.4
diffusion = 0.2
coupling = 0.5
upper_gravity = 0.8
density_ratio = 0.7
speed_floor = 0.0001
load_factor = 4.0
solid_dt = 0.04

ROW_PAD = 24
CHUNK = 1024
ROW_BLOCK = 8


def extended(block, sides, width):
    for axis, dim in sides:
        count = lax.axis_size(axis)
        forward = [(i, i + 1) for i in range(count - 1)]
        backward = [(target, source) for source, target in forward]
        low = lax.ppermute(
            lax.slice_in_dim(block, block.shape[dim] - width, None, axis=dim), axis, forward
        )
        high = lax.ppermute(lax.slice_in_dim(block, 0, width, axis=dim), axis, backward)
        block = jnp.concatenate([low, block, high], axis=dim)
    return block


def legendre_four(x):
    return (35.0 * x**4 - 30.0 * x**2 + 3.0) / 8.0


def derivative_table():
    result = np.zeros((5, 5))
    for i in range(5):
        for j in range(5):
            if i != j:
                result[i, j] = (
                    legendre_four(gll_points[i])
                    / legendre_four(gll_points[j])
                    / (gll_points[i] - gll_points[j])
                )
    result[0, 0] = -5.0
    result[4, 4] = 5.0
    return result


TABLE = derivative_table().astype(np.float32)


def pressures(fields, buoyancy):
    press_one = buoyancy * (fields[0] + fields[1])
    press_two = upper_gravity * (density_ratio * fields[0] + fields[1])
    return jnp.concatenate([fields, press_one[None], press_two[None]], axis=0)


def advance(center, padded, drag_coefficient):
    ahead_x = padded[:, 2:, 1:-1]
    behind_x = padded[:, :-2, 1:-1]
    ahead_y = padded[:, 1:-1, 2:]
    behind_y = padded[:, 1:-1, :-2]
    slope_x = 0.5 * (ahead_x - behind_x)
    slope_y = 0.5 * (ahead_y - behind_y)
    spread = ahead_x + behind_x + ahead_y + behind_y - 4.0 * center
    flow_speed = jnp.sqrt(center[2] * center[2] + center[3] * center[3] + speed_floor)
    dense_depth = center[0] - flow_dt * (slope_x[2] + slope_y[3]) + diffusion * spread[0]
    light_depth = center[1] - flow_dt * (slope_x[4] + slope_y[5]) + diffusion * spread[1]
    dense_xmom = (
        center[2]
        - flow_dt
        * (
            slope_x[6]
            + drag_coefficient * flow_speed * center[2]
            + coupling * (center[2] - center[4])
        )
        + diffusion * spread[2]
    )
    dense_ymom = (
        center[3]
        - flow_dt
        * (
            slope_y[6]
            + drag_coefficient * flow_speed * center[3]
            + coupling * (center[3] - center[5])
        )
        + diffusion * spread[3]
    )
    light_xmom = (
        center[4]
        - flow_dt * (slope_x[7] + coupling * (center[4] - center[2]))
        + diffusion * spread[4]
    )
    light_ymom = (
        center[5]
        - flow_dt * (slope_y[7] + coupling * (center[5] - center[3]))
        + diffusion * spread[5]
    )
    return jnp.stack([dense_depth, light_depth, dense_xmom, dense_ymom, light_xmom, light_ymom])


def basal_traction(fields, buoyancy, drag_coefficient):
    flow_speed = jnp.sqrt(fields[2] * fields[2] + fields[3] * fields[3] + speed_floor)
    press_one = buoyancy * (fields[0] + fields[1])
    rubbing = load_factor * drag_coefficient * flow_speed
    return jnp.stack([rubbing * fields[2], rubbing * fields[3], -load_factor * press_one])


def weights_cube():
    cube = (
        gll_weights.reshape(5, 1, 1) * gll_weights.reshape(1, 5, 1) * gll_weights.reshape(1, 1, 5)
    )
    return jnp.asarray(cube.reshape(5, 5, 5, 1, 1, 1), jnp.float32)


def load_kernel(trac_ref, row_ref, col_ref, out_ref):
    slots = out_ref.shape[0]

    @pl.when(pl.program_id(0) == 0)
    def _():
        out_ref[...] = jnp.zeros(out_ref.shape, out_ref.dtype)

    def row_body(r, carry):
        for c0 in range(0, row_ref.shape[1], CHUNK):
            point_row = row_ref[pl.ds(r, 1), pl.ds(c0, CHUNK)]
            point_col = col_ref[pl.ds(r, 1), pl.ds(c0, CHUNK)]
            hit = lax.broadcasted_iota(jnp.int32, (ROW_PAD, CHUNK), 0) == point_row
            pieces = []
            for k in range(3):
                value = trac_ref[k, pl.ds(r, 1), pl.ds(c0, CHUNK)]
                high = value.astype(jnp.bfloat16).astype(jnp.float32)
                low = value - high
                pieces.append(jnp.where(hit, high, 0.0))
                pieces.append(jnp.where(hit, low, 0.0))
            weighted = jnp.concatenate(pieces, axis=0).astype(jnp.bfloat16)
            onehot = (
                lax.broadcasted_iota(jnp.int32, (slots, CHUNK), 0) == point_col
            ).astype(jnp.bfloat16)
            out_ref[...] += lax.dot_general(
                onehot,
                weighted,
                (((1,), (1,)), ((), ())),
                preferred_element_type=jnp.float32,
            )
        return carry

    lax.fori_loop(0, ROW_BLOCK, row_body, 0)


def load_table(trac, point_row, point_col, slots):
    rows, cols = point_row.shape
    return pl.pallas_call(
        load_kernel,
        grid=(rows // ROW_BLOCK,),
        in_specs=[
            pl.BlockSpec((3, ROW_BLOCK, cols), lambda g: (0, g, 0)),
            pl.BlockSpec((ROW_BLOCK, cols), lambda g: (g, 0)),
            pl.BlockSpec((ROW_BLOCK, cols), lambda g: (g, 0)),
        ],
        out_specs=pl.BlockSpec((slots, 6 * ROW_PAD), lambda g: (0, 0)),
        out_shape=jax.ShapeDtypeStruct((slots, 6 * ROW_PAD), jnp.float32),
        compiler_params=pltpu.CompilerParams(dimension_semantics=("arbitrary",)),
    )(trac, point_row, point_col)


def along(x, axis, transpose):
    table = TABLE.T if transpose else TABLE
    shape = [1] * (x.ndim + 1)
    shape[axis] = 5
    shape[axis + 1] = 5
    coefs = jnp.asarray(table.reshape(shape))
    return jnp.sum(coefs * jnp.expand_dims(x, axis), axis=axis + 1)


def internal_force(values, lame_first, shear_modulus):
    weights_3d = weights_cube()
    gradients = [[along(values[i], j, False) for i in range(3)] for j in range(3)]
    divergence = gradients[0][0] + gradients[1][1] + gradients[2][2]
    forces = []
    for i in range(3):
        pulled = None
        for j in range(3):
            stress = shear_modulus * (gradients[j][i] + gradients[i][j])
            if i == j:
                stress = stress + lame_first * divergence
            term = along(weights_3d * stress, j, True)
            pulled = term if pulled is None else pulled + term
        forces.append(-pulled)
    return jnp.stack(forces)


def shift_block(block, axis, forward):
    count = lax.axis_size(axis)
    pairs = [(i, i + 1) for i in range(count - 1)]
    if not forward:
        pairs = [(target, source) for source, target in pairs]
    return lax.ppermute(block, axis, pairs)


def shift_faces(low_face, high_face, dim, axis):
    count = lax.axis_size(axis)
    forward = [(i, i + 1) for i in range(count - 1)]
    backward = [(target, source) for source, target in forward]
    size = low_face.shape[dim]
    from_prev = lax.ppermute(lax.slice_in_dim(high_face, size - 1, size, axis=dim), axis, forward)
    from_next = lax.ppermute(lax.slice_in_dim(low_face, 0, 1, axis=dim), axis, backward)
    before = jnp.concatenate([from_prev, lax.slice_in_dim(high_face, 0, size - 1, axis=dim)], axis=dim)
    after = jnp.concatenate([lax.slice_in_dim(low_face, 1, size, axis=dim), from_next], axis=dim)
    return before, after


def assemble_dim(values, node_dim, elem_dim, axis):
    low_face = lax.index_in_dim(values, 0, node_dim, keepdims=False)
    high_face = lax.index_in_dim(values, 4, node_dim, keepdims=False)
    face_elem_dim = elem_dim - 1
    if axis is None:
        size = low_face.shape[face_elem_dim]
        zero = jnp.zeros_like(lax.slice_in_dim(low_face, 0, 1, axis=face_elem_dim))
        before = jnp.concatenate(
            [zero, lax.slice_in_dim(high_face, 0, size - 1, axis=face_elem_dim)], axis=face_elem_dim
        )
        after = jnp.concatenate(
            [lax.slice_in_dim(low_face, 1, size, axis=face_elem_dim), zero], axis=face_elem_dim
        )
    else:
        before, after = shift_faces(low_face, high_face, face_elem_dim, axis)
    new_low = jnp.expand_dims(low_face + before, node_dim)
    new_high = jnp.expand_dims(high_face + after, node_dim)
    middle = lax.slice_in_dim(values, 1, 4, axis=node_dim)
    return jnp.concatenate([new_low, middle, new_high], axis=node_dim)


def assemble(values):
    values = assemble_dim(values, 1, 5, "gx")
    values = assemble_dim(values, 2, 6, "gy")
    values = assemble_dim(values, 3, 4, None)
    return values


def per_device(
    flow_state,
    drag_coefficient,
    wet_mask,
    target_elem,
    target_node,
    displacement,
    previous,
    density,
    lame_first,
    shear_modulus,
):
    buoyancy = 1.0 - 0.6 * wet_mask.astype(jnp.float32)
    fields = flow_state
    depth = FLOW_STEPS
    cell_rows = fields.shape[1]
    cell_cols = fields.shape[2]
    bundle = jnp.concatenate([fields, buoyancy[None], drag_coefficient[None]], axis=0)
    widened = extended(bundle, (("gx", 1), ("gy", 2)), depth)
    row_ids = lax.axis_index("gx") * cell_rows + jnp.arange(cell_rows + 2 * depth) - depth
    col_ids = lax.axis_index("gy") * cell_cols + jnp.arange(cell_cols + 2 * depth) - depth
    row_inside = (row_ids >= 0) & (row_ids < cell_rows * lax.axis_size("gx"))
    col_inside = (col_ids >= 0) & (col_ids < cell_cols * lax.axis_size("gy"))
    inside = (row_inside[:, None] & col_inside[None, :]).astype(jnp.float32)
    wide_fields = widened[:6]
    wide_buoyancy = widened[6]
    wide_drag = widened[7]
    for counter in range(FLOW_STEPS):
        stacked = pressures(wide_fields, wide_buoyancy)
        padded = jnp.pad(stacked, ((0, 0), (1, 1), (1, 1)))
        wide_fields = advance(stacked, padded, wide_drag) * inside[None]
    fields = wide_fields[:, depth : depth + cell_rows, depth : depth + cell_cols]
    traction = basal_traction(fields, buoyancy, drag_coefficient)
    block_rows = displacement.shape[5]
    block_cols = displacement.shape[6]
    devices_y = lax.axis_size("gy")
    surface_cols = block_cols * devices_y
    elem_row = target_elem // surface_cols
    elem_col = target_elem % surface_cols
    local_x = elem_row - block_rows * lax.axis_index("gx") + 1
    local_y = elem_col - block_cols * lax.axis_index("gy") + 1
    point_rows = 4 * (block_rows + 2) + 1
    point_cols = 4 * (block_cols + 2) + 1
    span_x = 4 * block_rows
    span_y = 4 * block_cols
    point_row = 4 * local_x + target_node // 5
    point_col = 4 * local_y + target_node % 5
    slots = -(-point_cols // 16) * 16
    grid = load_table(traction, point_row, point_col, slots)
    grid = grid.reshape(slots, 3, 2, ROW_PAD)
    grid = grid[:, :, 0] + grid[:, :, 1]
    overlap_x = point_rows - span_x
    overlap_y = point_cols - span_y
    from_next = shift_block(grid[:, :, :overlap_x], "gx", False)
    from_prev = shift_block(grid[:, :, span_x:point_rows], "gx", True)
    grid = (
        grid
        + jnp.pad(from_next, ((0, 0), (0, 0), (span_x, ROW_PAD - point_rows)))
        + jnp.pad(from_prev, ((0, 0), (0, 0), (0, ROW_PAD - overlap_x)))
    )
    from_next = shift_block(grid[:overlap_y], "gy", False)
    from_prev = shift_block(grid[span_y:point_cols], "gy", True)
    grid = (
        grid
        + jnp.pad(from_next, ((span_y, slots - point_cols), (0, 0), (0, 0)))
        + jnp.pad(from_prev, ((0, slots - overlap_y), (0, 0), (0, 0)))
    )
    by_col = jnp.concatenate(
        [
            grid[4 : 4 + span_y].reshape(block_cols, 4, 3, ROW_PAD),
            grid[8 : 8 + span_y].reshape(block_cols, 4, 3, ROW_PAD)[:, 0:1],
        ],
        axis=1,
    )
    by_row = jnp.concatenate(
        [
            by_col[..., 4 : 4 + span_x].reshape(block_cols, 5, 3, block_rows, 4),
            by_col[..., 8 : 8 + span_x].reshape(block_cols, 5, 3, block_rows, 4)[..., 0:1],
        ],
        axis=-1,
    )
    surface_load = jnp.transpose(by_row, (2, 4, 1, 3, 0))
    surface_load = surface_load.reshape(3, 5, 5, 1, 1, block_rows, block_cols)
    layers = displacement.shape[4]
    load_padded = jnp.pad(
        surface_load,
        ((0, 0), (0, 0), (0, 0), (0, 4), (0, layers - 1), (0, 0), (0, 0)),
    )
    mass_parts = density[None, None, None, None] * weights_cube()[None]
    masses = None
    current = displacement
    for counter in range(SOLID_STEPS):
        force = internal_force(current, lame_first, shear_modulus)
        if masses is None:
            joined = assemble(jnp.concatenate([force, mass_parts], axis=0))
            force = joined[:3]
            masses = joined[3:]
        else:
            force = assemble(force)
        acceleration = (force + load_padded) / masses
        advanced = 2.0 * current - previous + solid_dt * solid_dt * acceleration
        previous = current
        current = advanced
    return (fields, current, previous)


def solution(mesh):
    return jax.shard_map(
        per_device,
        mesh=mesh,
        in_specs=(
            P(None, "gx", "gy"),
            P("gx", "gy"),
            P("gx", "gy"),
            P("gx", "gy"),
            P("gx", "gy"),
            P(None, None, None, None, None, "gx", "gy"),
            P(None, None, None, None, None, "gx", "gy"),
            P(None, "gx", "gy"),
            P(None, "gx", "gy"),
            P(None, "gx", "gy"),
        ),
        out_specs=(
            P(None, "gx", "gy"),
            P(None, None, None, None, None, "gx", "gy"),
            P(None, None, None, None, None, "gx", "gy"),
        ),
        check_vma=False,
    )
```

```python
import jax
import jax.numpy as jnp
import numpy as np
from jax import lax
from jax.experimental import pallas as pl
from jax.experimental.pallas import tpu as pltpu
from jax.sharding import PartitionSpec as P

FLOW_STEPS = 4
SOLID_STEPS = 2


gll_points = np.array([-1.0, -np.sqrt(3.0 / 7.0), 0.0, np.sqrt(3.0 / 7.0), 1.0])
gll_weights = np.array([0.1, 49.0 / 90.0, 32.0 / 45.0, 49.0 / 90.0, 0.1])
flow_dt = 0.4
diffusion = 0.2
coupling = 0.5
upper_gravity = 0.8
density_ratio = 0.7
speed_floor = 0.0001
load_factor = 4.0
solid_dt = 0.04

ROW_PAD = 24
CHUNK = 1024
ROW_BLOCK = 8


def extended(block, sides, width):
    for axis, dim in sides:
        count = lax.axis_size(axis)
        forward = [(i, i + 1) for i in range(count - 1)]
        backward = [(target, source) for source, target in forward]
        low = lax.ppermute(
            lax.slice_in_dim(block, block.shape[dim] - width, None, axis=dim), axis, forward
        )
        high = lax.ppermute(lax.slice_in_dim(block, 0, width, axis=dim), axis, backward)
        block = jnp.concatenate([low, block, high], axis=dim)
    return block


def legendre_four(x):
    return (35.0 * x**4 - 30.0 * x**2 + 3.0) / 8.0


def derivative_table():
    result = np.zeros((5, 5))
    for i in range(5):
        for j in range(5):
            if i != j:
                result[i, j] = (
                    legendre_four(gll_points[i])
                    / legendre_four(gll_points[j])
                    / (gll_points[i] - gll_points[j])
                )
    result[0, 0] = -5.0
    result[4, 4] = 5.0
    return result


TABLE = derivative_table().astype(np.float32)


def pressures(fields, buoyancy):
    press_one = buoyancy * (fields[0] + fields[1])
    press_two = upper_gravity * (density_ratio * fields[0] + fields[1])
    return jnp.concatenate([fields, press_one[None], press_two[None]], axis=0)


def advance(center, padded, drag_coefficient):
    ahead_x = padded[:, 2:, 1:-1]
    behind_x = padded[:, :-2, 1:-1]
    ahead_y = padded[:, 1:-1, 2:]
    behind_y = padded[:, 1:-1, :-2]
    slope_x = 0.5 * (ahead_x - behind_x)
    slope_y = 0.5 * (ahead_y - behind_y)
    spread = ahead_x + behind_x + ahead_y + behind_y - 4.0 * center
    flow_speed = jnp.sqrt(center[2] * center[2] + center[3] * center[3] + speed_floor)
    dense_depth = center[0] - flow_dt * (slope_x[2] + slope_y[3]) + diffusion * spread[0]
    light_depth = center[1] - flow_dt * (slope_x[4] + slope_y[5]) + diffusion * spread[1]
    dense_xmom = (
        center[2]
        - flow_dt
        * (
            slope_x[6]
            + drag_coefficient * flow_speed * center[2]
            + coupling * (center[2] - center[4])
        )
        + diffusion * spread[2]
    )
    dense_ymom = (
        center[3]
        - flow_dt
        * (
            slope_y[6]
            + drag_coefficient * flow_speed * center[3]
            + coupling * (center[3] - center[5])
        )
        + diffusion * spread[3]
    )
    light_xmom = (
        center[4]
        - flow_dt * (slope_x[7] + coupling * (center[4] - center[2]))
        + diffusion * spread[4]
    )
    light_ymom = (
        center[5]
        - flow_dt * (slope_y[7] + coupling * (center[5] - center[3]))
        + diffusion * spread[5]
    )
    return jnp.stack([dense_depth, light_depth, dense_xmom, dense_ymom, light_xmom, light_ymom])


def basal_traction(fields, buoyancy, drag_coefficient):
    flow_speed = jnp.sqrt(fields[2] * fields[2] + fields[3] * fields[3] + speed_floor)
    press_one = buoyancy * (fields[0] + fields[1])
    rubbing = load_factor * drag_coefficient * flow_speed
    return jnp.stack([rubbing * fields[2], rubbing * fields[3], -load_factor * press_one])


def weights_cube():
    cube = (
        gll_weights.reshape(5, 1, 1) * gll_weights.reshape(1, 5, 1) * gll_weights.reshape(1, 1, 5)
    )
    return jnp.asarray(cube.reshape(5, 5, 5, 1, 1, 1), jnp.float32)


def load_kernel(trac_ref, row_ref, col_ref, out_ref):
    slots = out_ref.shape[0]

    @pl.when(pl.program_id(0) == 0)
    def _():
        out_ref[...] = jnp.zeros(out_ref.shape, out_ref.dtype)

    def row_body(r, carry):
        for c0 in range(0, row_ref.shape[1], CHUNK):
            point_row = row_ref[pl.ds(r, 1), pl.ds(c0, CHUNK)]
            point_col = col_ref[pl.ds(r, 1), pl.ds(c0, CHUNK)]
            hit = lax.broadcasted_iota(jnp.int32, (ROW_PAD, CHUNK), 0) == point_row
            pieces = []
            for k in range(3):
                value = trac_ref[k, pl.ds(r, 1), pl.ds(c0, CHUNK)]
                high = value.astype(jnp.bfloat16).astype(jnp.float32)
                low = value - high
                pieces.append(jnp.where(hit, high, 0.0))
                pieces.append(jnp.where(hit, low, 0.0))
            weighted = jnp.concatenate(pieces, axis=0).astype(jnp.bfloat16)
            onehot = (
                lax.broadcasted_iota(jnp.int32, (slots, CHUNK), 0) == point_col
            ).astype(jnp.bfloat16)
            out_ref[...] += lax.dot_general(
                onehot,
                weighted,
                (((1,), (1,)), ((), ())),
                preferred_element_type=jnp.float32,
            )
        return carry

    lax.fori_loop(0, ROW_BLOCK, row_body, 0)


def load_table(trac, point_row, point_col, slots):
    rows, cols = point_row.shape
    return pl.pallas_call(
        load_kernel,
        grid=(rows // ROW_BLOCK,),
        in_specs=[
            pl.BlockSpec((3, ROW_BLOCK, cols), lambda g: (0, g, 0)),
            pl.BlockSpec((ROW_BLOCK, cols), lambda g: (g, 0)),
            pl.BlockSpec((ROW_BLOCK, cols), lambda g: (g, 0)),
        ],
        out_specs=pl.BlockSpec((slots, 6 * ROW_PAD), lambda g: (0, 0)),
        out_shape=jax.ShapeDtypeStruct((slots, 6 * ROW_PAD), jnp.float32),
        compiler_params=pltpu.CompilerParams(dimension_semantics=("arbitrary",)),
    )(trac, point_row, point_col)


def along(x, axis, transpose):
    table = TABLE.T if transpose else TABLE
    shape = [1] * (x.ndim + 1)
    shape[axis] = 5
    shape[axis + 1] = 5
    coefs = jnp.asarray(table.reshape(shape))
    return jnp.sum(coefs * jnp.expand_dims(x, axis), axis=axis + 1)


def internal_force(values, lame_first, shear_modulus):
    weights_3d = weights_cube()
    gradients = [[along(values[i], j, False) for i in range(3)] for j in range(3)]
    divergence = gradients[0][0] + gradients[1][1] + gradients[2][2]
    forces = []
    for i in range(3):
        pulled = None
        for j in range(3):
            stress = shear_modulus * (gradients[j][i] + gradients[i][j])
            if i == j:
                stress = stress + lame_first * divergence
            term = along(weights_3d * stress, j, True)
            pulled = term if pulled is None else pulled + term
        forces.append(-pulled)
    return jnp.stack(forces)


def shift_block(block, axis, forward):
    count = lax.axis_size(axis)
    pairs = [(i, i + 1) for i in range(count - 1)]
    if not forward:
        pairs = [(target, source) for source, target in pairs]
    return lax.ppermute(block, axis, pairs)


def shift_faces(low_face, high_face, dim, axis):
    count = lax.axis_size(axis)
    forward = [(i, i + 1) for i in range(count - 1)]
    backward = [(target, source) for source, target in forward]
    size = low_face.shape[dim]
    from_prev = lax.ppermute(lax.slice_in_dim(high_face, size - 1, size, axis=dim), axis, forward)
    from_next = lax.ppermute(lax.slice_in_dim(low_face, 0, 1, axis=dim), axis, backward)
    before = jnp.concatenate([from_prev, lax.slice_in_dim(high_face, 0, size - 1, axis=dim)], axis=dim)
    after = jnp.concatenate([lax.slice_in_dim(low_face, 1, size, axis=dim), from_next], axis=dim)
    return before, after


def assemble_dim(values, node_dim, elem_dim, axis):
    low_face = lax.index_in_dim(values, 0, node_dim, keepdims=False)
    high_face = lax.index_in_dim(values, 4, node_dim, keepdims=False)
    face_elem_dim = elem_dim - 1
    if axis is None:
        size = low_face.shape[face_elem_dim]
        zero = jnp.zeros_like(lax.slice_in_dim(low_face, 0, 1, axis=face_elem_dim))
        before = jnp.concatenate(
            [zero, lax.slice_in_dim(high_face, 0, size - 1, axis=face_elem_dim)], axis=face_elem_dim
        )
        after = jnp.concatenate(
            [lax.slice_in_dim(low_face, 1, size, axis=face_elem_dim), zero], axis=face_elem_dim
        )
    else:
        before, after = shift_faces(low_face, high_face, face_elem_dim, axis)
    new_low = jnp.expand_dims(low_face + before, node_dim)
    new_high = jnp.expand_dims(high_face + after, node_dim)
    middle = lax.slice_in_dim(values, 1, 4, axis=node_dim)
    return jnp.concatenate([new_low, middle, new_high], axis=node_dim)


def assemble(values):
    values = assemble_dim(values, 1, 5, "gx")
    values = assemble_dim(values, 2, 6, "gy")
    values = assemble_dim(values, 3, 4, None)
    return values


def per_device(
    flow_state,
    drag_coefficient,
    wet_mask,
    target_elem,
    target_node,
    displacement,
    previous,
    density,
    lame_first,
    shear_modulus,
):
    buoyancy = 1.0 - 0.6 * wet_mask.astype(jnp.float32)
    fields = flow_state
    depth = FLOW_STEPS
    cell_rows = fields.shape[1]
    cell_cols = fields.shape[2]
    bundle = jnp.concatenate([fields, buoyancy[None], drag_coefficient[None]], axis=0)
    first_force = internal_force(displacement, lame_first, shear_modulus)
    rows_widened = extended(bundle, (("gx", 1),), depth)
    rows_widened, first_force = lax.optimization_barrier((rows_widened, first_force))
    widened = extended(rows_widened, (("gy", 2),), depth)
    row_ids = lax.axis_index("gx") * cell_rows + jnp.arange(cell_rows + 2 * depth) - depth
    col_ids = lax.axis_index("gy") * cell_cols + jnp.arange(cell_cols + 2 * depth) - depth
    row_inside = (row_ids >= 0) & (row_ids < cell_rows * lax.axis_size("gx"))
    col_inside = (col_ids >= 0) & (col_ids < cell_cols * lax.axis_size("gy"))
    inside = (row_inside[:, None] & col_inside[None, :]).astype(jnp.float32)
    wide_fields = widened[:6]
    wide_buoyancy = widened[6]
    wide_drag = widened[7]
    for counter in range(FLOW_STEPS):
        stacked = pressures(wide_fields, wide_buoyancy)
        padded = jnp.pad(stacked, ((0, 0), (1, 1), (1, 1)))
        wide_fields = advance(stacked, padded, wide_drag) * inside[None]
    fields = wide_fields[:, depth : depth + cell_rows, depth : depth + cell_cols]
    traction = basal_traction(fields, buoyancy, drag_coefficient)
    mass_parts = density[None, None, None, None] * weights_cube()[None]
    joined = assemble(jnp.concatenate([first_force, mass_parts], axis=0))
    traction, joined = lax.optimization_barrier((traction, joined))
    block_rows = displacement.shape[5]
    block_cols = displacement.shape[6]
    devices_y = lax.axis_size("gy")
    surface_cols = block_cols * devices_y
    elem_row = target_elem // surface_cols
    elem_col = target_elem % surface_cols
    local_x = elem_row - block_rows * lax.axis_index("gx") + 1
    local_y = elem_col - block_cols * lax.axis_index("gy") + 1
    point_rows = 4 * (block_rows + 2) + 1
    point_cols = 4 * (block_cols + 2) + 1
    span_x = 4 * block_rows
    span_y = 4 * block_cols
    point_row = 4 * local_x + target_node // 5
    point_col = 4 * local_y + target_node % 5
    slots = -(-point_cols // 16) * 16
    grid = load_table(traction, point_row, point_col, slots)
    grid = grid.reshape(slots, 3, 2, ROW_PAD)
    grid = grid[:, :, 0] + grid[:, :, 1]
    overlap_x = point_rows - span_x
    overlap_y = point_cols - span_y
    from_next = shift_block(grid[:, :, :overlap_x], "gx", False)
    from_prev = shift_block(grid[:, :, span_x:point_rows], "gx", True)
    grid = (
        grid
        + jnp.pad(from_next, ((0, 0), (0, 0), (span_x, ROW_PAD - point_rows)))
        + jnp.pad(from_prev, ((0, 0), (0, 0), (0, ROW_PAD - overlap_x)))
    )
    from_next = shift_block(grid[:overlap_y], "gy", False)
    from_prev = shift_block(grid[span_y:point_cols], "gy", True)
    grid = (
        grid
        + jnp.pad(from_next, ((span_y, slots - point_cols), (0, 0), (0, 0)))
        + jnp.pad(from_prev, ((0, slots - overlap_y), (0, 0), (0, 0)))
    )
    by_col = jnp.concatenate(
        [
            grid[4 : 4 + span_y].reshape(block_cols, 4, 3, ROW_PAD),
            grid[8 : 8 + span_y].reshape(block_cols, 4, 3, ROW_PAD)[:, 0:1],
        ],
        axis=1,
    )
    by_row = jnp.concatenate(
        [
            by_col[..., 4 : 4 + span_x].reshape(block_cols, 5, 3, block_rows, 4),
            by_col[..., 8 : 8 + span_x].reshape(block_cols, 5, 3, block_rows, 4)[..., 0:1],
        ],
        axis=-1,
    )
    surface_load = jnp.transpose(by_row, (2, 4, 1, 3, 0))
    surface_load = surface_load.reshape(3, 5, 5, 1, 1, block_rows, block_cols)
    layers = displacement.shape[4]
    load_padded = jnp.pad(
        surface_load,
        ((0, 0), (0, 0), (0, 0), (0, 4), (0, layers - 1), (0, 0), (0, 0)),
    )
    masses = joined[3:]
    current = displacement
    for counter in range(SOLID_STEPS):
        if counter == 0:
            force = joined[:3]
        else:
            force = assemble(internal_force(current, lame_first, shear_modulus))
        acceleration = (force + load_padded) / masses
        advanced = 2.0 * current - previous + solid_dt * solid_dt * acceleration
        previous = current
        current = advanced
    return (fields, current, previous)


def solution(mesh):
    return jax.shard_map(
        per_device,
        mesh=mesh,
        in_specs=(
            P(None, "gx", "gy"),
            P("gx", "gy"),
            P("gx", "gy"),
            P("gx", "gy"),
            P("gx", "gy"),
            P(None, None, None, None, None, "gx", "gy"),
            P(None, None, None, None, None, "gx", "gy"),
            P(None, "gx", "gy"),
            P(None, "gx", "gy"),
            P(None, "gx", "gy"),
        ),
        out_specs=(
            P(None, "gx", "gy"),
            P(None, None, None, None, None, "gx", "gy"),
            P(None, None, None, None, None, "gx", "gy"),
        ),
        check_vma=False,
    )
```

```python
import jax
import jax.numpy as jnp
import numpy as np
from jax import lax
from jax.experimental import pallas as pl
from jax.experimental.pallas import tpu as pltpu
from jax.sharding import PartitionSpec as P

FLOW_STEPS = 4
SOLID_STEPS = 2


gll_points = np.array([-1.0, -np.sqrt(3.0 / 7.0), 0.0, np.sqrt(3.0 / 7.0), 1.0])
gll_weights = np.array([0.1, 49.0 / 90.0, 32.0 / 45.0, 49.0 / 90.0, 0.1])
flow_dt = 0.4
diffusion = 0.2
coupling = 0.5
upper_gravity = 0.8
density_ratio = 0.7
speed_floor = 0.0001
load_factor = 4.0
solid_dt = 0.04

ROW_PAD = 24
CHUNK = 1024
ROW_BLOCK = 8


def extended(block, sides, width):
    for axis, dim in sides:
        count = lax.axis_size(axis)
        forward = [(i, i + 1) for i in range(count - 1)]
        backward = [(target, source) for source, target in forward]
        low = lax.ppermute(
            lax.slice_in_dim(block, block.shape[dim] - width, None, axis=dim), axis, forward
        )
        high = lax.ppermute(lax.slice_in_dim(block, 0, width, axis=dim), axis, backward)
        block = jnp.concatenate([low, block, high], axis=dim)
    return block


def legendre_four(x):
    return (35.0 * x**4 - 30.0 * x**2 + 3.0) / 8.0


def derivative_table():
    result = np.zeros((5, 5))
    for i in range(5):
        for j in range(5):
            if i != j:
                result[i, j] = (
                    legendre_four(gll_points[i])
                    / legendre_four(gll_points[j])
                    / (gll_points[i] - gll_points[j])
                )
    result[0, 0] = -5.0
    result[4, 4] = 5.0
    return result


TABLE = derivative_table().astype(np.float32)


def pressures(fields, buoyancy):
    press_one = buoyancy * (fields[0] + fields[1])
    press_two = upper_gravity * (density_ratio * fields[0] + fields[1])
    return jnp.concatenate([fields, press_one[None], press_two[None]], axis=0)


def advance(center, padded, drag_coefficient):
    ahead_x = padded[:, 2:, 1:-1]
    behind_x = padded[:, :-2, 1:-1]
    ahead_y = padded[:, 1:-1, 2:]
    behind_y = padded[:, 1:-1, :-2]
    slope_x = 0.5 * (ahead_x - behind_x)
    slope_y = 0.5 * (ahead_y - behind_y)
    spread = ahead_x + behind_x + ahead_y + behind_y - 4.0 * center
    flow_speed = jnp.sqrt(center[2] * center[2] + center[3] * center[3] + speed_floor)
    dense_depth = center[0] - flow_dt * (slope_x[2] + slope_y[3]) + diffusion * spread[0]
    light_depth = center[1] - flow_dt * (slope_x[4] + slope_y[5]) + diffusion * spread[1]
    dense_xmom = (
        center[2]
        - flow_dt
        * (
            slope_x[6]
            + drag_coefficient * flow_speed * center[2]
            + coupling * (center[2] - center[4])
        )
        + diffusion * spread[2]
    )
    dense_ymom = (
        center[3]
        - flow_dt
        * (
            slope_y[6]
            + drag_coefficient * flow_speed * center[3]
            + coupling * (center[3] - center[5])
        )
        + diffusion * spread[3]
    )
    light_xmom = (
        center[4]
        - flow_dt * (slope_x[7] + coupling * (center[4] - center[2]))
        + diffusion * spread[4]
    )
    light_ymom = (
        center[5]
        - flow_dt * (slope_y[7] + coupling * (center[5] - center[3]))
        + diffusion * spread[5]
    )
    return jnp.stack([dense_depth, light_depth, dense_xmom, dense_ymom, light_xmom, light_ymom])


def basal_traction(fields, buoyancy, drag_coefficient):
    flow_speed = jnp.sqrt(fields[2] * fields[2] + fields[3] * fields[3] + speed_floor)
    press_one = buoyancy * (fields[0] + fields[1])
    rubbing = load_factor * drag_coefficient * flow_speed
    return jnp.stack([rubbing * fields[2], rubbing * fields[3], -load_factor * press_one])


def weights_cube():
    cube = (
        gll_weights.reshape(5, 1, 1) * gll_weights.reshape(1, 5, 1) * gll_weights.reshape(1, 1, 5)
    )
    return jnp.asarray(cube.reshape(5, 5, 5, 1, 1, 1), jnp.float32)


def load_kernel(trac_ref, row_ref, col_ref, out_ref):
    slots = out_ref.shape[0]

    @pl.when(pl.program_id(0) == 0)
    def _():
        out_ref[...] = jnp.zeros(out_ref.shape, out_ref.dtype)

    def row_body(r, carry):
        for c0 in range(0, row_ref.shape[1], CHUNK):
            point_row = row_ref[pl.ds(r, 1), pl.ds(c0, CHUNK)]
            point_col = col_ref[pl.ds(r, 1), pl.ds(c0, CHUNK)]
            hit = lax.broadcasted_iota(jnp.int32, (ROW_PAD, CHUNK), 0) == point_row
            pieces = []
            for k in range(3):
                value = trac_ref[k, pl.ds(r, 1), pl.ds(c0, CHUNK)]
                high = value.astype(jnp.bfloat16).astype(jnp.float32)
                low = value - high
                pieces.append(jnp.where(hit, high, 0.0))
                pieces.append(jnp.where(hit, low, 0.0))
            weighted = jnp.concatenate(pieces, axis=0).astype(jnp.bfloat16)
            onehot = (
                lax.broadcasted_iota(jnp.int32, (slots, CHUNK), 0) == point_col
            ).astype(jnp.bfloat16)
            out_ref[...] += lax.dot_general(
                onehot,
                weighted,
                (((1,), (1,)), ((), ())),
                preferred_element_type=jnp.float32,
            )
        return carry

    lax.fori_loop(0, ROW_BLOCK, row_body, 0)


def load_table(trac, point_row, point_col, slots):
    rows, cols = point_row.shape
    return pl.pallas_call(
        load_kernel,
        grid=(rows // ROW_BLOCK,),
        in_specs=[
            pl.BlockSpec((3, ROW_BLOCK, cols), lambda g: (0, g, 0)),
            pl.BlockSpec((ROW_BLOCK, cols), lambda g: (g, 0)),
            pl.BlockSpec((ROW_BLOCK, cols), lambda g: (g, 0)),
        ],
        out_specs=pl.BlockSpec((slots, 6 * ROW_PAD), lambda g: (0, 0)),
        out_shape=jax.ShapeDtypeStruct((slots, 6 * ROW_PAD), jnp.float32),
        compiler_params=pltpu.CompilerParams(dimension_semantics=("arbitrary",)),
    )(trac, point_row, point_col)


def along(x, axis, transpose):
    table = TABLE.T if transpose else TABLE
    shape = [1] * (x.ndim + 1)
    shape[axis] = 5
    shape[axis + 1] = 5
    coefs = jnp.asarray(table.reshape(shape))
    return jnp.sum(coefs * jnp.expand_dims(x, axis), axis=axis + 1)


def internal_force(values, lame_first, shear_modulus):
    weights_3d = weights_cube()
    gradients = [[along(values[i], j, False) for i in range(3)] for j in range(3)]
    divergence = gradients[0][0] + gradients[1][1] + gradients[2][2]
    forces = []
    for i in range(3):
        pulled = None
        for j in range(3):
            stress = shear_modulus * (gradients[j][i] + gradients[i][j])
            if i == j:
                stress = stress + lame_first * divergence
            term = along(weights_3d * stress, j, True)
            pulled = term if pulled is None else pulled + term
        forces.append(-pulled)
    return jnp.stack(forces)


def shift_block(block, axis, forward):
    count = lax.axis_size(axis)
    pairs = [(i, i + 1) for i in range(count - 1)]
    if not forward:
        pairs = [(target, source) for source, target in pairs]
    return lax.ppermute(block, axis, pairs)


def shift_faces(low_face, high_face, dim, axis):
    count = lax.axis_size(axis)
    forward = [(i, i + 1) for i in range(count - 1)]
    backward = [(target, source) for source, target in forward]
    size = low_face.shape[dim]
    from_prev = lax.ppermute(lax.slice_in_dim(high_face, size - 1, size, axis=dim), axis, forward)
    from_next = lax.ppermute(lax.slice_in_dim(low_face, 0, 1, axis=dim), axis, backward)
    before = jnp.concatenate([from_prev, lax.slice_in_dim(high_face, 0, size - 1, axis=dim)], axis=dim)
    after = jnp.concatenate([lax.slice_in_dim(low_face, 1, size, axis=dim), from_next], axis=dim)
    return before, after


def assemble_dim(values, node_dim, elem_dim, axis):
    low_face = lax.index_in_dim(values, 0, node_dim, keepdims=False)
    high_face = lax.index_in_dim(values, 4, node_dim, keepdims=False)
    face_elem_dim = elem_dim - 1
    if axis is None:
        size = low_face.shape[face_elem_dim]
        zero = jnp.zeros_like(lax.slice_in_dim(low_face, 0, 1, axis=face_elem_dim))
        before = jnp.concatenate(
            [zero, lax.slice_in_dim(high_face, 0, size - 1, axis=face_elem_dim)], axis=face_elem_dim
        )
        after = jnp.concatenate(
            [lax.slice_in_dim(low_face, 1, size, axis=face_elem_dim), zero], axis=face_elem_dim
        )
    else:
        before, after = shift_faces(low_face, high_face, face_elem_dim, axis)
    new_low = jnp.expand_dims(low_face + before, node_dim)
    new_high = jnp.expand_dims(high_face + after, node_dim)
    middle = lax.slice_in_dim(values, 1, 4, axis=node_dim)
    return jnp.concatenate([new_low, middle, new_high], axis=node_dim)


def assemble(values):
    values = assemble_dim(values, 1, 5, "gx")
    values = assemble_dim(values, 2, 6, "gy")
    values = assemble_dim(values, 3, 4, None)
    return values


def per_device(
    flow_state,
    drag_coefficient,
    wet_mask,
    target_elem,
    target_node,
    displacement,
    previous,
    density,
    lame_first,
    shear_modulus,
):
    buoyancy = 1.0 - 0.6 * wet_mask.astype(jnp.float32)
    fields = flow_state
    depth = FLOW_STEPS
    cell_rows = fields.shape[1]
    cell_cols = fields.shape[2]
    bundle = jnp.concatenate([fields, buoyancy[None], drag_coefficient[None]], axis=0)
    first_force = internal_force(displacement, lame_first, shear_modulus)
    rows_widened = extended(bundle, (("gx", 1),), depth)
    rows_widened, first_force = lax.optimization_barrier((rows_widened, first_force))
    widened = extended(rows_widened, (("gy", 2),), depth)
    row_ids = lax.axis_index("gx") * cell_rows + jnp.arange(cell_rows + 2 * depth) - depth
    col_ids = lax.axis_index("gy") * cell_cols + jnp.arange(cell_cols + 2 * depth) - depth
    row_inside = (row_ids >= 0) & (row_ids < cell_rows * lax.axis_size("gx"))
    col_inside = (col_ids >= 0) & (col_ids < cell_cols * lax.axis_size("gy"))
    inside = (row_inside[:, None] & col_inside[None, :]).astype(jnp.float32)
    wide_fields = widened[:6]
    wide_buoyancy = widened[6]
    wide_drag = widened[7]
    for counter in range(FLOW_STEPS):
        stacked = pressures(wide_fields, wide_buoyancy)
        padded = jnp.pad(stacked, ((0, 0), (1, 1), (1, 1)))
        wide_fields = advance(stacked, padded, wide_drag) * inside[None]
    fields = wide_fields[:, depth : depth + cell_rows, depth : depth + cell_cols]
    traction = basal_traction(fields, buoyancy, drag_coefficient)
    mass_parts = density[None, None, None, None] * weights_cube()[None]
    joined = assemble_dim(jnp.concatenate([first_force, mass_parts], axis=0), 1, 5, "gx")
    traction, joined = lax.optimization_barrier((traction, joined))
    joined = assemble_dim(assemble_dim(joined, 2, 6, "gy"), 3, 4, None)
    block_rows = displacement.shape[5]
    block_cols = displacement.shape[6]
    devices_y = lax.axis_size("gy")
    surface_cols = block_cols * devices_y
    elem_row = target_elem // surface_cols
    elem_col = target_elem % surface_cols
    local_x = elem_row - block_rows * lax.axis_index("gx") + 1
    local_y = elem_col - block_cols * lax.axis_index("gy") + 1
    point_rows = 4 * (block_rows + 2) + 1
    point_cols = 4 * (block_cols + 2) + 1
    span_x = 4 * block_rows
    span_y = 4 * block_cols
    point_row = 4 * local_x + target_node // 5
    point_col = 4 * local_y + target_node % 5
    slots = -(-point_cols // 16) * 16
    grid = load_table(traction, point_row, point_col, slots)
    grid = grid.reshape(slots, 3, 2, ROW_PAD)
    grid = grid[:, :, 0] + grid[:, :, 1]
    overlap_x = point_rows - span_x
    overlap_y = point_cols - span_y
    from_next = shift_block(grid[:, :, :overlap_x], "gx", False)
    from_prev = shift_block(grid[:, :, span_x:point_rows], "gx", True)
    grid = (
        grid
        + jnp.pad(from_next, ((0, 0), (0, 0), (span_x, ROW_PAD - point_rows)))
        + jnp.pad(from_prev, ((0, 0), (0, 0), (0, ROW_PAD - overlap_x)))
    )
    from_next = shift_block(grid[:overlap_y], "gy", False)
    from_prev = shift_block(grid[span_y:point_cols], "gy", True)
    grid = (
        grid
        + jnp.pad(from_next, ((span_y, slots - point_cols), (0, 0), (0, 0)))
        + jnp.pad(from_prev, ((0, slots - overlap_y), (0, 0), (0, 0)))
    )
    by_col = jnp.concatenate(
        [
            grid[4 : 4 + span_y].reshape(block_cols, 4, 3, ROW_PAD),
            grid[8 : 8 + span_y].reshape(block_cols, 4, 3, ROW_PAD)[:, 0:1],
        ],
        axis=1,
    )
    by_row = jnp.concatenate(
        [
            by_col[..., 4 : 4 + span_x].reshape(block_cols, 5, 3, block_rows, 4),
            by_col[..., 8 : 8 + span_x].reshape(block_cols, 5, 3, block_rows, 4)[..., 0:1],
        ],
        axis=-1,
    )
    surface_load = jnp.transpose(by_row, (2, 4, 1, 3, 0))
    surface_load = surface_load.reshape(3, 5, 5, 1, 1, block_rows, block_cols)
    layers = displacement.shape[4]
    load_padded = jnp.pad(
        surface_load,
        ((0, 0), (0, 0), (0, 0), (0, 4), (0, layers - 1), (0, 0), (0, 0)),
    )
    masses = joined[3:]
    current = displacement
    for counter in range(SOLID_STEPS):
        if counter == 0:
            force = joined[:3]
        else:
            force = assemble(internal_force(current, lame_first, shear_modulus))
        acceleration = (force + load_padded) / masses
        advanced = 2.0 * current - previous + solid_dt * solid_dt * acceleration
        previous = current
        current = advanced
    return (fields, current, previous)


def solution(mesh):
    return jax.shard_map(
        per_device,
        mesh=mesh,
        in_specs=(
            P(None, "gx", "gy"),
            P("gx", "gy"),
            P("gx", "gy"),
            P("gx", "gy"),
            P("gx", "gy"),
            P(None, None, None, None, None, "gx", "gy"),
            P(None, None, None, None, None, "gx", "gy"),
            P(None, "gx", "gy"),
            P(None, "gx", "gy"),
            P(None, "gx", "gy"),
        ),
        out_specs=(
            P(None, "gx", "gy"),
            P(None, None, None, None, None, "gx", "gy"),
            P(None, None, None, None, None, "gx", "gy"),
        ),
        check_vma=False,
    )
```

```python
import jax
import jax.numpy as jnp
import numpy as np
from jax import lax
from jax.experimental import pallas as pl
from jax.experimental.pallas import tpu as pltpu
from jax.sharding import PartitionSpec as P

FLOW_STEPS = 4
SOLID_STEPS = 2


gll_points = np.array([-1.0, -np.sqrt(3.0 / 7.0), 0.0, np.sqrt(3.0 / 7.0), 1.0])
gll_weights = np.array([0.1, 49.0 / 90.0, 32.0 / 45.0, 49.0 / 90.0, 0.1])
flow_dt = 0.4
diffusion = 0.2
coupling = 0.5
upper_gravity = 0.8
density_ratio = 0.7
speed_floor = 0.0001
load_factor = 4.0
solid_dt = 0.04

ROW_PAD = 24
CHUNK = 1024
ROW_BLOCK = 8


def extended(block, sides, width):
    for axis, dim in sides:
        count = lax.axis_size(axis)
        forward = [(i, i + 1) for i in range(count - 1)]
        backward = [(target, source) for source, target in forward]
        low = lax.ppermute(
            lax.slice_in_dim(block, block.shape[dim] - width, None, axis=dim), axis, forward
        )
        high = lax.ppermute(lax.slice_in_dim(block, 0, width, axis=dim), axis, backward)
        block = jnp.concatenate([low, block, high], axis=dim)
    return block


def legendre_four(x):
    return (35.0 * x**4 - 30.0 * x**2 + 3.0) / 8.0


def derivative_table():
    result = np.zeros((5, 5))
    for i in range(5):
        for j in range(5):
            if i != j:
                result[i, j] = (
                    legendre_four(gll_points[i])
                    / legendre_four(gll_points[j])
                    / (gll_points[i] - gll_points[j])
                )
    result[0, 0] = -5.0
    result[4, 4] = 5.0
    return result


TABLE = derivative_table().astype(np.float32)


def pressures(fields, buoyancy):
    press_one = buoyancy * (fields[0] + fields[1])
    press_two = upper_gravity * (density_ratio * fields[0] + fields[1])
    return jnp.concatenate([fields, press_one[None], press_two[None]], axis=0)


def advance(center, padded, drag_coefficient):
    ahead_x = padded[:, 2:, 1:-1]
    behind_x = padded[:, :-2, 1:-1]
    ahead_y = padded[:, 1:-1, 2:]
    behind_y = padded[:, 1:-1, :-2]
    slope_x = 0.5 * (ahead_x - behind_x)
    slope_y = 0.5 * (ahead_y - behind_y)
    spread = ahead_x + behind_x + ahead_y + behind_y - 4.0 * center
    flow_speed = jnp.sqrt(center[2] * center[2] + center[3] * center[3] + speed_floor)
    dense_depth = center[0] - flow_dt * (slope_x[2] + slope_y[3]) + diffusion * spread[0]
    light_depth = center[1] - flow_dt * (slope_x[4] + slope_y[5]) + diffusion * spread[1]
    dense_xmom = (
        center[2]
        - flow_dt
        * (
            slope_x[6]
            + drag_coefficient * flow_speed * center[2]
            + coupling * (center[2] - center[4])
        )
        + diffusion * spread[2]
    )
    dense_ymom = (
        center[3]
        - flow_dt
        * (
            slope_y[6]
            + drag_coefficient * flow_speed * center[3]
            + coupling * (center[3] - center[5])
        )
        + diffusion * spread[3]
    )
    light_xmom = (
        center[4]
        - flow_dt * (slope_x[7] + coupling * (center[4] - center[2]))
        + diffusion * spread[4]
    )
    light_ymom = (
        center[5]
        - flow_dt * (slope_y[7] + coupling * (center[5] - center[3]))
        + diffusion * spread[5]
    )
    return jnp.stack([dense_depth, light_depth, dense_xmom, dense_ymom, light_xmom, light_ymom])


def basal_traction(fields, buoyancy, drag_coefficient):
    flow_speed = jnp.sqrt(fields[2] * fields[2] + fields[3] * fields[3] + speed_floor)
    press_one = buoyancy * (fields[0] + fields[1])
    rubbing = load_factor * drag_coefficient * flow_speed
    return jnp.stack([rubbing * fields[2], rubbing * fields[3], -load_factor * press_one])


def weights_cube():
    cube = (
        gll_weights.reshape(5, 1, 1) * gll_weights.reshape(1, 5, 1) * gll_weights.reshape(1, 1, 5)
    )
    return jnp.asarray(cube.reshape(5, 5, 5, 1, 1, 1), jnp.float32)


def load_kernel(trac_ref, row_ref, col_ref, out_ref):
    slots = out_ref.shape[0]

    @pl.when(pl.program_id(0) == 0)
    def _():
        out_ref[...] = jnp.zeros(out_ref.shape, out_ref.dtype)

    def row_body(r, carry):
        for c0 in range(0, row_ref.shape[1], CHUNK):
            point_row = row_ref[pl.ds(r, 1), pl.ds(c0, CHUNK)]
            point_col = col_ref[pl.ds(r, 1), pl.ds(c0, CHUNK)]
            hit = lax.broadcasted_iota(jnp.int32, (ROW_PAD, CHUNK), 0) == point_row
            pieces = []
            for k in range(3):
                value = trac_ref[k, pl.ds(r, 1), pl.ds(c0, CHUNK)]
                high = value.astype(jnp.bfloat16).astype(jnp.float32)
                low = value - high
                pieces.append(jnp.where(hit, high, 0.0))
                pieces.append(jnp.where(hit, low, 0.0))
            weighted = jnp.concatenate(pieces, axis=0).astype(jnp.bfloat16)
            onehot = (
                lax.broadcasted_iota(jnp.int32, (slots, CHUNK), 0) == point_col
            ).astype(jnp.bfloat16)
            out_ref[...] += lax.dot_general(
                onehot,
                weighted,
                (((1,), (1,)), ((), ())),
                preferred_element_type=jnp.float32,
            )
        return carry

    lax.fori_loop(0, ROW_BLOCK, row_body, 0)


def load_table(trac, point_row, point_col, slots):
    rows, cols = point_row.shape
    return pl.pallas_call(
        load_kernel,
        grid=(rows // ROW_BLOCK,),
        in_specs=[
            pl.BlockSpec((3, ROW_BLOCK, cols), lambda g: (0, g, 0)),
            pl.BlockSpec((ROW_BLOCK, cols), lambda g: (g, 0)),
            pl.BlockSpec((ROW_BLOCK, cols), lambda g: (g, 0)),
        ],
        out_specs=pl.BlockSpec((slots, 6 * ROW_PAD), lambda g: (0, 0)),
        out_shape=jax.ShapeDtypeStruct((slots, 6 * ROW_PAD), jnp.float32),
        compiler_params=pltpu.CompilerParams(dimension_semantics=("arbitrary",)),
    )(trac, point_row, point_col)


def along(x, axis, transpose):
    table = TABLE.T if transpose else TABLE
    shape = [1] * (x.ndim + 1)
    shape[axis] = 5
    shape[axis + 1] = 5
    coefs = jnp.asarray(table.reshape(shape))
    return jnp.sum(coefs * jnp.expand_dims(x, axis), axis=axis + 1)


def internal_force(values, lame_first, shear_modulus):
    weights_3d = weights_cube()
    gradients = [[along(values[i], j, False) for i in range(3)] for j in range(3)]
    divergence = gradients[0][0] + gradients[1][1] + gradients[2][2]
    forces = []
    for i in range(3):
        pulled = None
        for j in range(3):
            stress = shear_modulus * (gradients[j][i] + gradients[i][j])
            if i == j:
                stress = stress + lame_first * divergence
            term = along(weights_3d * stress, j, True)
            pulled = term if pulled is None else pulled + term
        forces.append(-pulled)
    return jnp.stack(forces)


def shift_block(block, axis, forward):
    count = lax.axis_size(axis)
    pairs = [(i, i + 1) for i in range(count - 1)]
    if not forward:
        pairs = [(target, source) for source, target in pairs]
    return lax.ppermute(block, axis, pairs)


def send_many(arrays, axis, forward):
    count = lax.axis_size(axis)
    pairs = [(i, i + 1) for i in range(count - 1)]
    if not forward:
        pairs = [(target, source) for source, target in pairs]
    flat = jnp.concatenate([a.reshape(-1) for a in arrays])
    moved = lax.ppermute(flat, axis, pairs)
    out = []
    offset = 0
    for a in arrays:
        out.append(moved[offset : offset + a.size].reshape(a.shape))
        offset += a.size
    return out


def assemble_dim(values, node_dim, elem_dim, axis, extra_forward=(), extra_backward=()):
    low_face = lax.index_in_dim(values, 0, node_dim, keepdims=False)
    high_face = lax.index_in_dim(values, 4, node_dim, keepdims=False)
    face_elem_dim = elem_dim - 1
    size = low_face.shape[face_elem_dim]
    got_forward, got_backward = [], []
    if axis is None:
        zero = jnp.zeros_like(lax.slice_in_dim(low_face, 0, 1, axis=face_elem_dim))
        from_prev, from_next = zero, zero
    else:
        got_forward = send_many(
            [lax.slice_in_dim(high_face, size - 1, size, axis=face_elem_dim)] + list(extra_forward),
            axis,
            True,
        )
        got_backward = send_many(
            [lax.slice_in_dim(low_face, 0, 1, axis=face_elem_dim)] + list(extra_backward),
            axis,
            False,
        )
        from_prev = got_forward[0]
        from_next = got_backward[0]
    before = jnp.concatenate(
        [from_prev, lax.slice_in_dim(high_face, 0, size - 1, axis=face_elem_dim)], axis=face_elem_dim
    )
    after = jnp.concatenate(
        [lax.slice_in_dim(low_face, 1, size, axis=face_elem_dim), from_next], axis=face_elem_dim
    )
    new_low = jnp.expand_dims(low_face + before, node_dim)
    new_high = jnp.expand_dims(high_face + after, node_dim)
    middle = lax.slice_in_dim(values, 1, 4, axis=node_dim)
    result = jnp.concatenate([new_low, middle, new_high], axis=node_dim)
    if extra_forward or extra_backward:
        return result, got_forward[1:], got_backward[1:]
    return result


def assemble(values):
    values = assemble_dim(values, 1, 5, "gx")
    values = assemble_dim(values, 2, 6, "gy")
    values = assemble_dim(values, 3, 4, None)
    return values


def per_device(
    flow_state,
    drag_coefficient,
    wet_mask,
    target_elem,
    target_node,
    displacement,
    previous,
    density,
    lame_first,
    shear_modulus,
):
    buoyancy = 1.0 - 0.6 * wet_mask.astype(jnp.float32)
    fields = flow_state
    depth = FLOW_STEPS
    cell_rows = fields.shape[1]
    cell_cols = fields.shape[2]
    bundle = jnp.concatenate([fields, buoyancy[None], drag_coefficient[None]], axis=0)
    first_force = internal_force(displacement, lame_first, shear_modulus)
    rows_widened = extended(bundle, (("gx", 1),), depth)
    rows_widened, first_force = lax.optimization_barrier((rows_widened, first_force))
    widened = extended(rows_widened, (("gy", 2),), depth)
    row_ids = lax.axis_index("gx") * cell_rows + jnp.arange(cell_rows + 2 * depth) - depth
    col_ids = lax.axis_index("gy") * cell_cols + jnp.arange(cell_cols + 2 * depth) - depth
    row_inside = (row_ids >= 0) & (row_ids < cell_rows * lax.axis_size("gx"))
    col_inside = (col_ids >= 0) & (col_ids < cell_cols * lax.axis_size("gy"))
    inside = (row_inside[:, None] & col_inside[None, :]).astype(jnp.float32)
    wide_fields = widened[:6]
    wide_buoyancy = widened[6]
    wide_drag = widened[7]
    for counter in range(FLOW_STEPS):
        stacked = pressures(wide_fields, wide_buoyancy)
        padded = jnp.pad(stacked, ((0, 0), (1, 1), (1, 1)))
        wide_fields = advance(stacked, padded, wide_drag) * inside[None]
    fields = wide_fields[:, depth : depth + cell_rows, depth : depth + cell_cols]
    traction = basal_traction(fields, buoyancy, drag_coefficient)
    block_rows = displacement.shape[5]
    block_cols = displacement.shape[6]
    devices_y = lax.axis_size("gy")
    surface_cols = block_cols * devices_y
    elem_row = target_elem // surface_cols
    elem_col = target_elem % surface_cols
    local_x = elem_row - block_rows * lax.axis_index("gx") + 1
    local_y = elem_col - block_cols * lax.axis_index("gy") + 1
    point_rows = 4 * (block_rows + 2) + 1
    point_cols = 4 * (block_cols + 2) + 1
    span_x = 4 * block_rows
    span_y = 4 * block_cols
    point_row = 4 * local_x + target_node // 5
    point_col = 4 * local_y + target_node % 5
    slots = -(-point_cols // 16) * 16
    grid = load_table(traction, point_row, point_col, slots)
    grid = grid.reshape(slots, 3, 2, ROW_PAD)
    grid = grid[:, :, 0] + grid[:, :, 1]
    overlap_x = point_rows - span_x
    overlap_y = point_cols - span_y
    mass_parts = density[None, None, None, None] * weights_cube()[None]
    joined = jnp.concatenate([first_force, mass_parts], axis=0)
    joined, (from_prev,), (from_next,) = assemble_dim(
        joined, 1, 5, "gx", [grid[:, :, span_x:point_rows]], [grid[:, :, :overlap_x]]
    )
    grid = (
        grid
        + jnp.pad(from_next, ((0, 0), (0, 0), (span_x, ROW_PAD - point_rows)))
        + jnp.pad(from_prev, ((0, 0), (0, 0), (0, ROW_PAD - overlap_x)))
    )
    joined, (from_prev,), (from_next,) = assemble_dim(
        joined, 2, 6, "gy", [grid[span_y:point_cols]], [grid[:overlap_y]]
    )
    grid = (
        grid
        + jnp.pad(from_next, ((span_y, slots - point_cols), (0, 0), (0, 0)))
        + jnp.pad(from_prev, ((0, slots - overlap_y), (0, 0), (0, 0)))
    )
    joined = assemble_dim(joined, 3, 4, None)
    by_col = jnp.concatenate(
        [
            grid[4 : 4 + span_y].reshape(block_cols, 4, 3, ROW_PAD),
            grid[8 : 8 + span_y].reshape(block_cols, 4, 3, ROW_PAD)[:, 0:1],
        ],
        axis=1,
    )
    by_row = jnp.concatenate(
        [
            by_col[..., 4 : 4 + span_x].reshape(block_cols, 5, 3, block_rows, 4),
            by_col[..., 8 : 8 + span_x].reshape(block_cols, 5, 3, block_rows, 4)[..., 0:1],
        ],
        axis=-1,
    )
    surface_load = jnp.transpose(by_row, (2, 4, 1, 3, 0))
    surface_load = surface_load.reshape(3, 5, 5, 1, 1, block_rows, block_cols)
    layers = displacement.shape[4]
    load_padded = jnp.pad(
        surface_load,
        ((0, 0), (0, 0), (0, 0), (0, 4), (0, layers - 1), (0, 0), (0, 0)),
    )
    masses = joined[3:]
    current = displacement
    for counter in range(SOLID_STEPS):
        if counter == 0:
            force = joined[:3]
        else:
            force = assemble(internal_force(current, lame_first, shear_modulus))
        acceleration = (force + load_padded) / masses
        advanced = 2.0 * current - previous + solid_dt * solid_dt * acceleration
        previous = current
        current = advanced
    return (fields, current, previous)


def solution(mesh):
    return jax.shard_map(
        per_device,
        mesh=mesh,
        in_specs=(
            P(None, "gx", "gy"),
            P("gx", "gy"),
            P("gx", "gy"),
            P("gx", "gy"),
            P("gx", "gy"),
            P(None, None, None, None, None, "gx", "gy"),
            P(None, None, None, None, None, "gx", "gy"),
            P(None, "gx", "gy"),
            P(None, "gx", "gy"),
            P(None, "gx", "gy"),
        ),
        out_specs=(
            P(None, "gx", "gy"),
            P(None, None, None, None, None, "gx", "gy"),
            P(None, None, None, None, None, "gx", "gy"),
        ),
        check_vma=False,
    )
```

```python
import jax
import jax.numpy as jnp
import numpy as np
from jax import lax
from jax.experimental import pallas as pl
from jax.experimental.pallas import tpu as pltpu
from jax.sharding import PartitionSpec as P

FLOW_STEPS = 4
SOLID_STEPS = 2


gll_points = np.array([-1.0, -np.sqrt(3.0 / 7.0), 0.0, np.sqrt(3.0 / 7.0), 1.0])
gll_weights = np.array([0.1, 49.0 / 90.0, 32.0 / 45.0, 49.0 / 90.0, 0.1])
flow_dt = 0.4
diffusion = 0.2
coupling = 0.5
upper_gravity = 0.8
density_ratio = 0.7
speed_floor = 0.0001
load_factor = 4.0
solid_dt = 0.04

ROW_PAD = 24
CHUNK = 1024
ROW_BLOCK = 8


def extended(block, sides, width):
    for axis, dim in sides:
        count = lax.axis_size(axis)
        forward = [(i, i + 1) for i in range(count - 1)]
        backward = [(target, source) for source, target in forward]
        low = lax.ppermute(
            lax.slice_in_dim(block, block.shape[dim] - width, None, axis=dim), axis, forward
        )
        high = lax.ppermute(lax.slice_in_dim(block, 0, width, axis=dim), axis, backward)
        block = jnp.concatenate([low, block, high], axis=dim)
    return block


def legendre_four(x):
    return (35.0 * x**4 - 30.0 * x**2 + 3.0) / 8.0


def derivative_table():
    result = np.zeros((5, 5))
    for i in range(5):
        for j in range(5):
            if i != j:
                result[i, j] = (
                    legendre_four(gll_points[i])
                    / legendre_four(gll_points[j])
                    / (gll_points[i] - gll_points[j])
                )
    result[0, 0] = -5.0
    result[4, 4] = 5.0
    return result


TABLE = derivative_table().astype(np.float32)


def pressures(fields, buoyancy):
    press_one = buoyancy * (fields[0] + fields[1])
    press_two = upper_gravity * (density_ratio * fields[0] + fields[1])
    return jnp.concatenate([fields, press_one[None], press_two[None]], axis=0)


def advance(center, padded, drag_coefficient):
    ahead_x = padded[:, 2:, 1:-1]
    behind_x = padded[:, :-2, 1:-1]
    ahead_y = padded[:, 1:-1, 2:]
    behind_y = padded[:, 1:-1, :-2]
    slope_x = 0.5 * (ahead_x - behind_x)
    slope_y = 0.5 * (ahead_y - behind_y)
    spread = ahead_x + behind_x + ahead_y + behind_y - 4.0 * center
    flow_speed = jnp.sqrt(center[2] * center[2] + center[3] * center[3] + speed_floor)
    dense_depth = center[0] - flow_dt * (slope_x[2] + slope_y[3]) + diffusion * spread[0]
    light_depth = center[1] - flow_dt * (slope_x[4] + slope_y[5]) + diffusion * spread[1]
    dense_xmom = (
        center[2]
        - flow_dt
        * (
            slope_x[6]
            + drag_coefficient * flow_speed * center[2]
            + coupling * (center[2] - center[4])
        )
        + diffusion * spread[2]
    )
    dense_ymom = (
        center[3]
        - flow_dt
        * (
            slope_y[6]
            + drag_coefficient * flow_speed * center[3]
            + coupling * (center[3] - center[5])
        )
        + diffusion * spread[3]
    )
    light_xmom = (
        center[4]
        - flow_dt * (slope_x[7] + coupling * (center[4] - center[2]))
        + diffusion * spread[4]
    )
    light_ymom = (
        center[5]
        - flow_dt * (slope_y[7] + coupling * (center[5] - center[3]))
        + diffusion * spread[5]
    )
    return jnp.stack([dense_depth, light_depth, dense_xmom, dense_ymom, light_xmom, light_ymom])


def basal_traction(fields, buoyancy, drag_coefficient):
    flow_speed = jnp.sqrt(fields[2] * fields[2] + fields[3] * fields[3] + speed_floor)
    press_one = buoyancy * (fields[0] + fields[1])
    rubbing = load_factor * drag_coefficient * flow_speed
    return jnp.stack([rubbing * fields[2], rubbing * fields[3], -load_factor * press_one])


def weights_cube():
    cube = (
        gll_weights.reshape(5, 1, 1) * gll_weights.reshape(1, 5, 1) * gll_weights.reshape(1, 1, 5)
    )
    return jnp.asarray(cube.reshape(5, 5, 5, 1, 1, 1), jnp.float32)


def load_kernel(trac_ref, row_ref, col_ref, out_ref):
    slots = out_ref.shape[0]

    @pl.when(pl.program_id(0) == 0)
    def _():
        out_ref[...] = jnp.zeros(out_ref.shape, out_ref.dtype)

    def row_body(r, carry):
        for c0 in range(0, row_ref.shape[1], CHUNK):
            point_row = row_ref[pl.ds(r, 1), pl.ds(c0, CHUNK)]
            point_col = col_ref[pl.ds(r, 1), pl.ds(c0, CHUNK)]
            hit = lax.broadcasted_iota(jnp.int32, (ROW_PAD, CHUNK), 0) == point_row
            pieces = []
            for k in range(3):
                value = trac_ref[k, pl.ds(r, 1), pl.ds(c0, CHUNK)]
                high = value.astype(jnp.bfloat16).astype(jnp.float32)
                low = value - high
                pieces.append(jnp.where(hit, high, 0.0))
                pieces.append(jnp.where(hit, low, 0.0))
            weighted = jnp.concatenate(pieces, axis=0).astype(jnp.bfloat16)
            onehot = (
                lax.broadcasted_iota(jnp.int32, (slots, CHUNK), 0) == point_col
            ).astype(jnp.bfloat16)
            out_ref[...] += lax.dot_general(
                onehot,
                weighted,
                (((1,), (1,)), ((), ())),
                preferred_element_type=jnp.float32,
            )
        return carry

    lax.fori_loop(0, ROW_BLOCK, row_body, 0)


def load_table(trac, point_row, point_col, slots):
    rows, cols = point_row.shape
    return pl.pallas_call(
        load_kernel,
        grid=(rows // ROW_BLOCK,),
        in_specs=[
            pl.BlockSpec((3, ROW_BLOCK, cols), lambda g: (0, g, 0)),
            pl.BlockSpec((ROW_BLOCK, cols), lambda g: (g, 0)),
            pl.BlockSpec((ROW_BLOCK, cols), lambda g: (g, 0)),
        ],
        out_specs=pl.BlockSpec((slots, 6 * ROW_PAD), lambda g: (0, 0)),
        out_shape=jax.ShapeDtypeStruct((slots, 6 * ROW_PAD), jnp.float32),
        compiler_params=pltpu.CompilerParams(dimension_semantics=("arbitrary",)),
    )(trac, point_row, point_col)


def along(x, axis, transpose):
    table = TABLE.T if transpose else TABLE
    shape = [1] * (x.ndim + 1)
    shape[axis] = 5
    shape[axis + 1] = 5
    coefs = jnp.asarray(table.reshape(shape))
    return jnp.sum(coefs * jnp.expand_dims(x, axis), axis=axis + 1)


def internal_force(values, lame_first, shear_modulus):
    shape = values.shape
    merged = shape[:4] + (shape[4] * shape[5], shape[6])
    values = values.reshape(merged)
    lame_first = lame_first.reshape(merged[4:])
    shear_modulus = shear_modulus.reshape(merged[4:])
    weights_3d = weights_cube().reshape(5, 5, 5, 1, 1)
    gradients = [[along(values[i], j, False) for i in range(3)] for j in range(3)]
    divergence = gradients[0][0] + gradients[1][1] + gradients[2][2]
    forces = []
    for i in range(3):
        pulled = None
        for j in range(3):
            stress = shear_modulus * (gradients[j][i] + gradients[i][j])
            if i == j:
                stress = stress + lame_first * divergence
            term = along(weights_3d * stress, j, True)
            pulled = term if pulled is None else pulled + term
        forces.append(-pulled)
    return jnp.stack(forces).reshape(shape)


def shift_block(block, axis, forward):
    count = lax.axis_size(axis)
    pairs = [(i, i + 1) for i in range(count - 1)]
    if not forward:
        pairs = [(target, source) for source, target in pairs]
    return lax.ppermute(block, axis, pairs)


def shift_faces(low_face, high_face, dim, axis):
    count = lax.axis_size(axis)
    forward = [(i, i + 1) for i in range(count - 1)]
    backward = [(target, source) for source, target in forward]
    size = low_face.shape[dim]
    from_prev = lax.ppermute(lax.slice_in_dim(high_face, size - 1, size, axis=dim), axis, forward)
    from_next = lax.ppermute(lax.slice_in_dim(low_face, 0, 1, axis=dim), axis, backward)
    before = jnp.concatenate([from_prev, lax.slice_in_dim(high_face, 0, size - 1, axis=dim)], axis=dim)
    after = jnp.concatenate([lax.slice_in_dim(low_face, 1, size, axis=dim), from_next], axis=dim)
    return before, after


def assemble_dim(values, node_dim, elem_dim, axis):
    low_face = lax.index_in_dim(values, 0, node_dim, keepdims=False)
    high_face = lax.index_in_dim(values, 4, node_dim, keepdims=False)
    face_elem_dim = elem_dim - 1
    if axis is None:
        size = low_face.shape[face_elem_dim]
        zero = jnp.zeros_like(lax.slice_in_dim(low_face, 0, 1, axis=face_elem_dim))
        before = jnp.concatenate(
            [zero, lax.slice_in_dim(high_face, 0, size - 1, axis=face_elem_dim)], axis=face_elem_dim
        )
        after = jnp.concatenate(
            [lax.slice_in_dim(low_face, 1, size, axis=face_elem_dim), zero], axis=face_elem_dim
        )
    else:
        before, after = shift_faces(low_face, high_face, face_elem_dim, axis)
    new_low = jnp.expand_dims(low_face + before, node_dim)
    new_high = jnp.expand_dims(high_face + after, node_dim)
    middle = lax.slice_in_dim(values, 1, 4, axis=node_dim)
    return jnp.concatenate([new_low, middle, new_high], axis=node_dim)


def assemble(values):
    values = assemble_dim(values, 1, 5, "gx")
    values = assemble_dim(values, 2, 6, "gy")
    values = assemble_dim(values, 3, 4, None)
    return values


def per_device(
    flow_state,
    drag_coefficient,
    wet_mask,
    target_elem,
    target_node,
    displacement,
    previous,
    density,
    lame_first,
    shear_modulus,
):
    buoyancy = 1.0 - 0.6 * wet_mask.astype(jnp.float32)
    fields = flow_state
    depth = FLOW_STEPS
    cell_rows = fields.shape[1]
    cell_cols = fields.shape[2]
    bundle = jnp.concatenate([fields, buoyancy[None], drag_coefficient[None]], axis=0)
    first_force = internal_force(displacement, lame_first, shear_modulus)
    rows_widened = extended(bundle, (("gx", 1),), depth)
    rows_widened, first_force = lax.optimization_barrier((rows_widened, first_force))
    widened = extended(rows_widened, (("gy", 2),), depth)
    row_ids = lax.axis_index("gx") * cell_rows + jnp.arange(cell_rows + 2 * depth) - depth
    col_ids = lax.axis_index("gy") * cell_cols + jnp.arange(cell_cols + 2 * depth) - depth
    row_inside = (row_ids >= 0) & (row_ids < cell_rows * lax.axis_size("gx"))
    col_inside = (col_ids >= 0) & (col_ids < cell_cols * lax.axis_size("gy"))
    inside = (row_inside[:, None] & col_inside[None, :]).astype(jnp.float32)
    wide_fields = widened[:6]
    wide_buoyancy = widened[6]
    wide_drag = widened[7]
    for counter in range(FLOW_STEPS):
        stacked = pressures(wide_fields, wide_buoyancy)
        padded = jnp.pad(stacked, ((0, 0), (1, 1), (1, 1)))
        wide_fields = advance(stacked, padded, wide_drag) * inside[None]
    fields = wide_fields[:, depth : depth + cell_rows, depth : depth + cell_cols]
    traction = basal_traction(fields, buoyancy, drag_coefficient)
    mass_parts = density[None, None, None, None] * weights_cube()[None]
    joined = assemble(jnp.concatenate([first_force, mass_parts], axis=0))
    traction, joined = lax.optimization_barrier((traction, joined))
    block_rows = displacement.shape[5]
    block_cols = displacement.shape[6]
    devices_y = lax.axis_size("gy")
    surface_cols = block_cols * devices_y
    elem_row = target_elem // surface_cols
    elem_col = target_elem % surface_cols
    local_x = elem_row - block_rows * lax.axis_index("gx") + 1
    local_y = elem_col - block_cols * lax.axis_index("gy") + 1
    point_rows = 4 * (block_rows + 2) + 1
    point_cols = 4 * (block_cols + 2) + 1
    span_x = 4 * block_rows
    span_y = 4 * block_cols
    point_row = 4 * local_x + target_node // 5
    point_col = 4 * local_y + target_node % 5
    slots = -(-point_cols // 16) * 16
    grid = load_table(traction, point_row, point_col, slots)
    grid = grid.reshape(slots, 3, 2, ROW_PAD)
    grid = grid[:, :, 0] + grid[:, :, 1]
    overlap_x = point_rows - span_x
    overlap_y = point_cols - span_y
    from_next = shift_block(grid[:, :, :overlap_x], "gx", False)
    from_prev = shift_block(grid[:, :, span_x:point_rows], "gx", True)
    grid = (
        grid
        + jnp.pad(from_next, ((0, 0), (0, 0), (span_x, ROW_PAD - point_rows)))
        + jnp.pad(from_prev, ((0, 0), (0, 0), (0, ROW_PAD - overlap_x)))
    )
    from_next = shift_block(grid[:overlap_y], "gy", False)
    from_prev = shift_block(grid[span_y:point_cols], "gy", True)
    grid = (
        grid
        + jnp.pad(from_next, ((span_y, slots - point_cols), (0, 0), (0, 0)))
        + jnp.pad(from_prev, ((0, slots - overlap_y), (0, 0), (0, 0)))
    )
    by_col = jnp.concatenate(
        [
            grid[4 : 4 + span_y].reshape(block_cols, 4, 3, ROW_PAD),
            grid[8 : 8 + span_y].reshape(block_cols, 4, 3, ROW_PAD)[:, 0:1],
        ],
        axis=1,
    )
    by_row = jnp.concatenate(
        [
            by_col[..., 4 : 4 + span_x].reshape(block_cols, 5, 3, block_rows, 4),
            by_col[..., 8 : 8 + span_x].reshape(block_cols, 5, 3, block_rows, 4)[..., 0:1],
        ],
        axis=-1,
    )
    surface_load = jnp.transpose(by_row, (2, 4, 1, 3, 0))
    surface_load = surface_load.reshape(3, 5, 5, 1, 1, block_rows, block_cols)
    layers = displacement.shape[4]
    load_padded = jnp.pad(
        surface_load,
        ((0, 0), (0, 0), (0, 0), (0, 4), (0, layers - 1), (0, 0), (0, 0)),
    )
    masses = joined[3:]
    current = displacement
    for counter in range(SOLID_STEPS):
        if counter == 0:
            force = joined[:3]
        else:
            force = assemble(internal_force(current, lame_first, shear_modulus))
        acceleration = (force + load_padded) / masses
        advanced = 2.0 * current - previous + solid_dt * solid_dt * acceleration
        previous = current
        current = advanced
    return (fields, current, previous)


def solution(mesh):
    return jax.shard_map(
        per_device,
        mesh=mesh,
        in_specs=(
            P(None, "gx", "gy"),
            P("gx", "gy"),
            P("gx", "gy"),
            P("gx", "gy"),
            P("gx", "gy"),
            P(None, None, None, None, None, "gx", "gy"),
            P(None, None, None, None, None, "gx", "gy"),
            P(None, "gx", "gy"),
            P(None, "gx", "gy"),
            P(None, "gx", "gy"),
        ),
        out_specs=(
            P(None, "gx", "gy"),
            P(None, None, None, None, None, "gx", "gy"),
            P(None, None, None, None, None, "gx", "gy"),
        ),
        check_vma=False,
    )
```

```python
import jax
import jax.numpy as jnp
import numpy as np
from jax import lax
from jax.experimental import pallas as pl
from jax.experimental.pallas import tpu as pltpu
from jax.sharding import PartitionSpec as P

FLOW_STEPS = 4
SOLID_STEPS = 2


gll_points = np.array([-1.0, -np.sqrt(3.0 / 7.0), 0.0, np.sqrt(3.0 / 7.0), 1.0])
gll_weights = np.array([0.1, 49.0 / 90.0, 32.0 / 45.0, 49.0 / 90.0, 0.1])
flow_dt = 0.4
diffusion = 0.2
coupling = 0.5
upper_gravity = 0.8
density_ratio = 0.7
speed_floor = 0.0001
load_factor = 4.0
solid_dt = 0.04

ROW_PAD = 24
CHUNK = 1024
ROW_BLOCK = 8


def extended(block, sides, width):
    for axis, dim in sides:
        count = lax.axis_size(axis)
        forward = [(i, i + 1) for i in range(count - 1)]
        backward = [(target, source) for source, target in forward]
        low = lax.ppermute(
            lax.slice_in_dim(block, block.shape[dim] - width, None, axis=dim), axis, forward
        )
        high = lax.ppermute(lax.slice_in_dim(block, 0, width, axis=dim), axis, backward)
        block = jnp.concatenate([low, block, high], axis=dim)
    return block


def legendre_four(x):
    return (35.0 * x**4 - 30.0 * x**2 + 3.0) / 8.0


def derivative_table():
    result = np.zeros((5, 5))
    for i in range(5):
        for j in range(5):
            if i != j:
                result[i, j] = (
                    legendre_four(gll_points[i])
                    / legendre_four(gll_points[j])
                    / (gll_points[i] - gll_points[j])
                )
    result[0, 0] = -5.0
    result[4, 4] = 5.0
    return result


TABLE = derivative_table().astype(np.float32)


def pressures(fields, buoyancy):
    press_one = buoyancy * (fields[0] + fields[1])
    press_two = upper_gravity * (density_ratio * fields[0] + fields[1])
    return jnp.concatenate([fields, press_one[None], press_two[None]], axis=0)


def advance(center, padded, drag_coefficient):
    ahead_x = padded[:, 2:, 1:-1]
    behind_x = padded[:, :-2, 1:-1]
    ahead_y = padded[:, 1:-1, 2:]
    behind_y = padded[:, 1:-1, :-2]
    slope_x = 0.5 * (ahead_x - behind_x)
    slope_y = 0.5 * (ahead_y - behind_y)
    spread = ahead_x + behind_x + ahead_y + behind_y - 4.0 * center
    flow_speed = jnp.sqrt(center[2] * center[2] + center[3] * center[3] + speed_floor)
    dense_depth = center[0] - flow_dt * (slope_x[2] + slope_y[3]) + diffusion * spread[0]
    light_depth = center[1] - flow_dt * (slope_x[4] + slope_y[5]) + diffusion * spread[1]
    dense_xmom = (
        center[2]
        - flow_dt
        * (
            slope_x[6]
            + drag_coefficient * flow_speed * center[2]
            + coupling * (center[2] - center[4])
        )
        + diffusion * spread[2]
    )
    dense_ymom = (
        center[3]
        - flow_dt
        * (
            slope_y[6]
            + drag_coefficient * flow_speed * center[3]
            + coupling * (center[3] - center[5])
        )
        + diffusion * spread[3]
    )
    light_xmom = (
        center[4]
        - flow_dt * (slope_x[7] + coupling * (center[4] - center[2]))
        + diffusion * spread[4]
    )
    light_ymom = (
        center[5]
        - flow_dt * (slope_y[7] + coupling * (center[5] - center[3]))
        + diffusion * spread[5]
    )
    return jnp.stack([dense_depth, light_depth, dense_xmom, dense_ymom, light_xmom, light_ymom])


def basal_traction(fields, buoyancy, drag_coefficient):
    flow_speed = jnp.sqrt(fields[2] * fields[2] + fields[3] * fields[3] + speed_floor)
    press_one = buoyancy * (fields[0] + fields[1])
    rubbing = load_factor * drag_coefficient * flow_speed
    return jnp.stack([rubbing * fields[2], rubbing * fields[3], -load_factor * press_one])


def weights_cube():
    cube = (
        gll_weights.reshape(5, 1, 1) * gll_weights.reshape(1, 5, 1) * gll_weights.reshape(1, 1, 5)
    )
    return jnp.asarray(cube.reshape(5, 5, 5, 1, 1, 1), jnp.float32)


def load_kernel(trac_ref, row_ref, col_ref, out_ref):
    slots = out_ref.shape[0]

    @pl.when(pl.program_id(0) == 0)
    def _():
        out_ref[...] = jnp.zeros(out_ref.shape, out_ref.dtype)

    def row_body(r, carry):
        for c0 in range(0, row_ref.shape[1], CHUNK):
            point_row = row_ref[pl.ds(r, 1), pl.ds(c0, CHUNK)]
            point_col = col_ref[pl.ds(r, 1), pl.ds(c0, CHUNK)]
            hit = lax.broadcasted_iota(jnp.int32, (ROW_PAD, CHUNK), 0) == point_row
            pieces = []
            for k in range(3):
                value = trac_ref[k, pl.ds(r, 1), pl.ds(c0, CHUNK)]
                high = value.astype(jnp.bfloat16).astype(jnp.float32)
                low = value - high
                pieces.append(jnp.where(hit, high, 0.0))
                pieces.append(jnp.where(hit, low, 0.0))
            weighted = jnp.concatenate(pieces, axis=0).astype(jnp.bfloat16)
            onehot = (
                lax.broadcasted_iota(jnp.int32, (slots, CHUNK), 0) == point_col
            ).astype(jnp.bfloat16)
            out_ref[...] += lax.dot_general(
                onehot,
                weighted,
                (((1,), (1,)), ((), ())),
                preferred_element_type=jnp.float32,
            )
        return carry

    lax.fori_loop(0, ROW_BLOCK, row_body, 0)


def load_table(trac, point_row, point_col, slots):
    rows, cols = point_row.shape
    return pl.pallas_call(
        load_kernel,
        grid=(rows // ROW_BLOCK,),
        in_specs=[
            pl.BlockSpec((3, ROW_BLOCK, cols), lambda g: (0, g, 0)),
            pl.BlockSpec((ROW_BLOCK, cols), lambda g: (g, 0)),
            pl.BlockSpec((ROW_BLOCK, cols), lambda g: (g, 0)),
        ],
        out_specs=pl.BlockSpec((slots, 6 * ROW_PAD), lambda g: (0, 0)),
        out_shape=jax.ShapeDtypeStruct((slots, 6 * ROW_PAD), jnp.float32),
        compiler_params=pltpu.CompilerParams(dimension_semantics=("arbitrary",)),
    )(trac, point_row, point_col)


def along(x, axis, transpose):
    table = TABLE.T if transpose else TABLE
    shape = [1] * (x.ndim + 1)
    shape[axis] = 5
    shape[axis + 1] = 5
    coefs = jnp.asarray(table.reshape(shape))
    return jnp.sum(coefs * jnp.expand_dims(x, axis), axis=axis + 1)


def internal_force(values, lame_first, shear_modulus):
    shape = values.shape
    merged = shape[:4] + (shape[4] * shape[5], shape[6])
    values = values.reshape(merged)
    lame_first = lame_first.reshape(merged[4:])
    shear_modulus = shear_modulus.reshape(merged[4:])
    weights_3d = weights_cube().reshape(5, 5, 5, 1, 1)
    gradients = [[along(values[i], j, False) for i in range(3)] for j in range(3)]
    divergence = gradients[0][0] + gradients[1][1] + gradients[2][2]
    forces = []
    for i in range(3):
        pulled = None
        for j in range(3):
            stress = shear_modulus * (gradients[j][i] + gradients[i][j])
            if i == j:
                stress = stress + lame_first * divergence
            term = along(weights_3d * stress, j, True)
            pulled = term if pulled is None else pulled + term
        forces.append(-pulled)
    return jnp.stack(forces).reshape(shape)


def shift_block(block, axis, forward):
    count = lax.axis_size(axis)
    pairs = [(i, i + 1) for i in range(count - 1)]
    if not forward:
        pairs = [(target, source) for source, target in pairs]
    return lax.ppermute(block, axis, pairs)


def shift_faces(low_face, high_face, dim, axis):
    count = lax.axis_size(axis)
    forward = [(i, i + 1) for i in range(count - 1)]
    backward = [(target, source) for source, target in forward]
    size = low_face.shape[dim]
    from_prev = lax.ppermute(lax.slice_in_dim(high_face, size - 1, size, axis=dim), axis, forward)
    from_next = lax.ppermute(lax.slice_in_dim(low_face, 0, 1, axis=dim), axis, backward)
    before = jnp.concatenate([from_prev, lax.slice_in_dim(high_face, 0, size - 1, axis=dim)], axis=dim)
    after = jnp.concatenate([lax.slice_in_dim(low_face, 1, size, axis=dim), from_next], axis=dim)
    return before, after


def assemble_dim(values, node_dim, elem_dim, axis):
    low_face = lax.index_in_dim(values, 0, node_dim, keepdims=False)
    high_face = lax.index_in_dim(values, 4, node_dim, keepdims=False)
    face_elem_dim = elem_dim - 1
    if axis is None:
        size = low_face.shape[face_elem_dim]
        zero = jnp.zeros_like(lax.slice_in_dim(low_face, 0, 1, axis=face_elem_dim))
        before = jnp.concatenate(
            [zero, lax.slice_in_dim(high_face, 0, size - 1, axis=face_elem_dim)], axis=face_elem_dim
        )
        after = jnp.concatenate(
            [lax.slice_in_dim(low_face, 1, size, axis=face_elem_dim), zero], axis=face_elem_dim
        )
    else:
        before, after = shift_faces(low_face, high_face, face_elem_dim, axis)
    new_low = jnp.expand_dims(low_face + before, node_dim)
    new_high = jnp.expand_dims(high_face + after, node_dim)
    middle = lax.slice_in_dim(values, 1, 4, axis=node_dim)
    return jnp.concatenate([new_low, middle, new_high], axis=node_dim)


def assemble(values):
    values = assemble_dim(values, 1, 5, "gx")
    values = assemble_dim(values, 2, 6, "gy")
    values = assemble_dim(values, 3, 4, None)
    return values


def per_device(
    flow_state,
    drag_coefficient,
    wet_mask,
    target_elem,
    target_node,
    displacement,
    previous,
    density,
    lame_first,
    shear_modulus,
):
    buoyancy = 1.0 - 0.6 * wet_mask.astype(jnp.float32)
    fields = flow_state
    depth = FLOW_STEPS
    cell_rows = fields.shape[1]
    cell_cols = fields.shape[2]
    bundle = jnp.concatenate([fields, buoyancy[None], drag_coefficient[None]], axis=0)
    first_force = internal_force(displacement, lame_first, shear_modulus)
    rows_widened = extended(bundle, (("gx", 1),), depth)
    rows_widened, first_force = lax.optimization_barrier((rows_widened, first_force))
    widened = extended(rows_widened, (("gy", 2),), depth)
    mass_parts = density[None, None, None, None] * weights_cube()[None]
    joined = assemble_dim(jnp.concatenate([first_force, mass_parts], axis=0), 1, 5, "gx")
    widened, joined = lax.optimization_barrier((widened, joined))
    row_ids = lax.axis_index("gx") * cell_rows + jnp.arange(cell_rows + 2 * depth) - depth
    col_ids = lax.axis_index("gy") * cell_cols + jnp.arange(cell_cols + 2 * depth) - depth
    row_inside = (row_ids >= 0) & (row_ids < cell_rows * lax.axis_size("gx"))
    col_inside = (col_ids >= 0) & (col_ids < cell_cols * lax.axis_size("gy"))
    inside = (row_inside[:, None] & col_inside[None, :]).astype(jnp.float32)
    wide_fields = widened[:6]
    wide_buoyancy = widened[6]
    wide_drag = widened[7]
    for counter in range(FLOW_STEPS):
        stacked = pressures(wide_fields, wide_buoyancy)
        padded = jnp.pad(stacked, ((0, 0), (1, 1), (1, 1)))
        wide_fields = advance(stacked, padded, wide_drag) * inside[None]
    fields = wide_fields[:, depth : depth + cell_rows, depth : depth + cell_cols]
    traction = basal_traction(fields, buoyancy, drag_coefficient)
    joined = assemble_dim(assemble_dim(joined, 2, 6, "gy"), 3, 4, None)
    traction, joined = lax.optimization_barrier((traction, joined))
    block_rows = displacement.shape[5]
    block_cols = displacement.shape[6]
    devices_y = lax.axis_size("gy")
    surface_cols = block_cols * devices_y
    elem_row = target_elem // surface_cols
    elem_col = target_elem % surface_cols
    local_x = elem_row - block_rows * lax.axis_index("gx") + 1
    local_y = elem_col - block_cols * lax.axis_index("gy") + 1
    point_rows = 4 * (block_rows + 2) + 1
    point_cols = 4 * (block_cols + 2) + 1
    span_x = 4 * block_rows
    span_y = 4 * block_cols
    point_row = 4 * local_x + target_node // 5
    point_col = 4 * local_y + target_node % 5
    slots = -(-point_cols // 16) * 16
    grid = load_table(traction, point_row, point_col, slots)
    grid = grid.reshape(slots, 3, 2, ROW_PAD)
    grid = grid[:, :, 0] + grid[:, :, 1]
    overlap_x = point_rows - span_x
    overlap_y = point_cols - span_y
    from_next = shift_block(grid[:, :, :overlap_x], "gx", False)
    from_prev = shift_block(grid[:, :, span_x:point_rows], "gx", True)
    grid = (
        grid
        + jnp.pad(from_next, ((0, 0), (0, 0), (span_x, ROW_PAD - point_rows)))
        + jnp.pad(from_prev, ((0, 0), (0, 0), (0, ROW_PAD - overlap_x)))
    )
    from_next = shift_block(grid[:overlap_y], "gy", False)
    from_prev = shift_block(grid[span_y:point_cols], "gy", True)
    grid = (
        grid
        + jnp.pad(from_next, ((span_y, slots - point_cols), (0, 0), (0, 0)))
        + jnp.pad(from_prev, ((0, slots - overlap_y), (0, 0), (0, 0)))
    )
    by_col = jnp.concatenate(
        [
            grid[4 : 4 + span_y].reshape(block_cols, 4, 3, ROW_PAD),
            grid[8 : 8 + span_y].reshape(block_cols, 4, 3, ROW_PAD)[:, 0:1],
        ],
        axis=1,
    )
    by_row = jnp.concatenate(
        [
            by_col[..., 4 : 4 + span_x].reshape(block_cols, 5, 3, block_rows, 4),
            by_col[..., 8 : 8 + span_x].reshape(block_cols, 5, 3, block_rows, 4)[..., 0:1],
        ],
        axis=-1,
    )
    surface_load = jnp.transpose(by_row, (2, 4, 1, 3, 0))
    surface_load = surface_load.reshape(3, 5, 5, 1, 1, block_rows, block_cols)
    layers = displacement.shape[4]
    load_padded = jnp.pad(
        surface_load,
        ((0, 0), (0, 0), (0, 0), (0, 4), (0, layers - 1), (0, 0), (0, 0)),
    )
    masses = joined[3:]
    current = displacement
    for counter in range(SOLID_STEPS):
        if counter == 0:
            force = joined[:3]
        else:
            force = assemble(internal_force(current, lame_first, shear_modulus))
        acceleration = (force + load_padded) / masses
        advanced = 2.0 * current - previous + solid_dt * solid_dt * acceleration
        previous = current
        current = advanced
    return (fields, current, previous)


def solution(mesh):
    return jax.shard_map(
        per_device,
        mesh=mesh,
        in_specs=(
            P(None, "gx", "gy"),
            P("gx", "gy"),
            P("gx", "gy"),
            P("gx", "gy"),
            P("gx", "gy"),
            P(None, None, None, None, None, "gx", "gy"),
            P(None, None, None, None, None, "gx", "gy"),
            P(None, "gx", "gy"),
            P(None, "gx", "gy"),
            P(None, "gx", "gy"),
        ),
        out_specs=(
            P(None, "gx", "gy"),
            P(None, None, None, None, None, "gx", "gy"),
            P(None, None, None, None, None, "gx", "gy"),
        ),
        check_vma=False,
    )
```

```python
import jax
import jax.numpy as jnp
import numpy as np
from jax import lax
from jax.experimental import pallas as pl
from jax.experimental.pallas import tpu as pltpu
from jax.sharding import PartitionSpec as P

FLOW_STEPS = 4
SOLID_STEPS = 2


gll_points = np.array([-1.0, -np.sqrt(3.0 / 7.0), 0.0, np.sqrt(3.0 / 7.0), 1.0])
gll_weights = np.array([0.1, 49.0 / 90.0, 32.0 / 45.0, 49.0 / 90.0, 0.1])
flow_dt = 0.4
diffusion = 0.2
coupling = 0.5
upper_gravity = 0.8
density_ratio = 0.7
speed_floor = 0.0001
load_factor = 4.0
solid_dt = 0.04

ROW_PAD = 24
CHUNK = 2048
ROW_BLOCK = 8


def extended(block, sides, width):
    for axis, dim in sides:
        count = lax.axis_size(axis)
        forward = [(i, i + 1) for i in range(count - 1)]
        backward = [(target, source) for source, target in forward]
        low = lax.ppermute(
            lax.slice_in_dim(block, block.shape[dim] - width, None, axis=dim), axis, forward
        )
        high = lax.ppermute(lax.slice_in_dim(block, 0, width, axis=dim), axis, backward)
        block = jnp.concatenate([low, block, high], axis=dim)
    return block


def legendre_four(x):
    return (35.0 * x**4 - 30.0 * x**2 + 3.0) / 8.0


def derivative_table():
    result = np.zeros((5, 5))
    for i in range(5):
        for j in range(5):
            if i != j:
                result[i, j] = (
                    legendre_four(gll_points[i])
                    / legendre_four(gll_points[j])
                    / (gll_points[i] - gll_points[j])
                )
    result[0, 0] = -5.0
    result[4, 4] = 5.0
    return result


TABLE = derivative_table().astype(np.float32)


def pressures(fields, buoyancy):
    press_one = buoyancy * (fields[0] + fields[1])
    press_two = upper_gravity * (density_ratio * fields[0] + fields[1])
    return jnp.concatenate([fields, press_one[None], press_two[None]], axis=0)


def advance(center, padded, drag_coefficient):
    ahead_x = padded[:, 2:, 1:-1]
    behind_x = padded[:, :-2, 1:-1]
    ahead_y = padded[:, 1:-1, 2:]
    behind_y = padded[:, 1:-1, :-2]
    slope_x = 0.5 * (ahead_x - behind_x)
    slope_y = 0.5 * (ahead_y - behind_y)
    spread = ahead_x + behind_x + ahead_y + behind_y - 4.0 * center
    flow_speed = jnp.sqrt(center[2] * center[2] + center[3] * center[3] + speed_floor)
    dense_depth = center[0] - flow_dt * (slope_x[2] + slope_y[3]) + diffusion * spread[0]
    light_depth = center[1] - flow_dt * (slope_x[4] + slope_y[5]) + diffusion * spread[1]
    dense_xmom = (
        center[2]
        - flow_dt
        * (
            slope_x[6]
            + drag_coefficient * flow_speed * center[2]
            + coupling * (center[2] - center[4])
        )
        + diffusion * spread[2]
    )
    dense_ymom = (
        center[3]
        - flow_dt
        * (
            slope_y[6]
            + drag_coefficient * flow_speed * center[3]
            + coupling * (center[3] - center[5])
        )
        + diffusion * spread[3]
    )
    light_xmom = (
        center[4]
        - flow_dt * (slope_x[7] + coupling * (center[4] - center[2]))
        + diffusion * spread[4]
    )
    light_ymom = (
        center[5]
        - flow_dt * (slope_y[7] + coupling * (center[5] - center[3]))
        + diffusion * spread[5]
    )
    return jnp.stack([dense_depth, light_depth, dense_xmom, dense_ymom, light_xmom, light_ymom])


def basal_traction(fields, buoyancy, drag_coefficient):
    flow_speed = jnp.sqrt(fields[2] * fields[2] + fields[3] * fields[3] + speed_floor)
    press_one = buoyancy * (fields[0] + fields[1])
    rubbing = load_factor * drag_coefficient * flow_speed
    return jnp.stack([rubbing * fields[2], rubbing * fields[3], -load_factor * press_one])


def weights_cube():
    cube = (
        gll_weights.reshape(5, 1, 1) * gll_weights.reshape(1, 5, 1) * gll_weights.reshape(1, 1, 5)
    )
    return jnp.asarray(cube.reshape(5, 5, 5, 1, 1, 1), jnp.float32)


def load_kernel(trac_ref, row_ref, col_ref, out_ref):
    slots = out_ref.shape[0]

    @pl.when(pl.program_id(0) == 0)
    def _():
        out_ref[...] = jnp.zeros(out_ref.shape, out_ref.dtype)

    def row_body(r, carry):
        for c0 in range(0, row_ref.shape[1], CHUNK):
            point_row = row_ref[pl.ds(r, 1), pl.ds(c0, CHUNK)]
            point_col = col_ref[pl.ds(r, 1), pl.ds(c0, CHUNK)]
            hit = lax.broadcasted_iota(jnp.int32, (ROW_PAD, CHUNK), 0) == point_row
            pieces = []
            for k in range(3):
                value = trac_ref[k, pl.ds(r, 1), pl.ds(c0, CHUNK)]
                high = value.astype(jnp.bfloat16).astype(jnp.float32)
                low = value - high
                pieces.append(jnp.where(hit, high, 0.0))
                pieces.append(jnp.where(hit, low, 0.0))
            weighted = jnp.concatenate(pieces, axis=0).astype(jnp.bfloat16)
            onehot = (
                lax.broadcasted_iota(jnp.int32, (slots, CHUNK), 0) == point_col
            ).astype(jnp.bfloat16)
            out_ref[...] += lax.dot_general(
                onehot,
                weighted,
                (((1,), (1,)), ((), ())),
                preferred_element_type=jnp.float32,
            )
        return carry

    lax.fori_loop(0, ROW_BLOCK, row_body, 0)


def load_table(trac, point_row, point_col, slots):
    rows, cols = point_row.shape
    return pl.pallas_call(
        load_kernel,
        grid=(rows // ROW_BLOCK,),
        in_specs=[
            pl.BlockSpec((3, ROW_BLOCK, cols), lambda g: (0, g, 0)),
            pl.BlockSpec((ROW_BLOCK, cols), lambda g: (g, 0)),
            pl.BlockSpec((ROW_BLOCK, cols), lambda g: (g, 0)),
        ],
        out_specs=pl.BlockSpec((slots, 6 * ROW_PAD), lambda g: (0, 0)),
        out_shape=jax.ShapeDtypeStruct((slots, 6 * ROW_PAD), jnp.float32),
        compiler_params=pltpu.CompilerParams(dimension_semantics=("arbitrary",)),
    )(trac, point_row, point_col)


def along(x, axis, transpose):
    table = TABLE.T if transpose else TABLE
    shape = [1] * (x.ndim + 1)
    shape[axis] = 5
    shape[axis + 1] = 5
    coefs = jnp.asarray(table.reshape(shape))
    return jnp.sum(coefs * jnp.expand_dims(x, axis), axis=axis + 1)


def internal_force(values, lame_first, shear_modulus):
    shape = values.shape
    merged = shape[:4] + (shape[4] * shape[5], shape[6])
    values = values.reshape(merged)
    lame_first = lame_first.reshape(merged[4:])
    shear_modulus = shear_modulus.reshape(merged[4:])
    weights_3d = weights_cube().reshape(5, 5, 5, 1, 1)
    gradients = [[along(values[i], j, False) for i in range(3)] for j in range(3)]
    divergence = gradients[0][0] + gradients[1][1] + gradients[2][2]
    forces = []
    for i in range(3):
        pulled = None
        for j in range(3):
            stress = shear_modulus * (gradients[j][i] + gradients[i][j])
            if i == j:
                stress = stress + lame_first * divergence
            term = along(weights_3d * stress, j, True)
            pulled = term if pulled is None else pulled + term
        forces.append(-pulled)
    return jnp.stack(forces).reshape(shape)


def shift_block(block, axis, forward):
    count = lax.axis_size(axis)
    pairs = [(i, i + 1) for i in range(count - 1)]
    if not forward:
        pairs = [(target, source) for source, target in pairs]
    return lax.ppermute(block, axis, pairs)


def shift_faces(low_face, high_face, dim, axis):
    count = lax.axis_size(axis)
    forward = [(i, i + 1) for i in range(count - 1)]
    backward = [(target, source) for source, target in forward]
    size = low_face.shape[dim]
    from_prev = lax.ppermute(lax.slice_in_dim(high_face, size - 1, size, axis=dim), axis, forward)
    from_next = lax.ppermute(lax.slice_in_dim(low_face, 0, 1, axis=dim), axis, backward)
    before = jnp.concatenate([from_prev, lax.slice_in_dim(high_face, 0, size - 1, axis=dim)], axis=dim)
    after = jnp.concatenate([lax.slice_in_dim(low_face, 1, size, axis=dim), from_next], axis=dim)
    return before, after


def assemble_dim(values, node_dim, elem_dim, axis):
    low_face = lax.index_in_dim(values, 0, node_dim, keepdims=False)
    high_face = lax.index_in_dim(values, 4, node_dim, keepdims=False)
    face_elem_dim = elem_dim - 1
    if axis is None:
        size = low_face.shape[face_elem_dim]
        zero = jnp.zeros_like(lax.slice_in_dim(low_face, 0, 1, axis=face_elem_dim))
        before = jnp.concatenate(
            [zero, lax.slice_in_dim(high_face, 0, size - 1, axis=face_elem_dim)], axis=face_elem_dim
        )
        after = jnp.concatenate(
            [lax.slice_in_dim(low_face, 1, size, axis=face_elem_dim), zero], axis=face_elem_dim
        )
    else:
        before, after = shift_faces(low_face, high_face, face_elem_dim, axis)
    new_low = jnp.expand_dims(low_face + before, node_dim)
    new_high = jnp.expand_dims(high_face + after, node_dim)
    middle = lax.slice_in_dim(values, 1, 4, axis=node_dim)
    return jnp.concatenate([new_low, middle, new_high], axis=node_dim)


def assemble(values):
    values = assemble_dim(values, 1, 5, "gx")
    values = assemble_dim(values, 2, 6, "gy")
    values = assemble_dim(values, 3, 4, None)
    return values


def per_device(
    flow_state,
    drag_coefficient,
    wet_mask,
    target_elem,
    target_node,
    displacement,
    previous,
    density,
    lame_first,
    shear_modulus,
):
    buoyancy = 1.0 - 0.6 * wet_mask.astype(jnp.float32)
    fields = flow_state
    depth = FLOW_STEPS
    cell_rows = fields.shape[1]
    cell_cols = fields.shape[2]
    bundle = jnp.concatenate([fields, buoyancy[None], drag_coefficient[None]], axis=0)
    first_force = internal_force(displacement, lame_first, shear_modulus)
    rows_widened = extended(bundle, (("gx", 1),), depth)
    rows_widened, first_force = lax.optimization_barrier((rows_widened, first_force))
    widened = extended(rows_widened, (("gy", 2),), depth)
    row_ids = lax.axis_index("gx") * cell_rows + jnp.arange(cell_rows + 2 * depth) - depth
    col_ids = lax.axis_index("gy") * cell_cols + jnp.arange(cell_cols + 2 * depth) - depth
    row_inside = (row_ids >= 0) & (row_ids < cell_rows * lax.axis_size("gx"))
    col_inside = (col_ids >= 0) & (col_ids < cell_cols * lax.axis_size("gy"))
    inside = (row_inside[:, None] & col_inside[None, :]).astype(jnp.float32)
    wide_fields = widened[:6]
    wide_buoyancy = widened[6]
    wide_drag = widened[7]
    for counter in range(FLOW_STEPS):
        stacked = pressures(wide_fields, wide_buoyancy)
        padded = jnp.pad(stacked, ((0, 0), (1, 1), (1, 1)))
        wide_fields = advance(stacked, padded, wide_drag) * inside[None]
    fields = wide_fields[:, depth : depth + cell_rows, depth : depth + cell_cols]
    traction = basal_traction(fields, buoyancy, drag_coefficient)
    mass_parts = density[None, None, None, None] * weights_cube()[None]
    joined = assemble(jnp.concatenate([first_force, mass_parts], axis=0))
    traction, joined = lax.optimization_barrier((traction, joined))
    block_rows = displacement.shape[5]
    block_cols = displacement.shape[6]
    devices_y = lax.axis_size("gy")
    surface_cols = block_cols * devices_y
    elem_row = target_elem // surface_cols
    elem_col = target_elem % surface_cols
    local_x = elem_row - block_rows * lax.axis_index("gx") + 1
    local_y = elem_col - block_cols * lax.axis_index("gy") + 1
    point_rows = 4 * (block_rows + 2) + 1
    point_cols = 4 * (block_cols + 2) + 1
    span_x = 4 * block_rows
    span_y = 4 * block_cols
    point_row = 4 * local_x + target_node // 5
    point_col = 4 * local_y + target_node % 5
    slots = -(-point_cols // 16) * 16
    grid = load_table(traction, point_row, point_col, slots)
    grid = grid.reshape(slots, 3, 2, ROW_PAD)
    grid = grid[:, :, 0] + grid[:, :, 1]
    overlap_x = point_rows - span_x
    overlap_y = point_cols - span_y
    from_next = shift_block(grid[:, :, :overlap_x], "gx", False)
    from_prev = shift_block(grid[:, :, span_x:point_rows], "gx", True)
    grid = (
        grid
        + jnp.pad(from_next, ((0, 0), (0, 0), (span_x, ROW_PAD - point_rows)))
        + jnp.pad(from_prev, ((0, 0), (0, 0), (0, ROW_PAD - overlap_x)))
    )
    from_next = shift_block(grid[:overlap_y], "gy", False)
    from_prev = shift_block(grid[span_y:point_cols], "gy", True)
    grid = (
        grid
        + jnp.pad(from_next, ((span_y, slots - point_cols), (0, 0), (0, 0)))
        + jnp.pad(from_prev, ((0, slots - overlap_y), (0, 0), (0, 0)))
    )
    by_col = jnp.concatenate(
        [
            grid[4 : 4 + span_y].reshape(block_cols, 4, 3, ROW_PAD),
            grid[8 : 8 + span_y].reshape(block_cols, 4, 3, ROW_PAD)[:, 0:1],
        ],
        axis=1,
    )
    by_row = jnp.concatenate(
        [
            by_col[..., 4 : 4 + span_x].reshape(block_cols, 5, 3, block_rows, 4),
            by_col[..., 8 : 8 + span_x].reshape(block_cols, 5, 3, block_rows, 4)[..., 0:1],
        ],
        axis=-1,
    )
    surface_load = jnp.transpose(by_row, (2, 4, 1, 3, 0))
    surface_load = surface_load.reshape(3, 5, 5, 1, 1, block_rows, block_cols)
    layers = displacement.shape[4]
    load_padded = jnp.pad(
        surface_load,
        ((0, 0), (0, 0), (0, 0), (0, 4), (0, layers - 1), (0, 0), (0, 0)),
    )
    masses = joined[3:]
    current = displacement
    for counter in range(SOLID_STEPS):
        if counter == 0:
            force = joined[:3]
        else:
            force = assemble(internal_force(current, lame_first, shear_modulus))
        acceleration = (force + load_padded) / masses
        advanced = 2.0 * current - previous + solid_dt * solid_dt * acceleration
        previous = current
        current = advanced
    return (fields, current, previous)


def solution(mesh):
    return jax.shard_map(
        per_device,
        mesh=mesh,
        in_specs=(
            P(None, "gx", "gy"),
            P("gx", "gy"),
            P("gx", "gy"),
            P("gx", "gy"),
            P("gx", "gy"),
            P(None, None, None, None, None, "gx", "gy"),
            P(None, None, None, None, None, "gx", "gy"),
            P(None, "gx", "gy"),
            P(None, "gx", "gy"),
            P(None, "gx", "gy"),
        ),
        out_specs=(
            P(None, "gx", "gy"),
            P(None, None, None, None, None, "gx", "gy"),
            P(None, None, None, None, None, "gx", "gy"),
        ),
        check_vma=False,
    )
```

```python
import jax
import jax.numpy as jnp
import numpy as np
from jax import lax
from jax.experimental import pallas as pl
from jax.experimental.pallas import tpu as pltpu
from jax.sharding import PartitionSpec as P

FLOW_STEPS = 4
SOLID_STEPS = 2


gll_points = np.array([-1.0, -np.sqrt(3.0 / 7.0), 0.0, np.sqrt(3.0 / 7.0), 1.0])
gll_weights = np.array([0.1, 49.0 / 90.0, 32.0 / 45.0, 49.0 / 90.0, 0.1])
flow_dt = 0.4
diffusion = 0.2
coupling = 0.5
upper_gravity = 0.8
density_ratio = 0.7
speed_floor = 0.0001
load_factor = 4.0
solid_dt = 0.04

ROW_PAD = 24
CHUNK = 2048
ROW_BLOCK = 8


def extended(block, sides, width):
    for axis, dim in sides:
        count = lax.axis_size(axis)
        forward = [(i, i + 1) for i in range(count - 1)]
        backward = [(target, source) for source, target in forward]
        low = lax.ppermute(
            lax.slice_in_dim(block, block.shape[dim] - width, None, axis=dim), axis, forward
        )
        high = lax.ppermute(lax.slice_in_dim(block, 0, width, axis=dim), axis, backward)
        block = jnp.concatenate([low, block, high], axis=dim)
    return block


def legendre_four(x):
    return (35.0 * x**4 - 30.0 * x**2 + 3.0) / 8.0


def derivative_table():
    result = np.zeros((5, 5))
    for i in range(5):
        for j in range(5):
            if i != j:
                result[i, j] = (
                    legendre_four(gll_points[i])
                    / legendre_four(gll_points[j])
                    / (gll_points[i] - gll_points[j])
                )
    result[0, 0] = -5.0
    result[4, 4] = 5.0
    return result


TABLE = derivative_table().astype(np.float32)


def pressures(fields, buoyancy):
    press_one = buoyancy * (fields[0] + fields[1])
    press_two = upper_gravity * (density_ratio * fields[0] + fields[1])
    return jnp.concatenate([fields, press_one[None], press_two[None]], axis=0)


def advance(center, padded, drag_coefficient):
    ahead_x = padded[:, 2:, 1:-1]
    behind_x = padded[:, :-2, 1:-1]
    ahead_y = padded[:, 1:-1, 2:]
    behind_y = padded[:, 1:-1, :-2]
    slope_x = 0.5 * (ahead_x - behind_x)
    slope_y = 0.5 * (ahead_y - behind_y)
    spread = ahead_x + behind_x + ahead_y + behind_y - 4.0 * center
    flow_speed = jnp.sqrt(center[2] * center[2] + center[3] * center[3] + speed_floor)
    dense_depth = center[0] - flow_dt * (slope_x[2] + slope_y[3]) + diffusion * spread[0]
    light_depth = center[1] - flow_dt * (slope_x[4] + slope_y[5]) + diffusion * spread[1]
    dense_xmom = (
        center[2]
        - flow_dt
        * (
            slope_x[6]
            + drag_coefficient * flow_speed * center[2]
            + coupling * (center[2] - center[4])
        )
        + diffusion * spread[2]
    )
    dense_ymom = (
        center[3]
        - flow_dt
        * (
            slope_y[6]
            + drag_coefficient * flow_speed * center[3]
            + coupling * (center[3] - center[5])
        )
        + diffusion * spread[3]
    )
    light_xmom = (
        center[4]
        - flow_dt * (slope_x[7] + coupling * (center[4] - center[2]))
        + diffusion * spread[4]
    )
    light_ymom = (
        center[5]
        - flow_dt * (slope_y[7] + coupling * (center[5] - center[3]))
        + diffusion * spread[5]
    )
    return jnp.stack([dense_depth, light_depth, dense_xmom, dense_ymom, light_xmom, light_ymom])


def basal_traction(fields, buoyancy, drag_coefficient):
    flow_speed = jnp.sqrt(fields[2] * fields[2] + fields[3] * fields[3] + speed_floor)
    press_one = buoyancy * (fields[0] + fields[1])
    rubbing = load_factor * drag_coefficient * flow_speed
    return jnp.stack([rubbing * fields[2], rubbing * fields[3], -load_factor * press_one])


def weights_cube():
    cube = (
        gll_weights.reshape(5, 1, 1) * gll_weights.reshape(1, 5, 1) * gll_weights.reshape(1, 1, 5)
    )
    return jnp.asarray(cube.reshape(5, 5, 5, 1, 1, 1), jnp.float32)


def load_kernel(trac_ref, row_ref, col_ref, out_ref):
    slots = out_ref.shape[0]

    @pl.when(pl.program_id(0) == 0)
    def _():
        out_ref[...] = jnp.zeros(out_ref.shape, out_ref.dtype)

    def row_body(r, carry):
        for c0 in range(0, row_ref.shape[1], CHUNK):
            point_row = row_ref[pl.ds(r, 1), pl.ds(c0, CHUNK)]
            point_col = col_ref[pl.ds(r, 1), pl.ds(c0, CHUNK)]
            hit = lax.broadcasted_iota(jnp.int32, (ROW_PAD, CHUNK), 0) == point_row
            pieces = []
            for k in range(3):
                value = trac_ref[k, pl.ds(r, 1), pl.ds(c0, CHUNK)]
                high = value.astype(jnp.bfloat16).astype(jnp.float32)
                low = value - high
                pieces.append(jnp.where(hit, high, 0.0))
                pieces.append(jnp.where(hit, low, 0.0))
            weighted = jnp.concatenate(pieces, axis=0).astype(jnp.bfloat16)
            onehot = (
                lax.broadcasted_iota(jnp.int32, (slots, CHUNK), 0) == point_col
            ).astype(jnp.bfloat16)
            out_ref[...] += lax.dot_general(
                onehot,
                weighted,
                (((1,), (1,)), ((), ())),
                preferred_element_type=jnp.float32,
            )
        return carry

    lax.fori_loop(0, ROW_BLOCK, row_body, 0)


def load_table(trac, point_row, point_col, slots):
    rows, cols = point_row.shape
    return pl.pallas_call(
        load_kernel,
        grid=(rows // ROW_BLOCK,),
        in_specs=[
            pl.BlockSpec((3, ROW_BLOCK, cols), lambda g: (0, g, 0)),
            pl.BlockSpec((ROW_BLOCK, cols), lambda g: (g, 0)),
            pl.BlockSpec((ROW_BLOCK, cols), lambda g: (g, 0)),
        ],
        out_specs=pl.BlockSpec((slots, 6 * ROW_PAD), lambda g: (0, 0)),
        out_shape=jax.ShapeDtypeStruct((slots, 6 * ROW_PAD), jnp.float32),
        compiler_params=pltpu.CompilerParams(dimension_semantics=("arbitrary",)),
    )(trac, point_row, point_col)


def along(x, axis, transpose):
    table = TABLE.T if transpose else TABLE
    shape = [1] * (x.ndim + 1)
    shape[axis] = 5
    shape[axis + 1] = 5
    coefs = jnp.asarray(table.reshape(shape))
    return jnp.sum(coefs * jnp.expand_dims(x, axis), axis=axis + 1)


def internal_force(values, lame_first, shear_modulus):
    shape = values.shape
    merged = shape[:4] + (shape[4] * shape[5], shape[6])
    values = values.reshape(merged)
    lame_first = lame_first.reshape(merged[4:])
    shear_modulus = shear_modulus.reshape(merged[4:])
    weights_3d = weights_cube().reshape(5, 5, 5, 1, 1)
    gradients = [[along(values[i], j, False) for i in range(3)] for j in range(3)]
    divergence = gradients[0][0] + gradients[1][1] + gradients[2][2]
    forces = []
    for i in range(3):
        pulled = None
        for j in range(3):
            stress = shear_modulus * (gradients[j][i] + gradients[i][j])
            if i == j:
                stress = stress + lame_first * divergence
            term = along(weights_3d * stress, j, True)
            pulled = term if pulled is None else pulled + term
        forces.append(-pulled)
    return jnp.stack(forces).reshape(shape)


def shift_block(block, axis, forward):
    count = lax.axis_size(axis)
    pairs = [(i, i + 1) for i in range(count - 1)]
    if not forward:
        pairs = [(target, source) for source, target in pairs]
    return lax.ppermute(block, axis, pairs)


def shift_faces(low_face, high_face, dim, axis):
    count = lax.axis_size(axis)
    forward = [(i, i + 1) for i in range(count - 1)]
    backward = [(target, source) for source, target in forward]
    size = low_face.shape[dim]
    from_prev = lax.ppermute(lax.slice_in_dim(high_face, size - 1, size, axis=dim), axis, forward)
    from_next = lax.ppermute(lax.slice_in_dim(low_face, 0, 1, axis=dim), axis, backward)
    before = jnp.concatenate([from_prev, lax.slice_in_dim(high_face, 0, size - 1, axis=dim)], axis=dim)
    after = jnp.concatenate([lax.slice_in_dim(low_face, 1, size, axis=dim), from_next], axis=dim)
    return before, after


def assemble_dim(values, node_dim, elem_dim, axis):
    low_face = lax.index_in_dim(values, 0, node_dim, keepdims=False)
    high_face = lax.index_in_dim(values, 4, node_dim, keepdims=False)
    face_elem_dim = elem_dim - 1
    if axis is None:
        size = low_face.shape[face_elem_dim]
        zero = jnp.zeros_like(lax.slice_in_dim(low_face, 0, 1, axis=face_elem_dim))
        before = jnp.concatenate(
            [zero, lax.slice_in_dim(high_face, 0, size - 1, axis=face_elem_dim)], axis=face_elem_dim
        )
        after = jnp.concatenate(
            [lax.slice_in_dim(low_face, 1, size, axis=face_elem_dim), zero], axis=face_elem_dim
        )
    else:
        before, after = shift_faces(low_face, high_face, face_elem_dim, axis)
    new_low = jnp.expand_dims(low_face + before, node_dim)
    new_high = jnp.expand_dims(high_face + after, node_dim)
    middle = lax.slice_in_dim(values, 1, 4, axis=node_dim)
    return jnp.concatenate([new_low, middle, new_high], axis=node_dim)


def assemble(values):
    values = assemble_dim(values, 1, 5, "gx")
    values = assemble_dim(values, 2, 6, "gy")
    values = assemble_dim(values, 3, 4, None)
    return values


def per_device(
    flow_state,
    drag_coefficient,
    wet_mask,
    target_elem,
    target_node,
    displacement,
    previous,
    density,
    lame_first,
    shear_modulus,
):
    buoyancy = 1.0 - 0.6 * wet_mask.astype(jnp.float32)
    fields = flow_state
    depth = FLOW_STEPS
    cell_rows = fields.shape[1]
    cell_cols = fields.shape[2]
    bundle = jnp.concatenate([fields, buoyancy[None], drag_coefficient[None]], axis=0)
    first_force = internal_force(displacement, lame_first, shear_modulus)
    rows_widened = extended(bundle, (("gx", 1),), depth)
    rows_widened, first_force = lax.optimization_barrier((rows_widened, first_force))
    widened = extended(rows_widened, (("gy", 2),), depth)
    row_ids = lax.axis_index("gx") * cell_rows + jnp.arange(cell_rows + 2 * depth) - depth
    col_ids = lax.axis_index("gy") * cell_cols + jnp.arange(cell_cols + 2 * depth) - depth
    row_inside = (row_ids >= 0) & (row_ids < cell_rows * lax.axis_size("gx"))
    col_inside = (col_ids >= 0) & (col_ids < cell_cols * lax.axis_size("gy"))
    inside = (row_inside[:, None] & col_inside[None, :]).astype(jnp.float32)
    wide_fields = widened[:6]
    wide_buoyancy = widened[6]
    wide_drag = widened[7]
    for counter in range(FLOW_STEPS):
        stacked = pressures(wide_fields, wide_buoyancy)
        padded = jnp.pad(stacked, ((0, 0), (1, 1), (1, 1)))
        wide_fields = advance(stacked, padded, wide_drag) * inside[None]
    fields = wide_fields[:, depth : depth + cell_rows, depth : depth + cell_cols]
    traction = basal_traction(fields, buoyancy, drag_coefficient)
    mass_parts = density[None, None, None, None] * weights_cube()[None]
    joined = assemble_dim(jnp.concatenate([first_force, mass_parts], axis=0), 1, 5, "gx")
    traction, joined = lax.optimization_barrier((traction, joined))
    joined = assemble_dim(assemble_dim(joined, 2, 6, "gy"), 3, 4, None)
    block_rows = displacement.shape[5]
    block_cols = displacement.shape[6]
    devices_y = lax.axis_size("gy")
    surface_cols = block_cols * devices_y
    elem_row = target_elem // surface_cols
    elem_col = target_elem % surface_cols
    local_x = elem_row - block_rows * lax.axis_index("gx") + 1
    local_y = elem_col - block_cols * lax.axis_index("gy") + 1
    point_rows = 4 * (block_rows + 2) + 1
    point_cols = 4 * (block_cols + 2) + 1
    span_x = 4 * block_rows
    span_y = 4 * block_cols
    point_row = 4 * local_x + target_node // 5
    point_col = 4 * local_y + target_node % 5
    slots = -(-point_cols // 16) * 16
    grid = load_table(traction, point_row, point_col, slots)
    grid, joined = lax.optimization_barrier((grid, joined))
    grid = grid.reshape(slots, 3, 2, ROW_PAD)
    grid = grid[:, :, 0] + grid[:, :, 1]
    overlap_x = point_rows - span_x
    overlap_y = point_cols - span_y
    from_next = shift_block(grid[:, :, :overlap_x], "gx", False)
    from_prev = shift_block(grid[:, :, span_x:point_rows], "gx", True)
    grid = (
        grid
        + jnp.pad(from_next, ((0, 0), (0, 0), (span_x, ROW_PAD - point_rows)))
        + jnp.pad(from_prev, ((0, 0), (0, 0), (0, ROW_PAD - overlap_x)))
    )
    from_next = shift_block(grid[:overlap_y], "gy", False)
    from_prev = shift_block(grid[span_y:point_cols], "gy", True)
    grid = (
        grid
        + jnp.pad(from_next, ((span_y, slots - point_cols), (0, 0), (0, 0)))
        + jnp.pad(from_prev, ((0, slots - overlap_y), (0, 0), (0, 0)))
    )
    by_col = jnp.concatenate(
        [
            grid[4 : 4 + span_y].reshape(block_cols, 4, 3, ROW_PAD),
            grid[8 : 8 + span_y].reshape(block_cols, 4, 3, ROW_PAD)[:, 0:1],
        ],
        axis=1,
    )
    by_row = jnp.concatenate(
        [
            by_col[..., 4 : 4 + span_x].reshape(block_cols, 5, 3, block_rows, 4),
            by_col[..., 8 : 8 + span_x].reshape(block_cols, 5, 3, block_rows, 4)[..., 0:1],
        ],
        axis=-1,
    )
    surface_load = jnp.transpose(by_row, (2, 4, 1, 3, 0))
    surface_load = surface_load.reshape(3, 5, 5, 1, 1, block_rows, block_cols)
    layers = displacement.shape[4]
    load_padded = jnp.pad(
        surface_load,
        ((0, 0), (0, 0), (0, 0), (0, 4), (0, layers - 1), (0, 0), (0, 0)),
    )
    masses = joined[3:]
    current = displacement
    for counter in range(SOLID_STEPS):
        if counter == 0:
            force = joined[:3]
        else:
            force = assemble(internal_force(current, lame_first, shear_modulus))
        acceleration = (force + load_padded) / masses
        advanced = 2.0 * current - previous + solid_dt * solid_dt * acceleration
        previous = current
        current = advanced
    return (fields, current, previous)


def solution(mesh):
    return jax.shard_map(
        per_device,
        mesh=mesh,
        in_specs=(
            P(None, "gx", "gy"),
            P("gx", "gy"),
            P("gx", "gy"),
            P("gx", "gy"),
            P("gx", "gy"),
            P(None, None, None, None, None, "gx", "gy"),
            P(None, None, None, None, None, "gx", "gy"),
            P(None, "gx", "gy"),
            P(None, "gx", "gy"),
            P(None, "gx", "gy"),
        ),
        out_specs=(
            P(None, "gx", "gy"),
            P(None, None, None, None, None, "gx", "gy"),
            P(None, None, None, None, None, "gx", "gy"),
        ),
        check_vma=False,
    )
```

```python
import jax
import jax.numpy as jnp
import numpy as np
from jax import lax
from jax.experimental import pallas as pl
from jax.experimental.pallas import tpu as pltpu
from jax.sharding import PartitionSpec as P

FLOW_STEPS = 4
SOLID_STEPS = 2


gll_points = np.array([-1.0, -np.sqrt(3.0 / 7.0), 0.0, np.sqrt(3.0 / 7.0), 1.0])
gll_weights = np.array([0.1, 49.0 / 90.0, 32.0 / 45.0, 49.0 / 90.0, 0.1])
flow_dt = 0.4
diffusion = 0.2
coupling = 0.5
upper_gravity = 0.8
density_ratio = 0.7
speed_floor = 0.0001
load_factor = 4.0
solid_dt = 0.04

ROW_PAD = 24
CHUNK = 2048
ROW_BLOCK = 8


def extended(block, sides, width):
    for axis, dim in sides:
        count = lax.axis_size(axis)
        forward = [(i, i + 1) for i in range(count - 1)]
        backward = [(target, source) for source, target in forward]
        low = lax.ppermute(
            lax.slice_in_dim(block, block.shape[dim] - width, None, axis=dim), axis, forward
        )
        high = lax.ppermute(lax.slice_in_dim(block, 0, width, axis=dim), axis, backward)
        block = jnp.concatenate([low, block, high], axis=dim)
    return block


def legendre_four(x):
    return (35.0 * x**4 - 30.0 * x**2 + 3.0) / 8.0


def derivative_table():
    result = np.zeros((5, 5))
    for i in range(5):
        for j in range(5):
            if i != j:
                result[i, j] = (
                    legendre_four(gll_points[i])
                    / legendre_four(gll_points[j])
                    / (gll_points[i] - gll_points[j])
                )
    result[0, 0] = -5.0
    result[4, 4] = 5.0
    return result


TABLE = derivative_table().astype(np.float32)


def pressures(fields, buoyancy):
    press_one = buoyancy * (fields[0] + fields[1])
    press_two = upper_gravity * (density_ratio * fields[0] + fields[1])
    return jnp.concatenate([fields, press_one[None], press_two[None]], axis=0)


def advance(center, padded, drag_coefficient):
    ahead_x = padded[:, 2:, 1:-1]
    behind_x = padded[:, :-2, 1:-1]
    ahead_y = padded[:, 1:-1, 2:]
    behind_y = padded[:, 1:-1, :-2]
    slope_x = 0.5 * (ahead_x - behind_x)
    slope_y = 0.5 * (ahead_y - behind_y)
    spread = ahead_x + behind_x + ahead_y + behind_y - 4.0 * center
    flow_speed = jnp.sqrt(center[2] * center[2] + center[3] * center[3] + speed_floor)
    dense_depth = center[0] - flow_dt * (slope_x[2] + slope_y[3]) + diffusion * spread[0]
    light_depth = center[1] - flow_dt * (slope_x[4] + slope_y[5]) + diffusion * spread[1]
    dense_xmom = (
        center[2]
        - flow_dt
        * (
            slope_x[6]
            + drag_coefficient * flow_speed * center[2]
            + coupling * (center[2] - center[4])
        )
        + diffusion * spread[2]
    )
    dense_ymom = (
        center[3]
        - flow_dt
        * (
            slope_y[6]
            + drag_coefficient * flow_speed * center[3]
            + coupling * (center[3] - center[5])
        )
        + diffusion * spread[3]
    )
    light_xmom = (
        center[4]
        - flow_dt * (slope_x[7] + coupling * (center[4] - center[2]))
        + diffusion * spread[4]
    )
    light_ymom = (
        center[5]
        - flow_dt * (slope_y[7] + coupling * (center[5] - center[3]))
        + diffusion * spread[5]
    )
    return jnp.stack([dense_depth, light_depth, dense_xmom, dense_ymom, light_xmom, light_ymom])


def basal_traction(fields, buoyancy, drag_coefficient):
    flow_speed = jnp.sqrt(fields[2] * fields[2] + fields[3] * fields[3] + speed_floor)
    press_one = buoyancy * (fields[0] + fields[1])
    rubbing = load_factor * drag_coefficient * flow_speed
    return jnp.stack([rubbing * fields[2], rubbing * fields[3], -load_factor * press_one])


def weights_cube():
    cube = (
        gll_weights.reshape(5, 1, 1) * gll_weights.reshape(1, 5, 1) * gll_weights.reshape(1, 1, 5)
    )
    return jnp.asarray(cube.reshape(5, 5, 5, 1, 1, 1), jnp.float32)


def load_kernel(trac_ref, row_ref, col_ref, out_ref):
    slots = out_ref.shape[0]

    @pl.when(pl.program_id(0) == 0)
    def _():
        out_ref[...] = jnp.zeros(out_ref.shape, out_ref.dtype)

    def row_body(r, carry):
        for c0 in range(0, row_ref.shape[1], CHUNK):
            point_row = row_ref[pl.ds(r, 1), pl.ds(c0, CHUNK)]
            point_col = col_ref[pl.ds(r, 1), pl.ds(c0, CHUNK)]
            hit = lax.broadcasted_iota(jnp.int32, (ROW_PAD, CHUNK), 0) == point_row
            pieces = []
            for k in range(3):
                value = trac_ref[k, pl.ds(r, 1), pl.ds(c0, CHUNK)]
                high = value.astype(jnp.bfloat16).astype(jnp.float32)
                low = value - high
                pieces.append(jnp.where(hit, high, 0.0))
                pieces.append(jnp.where(hit, low, 0.0))
            weighted = jnp.concatenate(pieces, axis=0).astype(jnp.bfloat16)
            onehot = (
                lax.broadcasted_iota(jnp.int32, (slots, CHUNK), 0) == point_col
            ).astype(jnp.bfloat16)
            out_ref[...] += lax.dot_general(
                onehot,
                weighted,
                (((1,), (1,)), ((), ())),
                preferred_element_type=jnp.float32,
            )
        return carry

    lax.fori_loop(0, ROW_BLOCK, row_body, 0, unroll=2)


def load_table(trac, point_row, point_col, slots):
    rows, cols = point_row.shape
    return pl.pallas_call(
        load_kernel,
        grid=(rows // ROW_BLOCK,),
        in_specs=[
            pl.BlockSpec((3, ROW_BLOCK, cols), lambda g: (0, g, 0)),
            pl.BlockSpec((ROW_BLOCK, cols), lambda g: (g, 0)),
            pl.BlockSpec((ROW_BLOCK, cols), lambda g: (g, 0)),
        ],
        out_specs=pl.BlockSpec((slots, 6 * ROW_PAD), lambda g: (0, 0)),
        out_shape=jax.ShapeDtypeStruct((slots, 6 * ROW_PAD), jnp.float32),
        compiler_params=pltpu.CompilerParams(dimension_semantics=("arbitrary",)),
    )(trac, point_row, point_col)


def along(x, axis, transpose):
    table = TABLE.T if transpose else TABLE
    shape = [1] * (x.ndim + 1)
    shape[axis] = 5
    shape[axis + 1] = 5
    coefs = jnp.asarray(table.reshape(shape))
    return jnp.sum(coefs * jnp.expand_dims(x, axis), axis=axis + 1)


def internal_force(values, lame_first, shear_modulus):
    shape = values.shape
    merged = shape[:4] + (shape[4] * shape[5], shape[6])
    values = values.reshape(merged)
    lame_first = lame_first.reshape(merged[4:])
    shear_modulus = shear_modulus.reshape(merged[4:])
    weights_3d = weights_cube().reshape(5, 5, 5, 1, 1)
    gradients = [[along(values[i], j, False) for i in range(3)] for j in range(3)]
    divergence = gradients[0][0] + gradients[1][1] + gradients[2][2]
    forces = []
    for i in range(3):
        pulled = None
        for j in range(3):
            stress = shear_modulus * (gradients[j][i] + gradients[i][j])
            if i == j:
                stress = stress + lame_first * divergence
            term = along(weights_3d * stress, j, True)
            pulled = term if pulled is None else pulled + term
        forces.append(-pulled)
    return jnp.stack(forces).reshape(shape)


def shift_block(block, axis, forward):
    count = lax.axis_size(axis)
    pairs = [(i, i + 1) for i in range(count - 1)]
    if not forward:
        pairs = [(target, source) for source, target in pairs]
    return lax.ppermute(block, axis, pairs)


def shift_faces(low_face, high_face, dim, axis):
    count = lax.axis_size(axis)
    forward = [(i, i + 1) for i in range(count - 1)]
    backward = [(target, source) for source, target in forward]
    size = low_face.shape[dim]
    from_prev = lax.ppermute(lax.slice_in_dim(high_face, size - 1, size, axis=dim), axis, forward)
    from_next = lax.ppermute(lax.slice_in_dim(low_face, 0, 1, axis=dim), axis, backward)
    before = jnp.concatenate([from_prev, lax.slice_in_dim(high_face, 0, size - 1, axis=dim)], axis=dim)
    after = jnp.concatenate([lax.slice_in_dim(low_face, 1, size, axis=dim), from_next], axis=dim)
    return before, after


def assemble_dim(values, node_dim, elem_dim, axis):
    low_face = lax.index_in_dim(values, 0, node_dim, keepdims=False)
    high_face = lax.index_in_dim(values, 4, node_dim, keepdims=False)
    face_elem_dim = elem_dim - 1
    if axis is None:
        size = low_face.shape[face_elem_dim]
        zero = jnp.zeros_like(lax.slice_in_dim(low_face, 0, 1, axis=face_elem_dim))
        before = jnp.concatenate(
            [zero, lax.slice_in_dim(high_face, 0, size - 1, axis=face_elem_dim)], axis=face_elem_dim
        )
        after = jnp.concatenate(
            [lax.slice_in_dim(low_face, 1, size, axis=face_elem_dim), zero], axis=face_elem_dim
        )
    else:
        before, after = shift_faces(low_face, high_face, face_elem_dim, axis)
    new_low = jnp.expand_dims(low_face + before, node_dim)
    new_high = jnp.expand_dims(high_face + after, node_dim)
    middle = lax.slice_in_dim(values, 1, 4, axis=node_dim)
    return jnp.concatenate([new_low, middle, new_high], axis=node_dim)


def assemble(values):
    values = assemble_dim(values, 1, 5, "gx")
    values = assemble_dim(values, 2, 6, "gy")
    values = assemble_dim(values, 3, 4, None)
    return values


def per_device(
    flow_state,
    drag_coefficient,
    wet_mask,
    target_elem,
    target_node,
    displacement,
    previous,
    density,
    lame_first,
    shear_modulus,
):
    buoyancy = 1.0 - 0.6 * wet_mask.astype(jnp.float32)
    fields = flow_state
    depth = FLOW_STEPS
    cell_rows = fields.shape[1]
    cell_cols = fields.shape[2]
    bundle = jnp.concatenate([fields, buoyancy[None], drag_coefficient[None]], axis=0)
    first_force = internal_force(displacement, lame_first, shear_modulus)
    rows_widened = extended(bundle, (("gx", 1),), depth)
    rows_widened, first_force = lax.optimization_barrier((rows_widened, first_force))
    widened = extended(rows_widened, (("gy", 2),), depth)
    row_ids = lax.axis_index("gx") * cell_rows + jnp.arange(cell_rows + 2 * depth) - depth
    col_ids = lax.axis_index("gy") * cell_cols + jnp.arange(cell_cols + 2 * depth) - depth
    row_inside = (row_ids >= 0) & (row_ids < cell_rows * lax.axis_size("gx"))
    col_inside = (col_ids >= 0) & (col_ids < cell_cols * lax.axis_size("gy"))
    inside = (row_inside[:, None] & col_inside[None, :]).astype(jnp.float32)
    wide_fields = widened[:6]
    wide_buoyancy = widened[6]
    wide_drag = widened[7]
    for counter in range(FLOW_STEPS):
        stacked = pressures(wide_fields, wide_buoyancy)
        padded = jnp.pad(stacked, ((0, 0), (1, 1), (1, 1)))
        wide_fields = advance(stacked, padded, wide_drag) * inside[None]
    fields = wide_fields[:, depth : depth + cell_rows, depth : depth + cell_cols]
    traction = basal_traction(fields, buoyancy, drag_coefficient)
    mass_parts = density[None, None, None, None] * weights_cube()[None]
    joined = assemble_dim(jnp.concatenate([first_force, mass_parts], axis=0), 1, 5, "gx")
    traction, joined = lax.optimization_barrier((traction, joined))
    joined = assemble_dim(assemble_dim(joined, 2, 6, "gy"), 3, 4, None)
    block_rows = displacement.shape[5]
    block_cols = displacement.shape[6]
    devices_y = lax.axis_size("gy")
    surface_cols = block_cols * devices_y
    elem_row = target_elem // surface_cols
    elem_col = target_elem % surface_cols
    local_x = elem_row - block_rows * lax.axis_index("gx") + 1
    local_y = elem_col - block_cols * lax.axis_index("gy") + 1
    point_rows = 4 * (block_rows + 2) + 1
    point_cols = 4 * (block_cols + 2) + 1
    span_x = 4 * block_rows
    span_y = 4 * block_cols
    point_row = 4 * local_x + target_node // 5
    point_col = 4 * local_y + target_node % 5
    slots = -(-point_cols // 16) * 16
    grid = load_table(traction, point_row, point_col, slots)
    grid, joined = lax.optimization_barrier((grid, joined))
    grid = grid.reshape(slots, 3, 2, ROW_PAD)
    grid = grid[:, :, 0] + grid[:, :, 1]
    overlap_x = point_rows - span_x
    overlap_y = point_cols - span_y
    from_next = shift_block(grid[:, :, :overlap_x], "gx", False)
    from_prev = shift_block(grid[:, :, span_x:point_rows], "gx", True)
    grid = (
        grid
        + jnp.pad(from_next, ((0, 0), (0, 0), (span_x, ROW_PAD - point_rows)))
        + jnp.pad(from_prev, ((0, 0), (0, 0), (0, ROW_PAD - overlap_x)))
    )
    from_next = shift_block(grid[:overlap_y], "gy", False)
    from_prev = shift_block(grid[span_y:point_cols], "gy", True)
    grid = (
        grid
        + jnp.pad(from_next, ((span_y, slots - point_cols), (0, 0), (0, 0)))
        + jnp.pad(from_prev, ((0, slots - overlap_y), (0, 0), (0, 0)))
    )
    by_col = jnp.concatenate(
        [
            grid[4 : 4 + span_y].reshape(block_cols, 4, 3, ROW_PAD),
            grid[8 : 8 + span_y].reshape(block_cols, 4, 3, ROW_PAD)[:, 0:1],
        ],
        axis=1,
    )
    by_row = jnp.concatenate(
        [
            by_col[..., 4 : 4 + span_x].reshape(block_cols, 5, 3, block_rows, 4),
            by_col[..., 8 : 8 + span_x].reshape(block_cols, 5, 3, block_rows, 4)[..., 0:1],
        ],
        axis=-1,
    )
    surface_load = jnp.transpose(by_row, (2, 4, 1, 3, 0))
    surface_load = surface_load.reshape(3, 5, 5, 1, 1, block_rows, block_cols)
    layers = displacement.shape[4]
    load_padded = jnp.pad(
        surface_load,
        ((0, 0), (0, 0), (0, 0), (0, 4), (0, layers - 1), (0, 0), (0, 0)),
    )
    masses = joined[3:]
    current = displacement
    for counter in range(SOLID_STEPS):
        if counter == 0:
            force = joined[:3]
        else:
            force = assemble(internal_force(current, lame_first, shear_modulus))
        acceleration = (force + load_padded) / masses
        advanced = 2.0 * current - previous + solid_dt * solid_dt * acceleration
        previous = current
        current = advanced
    return (fields, current, previous)


def solution(mesh):
    return jax.shard_map(
        per_device,
        mesh=mesh,
        in_specs=(
            P(None, "gx", "gy"),
            P("gx", "gy"),
            P("gx", "gy"),
            P("gx", "gy"),
            P("gx", "gy"),
            P(None, None, None, None, None, "gx", "gy"),
            P(None, None, None, None, None, "gx", "gy"),
            P(None, "gx", "gy"),
            P(None, "gx", "gy"),
            P(None, "gx", "gy"),
        ),
        out_specs=(
            P(None, "gx", "gy"),
            P(None, None, None, None, None, "gx", "gy"),
            P(None, None, None, None, None, "gx", "gy"),
        ),
        check_vma=False,
    )
```

```python
import jax
import jax.numpy as jnp
import numpy as np
from jax import lax
from jax.experimental import pallas as pl
from jax.experimental.pallas import tpu as pltpu
from jax.sharding import PartitionSpec as P

FLOW_STEPS = 4
SOLID_STEPS = 2


gll_points = np.array([-1.0, -np.sqrt(3.0 / 7.0), 0.0, np.sqrt(3.0 / 7.0), 1.0])
gll_weights = np.array([0.1, 49.0 / 90.0, 32.0 / 45.0, 49.0 / 90.0, 0.1])
flow_dt = 0.4
diffusion = 0.2
coupling = 0.5
upper_gravity = 0.8
density_ratio = 0.7
speed_floor = 0.0001
load_factor = 4.0
solid_dt = 0.04

ROW_PAD = 24
CHUNK = 2048
ROW_BLOCK = 8


def extended(block, sides, width):
    for axis, dim in sides:
        count = lax.axis_size(axis)
        forward = [(i, i + 1) for i in range(count - 1)]
        backward = [(target, source) for source, target in forward]
        low = lax.ppermute(
            lax.slice_in_dim(block, block.shape[dim] - width, None, axis=dim), axis, forward
        )
        high = lax.ppermute(lax.slice_in_dim(block, 0, width, axis=dim), axis, backward)
        block = jnp.concatenate([low, block, high], axis=dim)
    return block


def legendre_four(x):
    return (35.0 * x**4 - 30.0 * x**2 + 3.0) / 8.0


def derivative_table():
    result = np.zeros((5, 5))
    for i in range(5):
        for j in range(5):
            if i != j:
                result[i, j] = (
                    legendre_four(gll_points[i])
                    / legendre_four(gll_points[j])
                    / (gll_points[i] - gll_points[j])
                )
    result[0, 0] = -5.0
    result[4, 4] = 5.0
    return result


TABLE = derivative_table().astype(np.float32)


def pressures(fields, buoyancy):
    press_one = buoyancy * (fields[0] + fields[1])
    press_two = upper_gravity * (density_ratio * fields[0] + fields[1])
    return jnp.concatenate([fields, press_one[None], press_two[None]], axis=0)


def advance(center, padded, drag_coefficient):
    ahead_x = padded[:, 2:, 1:-1]
    behind_x = padded[:, :-2, 1:-1]
    ahead_y = padded[:, 1:-1, 2:]
    behind_y = padded[:, 1:-1, :-2]
    slope_x = 0.5 * (ahead_x - behind_x)
    slope_y = 0.5 * (ahead_y - behind_y)
    spread = ahead_x + behind_x + ahead_y + behind_y - 4.0 * center
    flow_speed = jnp.sqrt(center[2] * center[2] + center[3] * center[3] + speed_floor)
    dense_depth = center[0] - flow_dt * (slope_x[2] + slope_y[3]) + diffusion * spread[0]
    light_depth = center[1] - flow_dt * (slope_x[4] + slope_y[5]) + diffusion * spread[1]
    dense_xmom = (
        center[2]
        - flow_dt
        * (
            slope_x[6]
            + drag_coefficient * flow_speed * center[2]
            + coupling * (center[2] - center[4])
        )
        + diffusion * spread[2]
    )
    dense_ymom = (
        center[3]
        - flow_dt
        * (
            slope_y[6]
            + drag_coefficient * flow_speed * center[3]
            + coupling * (center[3] - center[5])
        )
        + diffusion * spread[3]
    )
    light_xmom = (
        center[4]
        - flow_dt * (slope_x[7] + coupling * (center[4] - center[2]))
        + diffusion * spread[4]
    )
    light_ymom = (
        center[5]
        - flow_dt * (slope_y[7] + coupling * (center[5] - center[3]))
        + diffusion * spread[5]
    )
    return jnp.stack([dense_depth, light_depth, dense_xmom, dense_ymom, light_xmom, light_ymom])


def basal_traction(fields, buoyancy, drag_coefficient):
    flow_speed = jnp.sqrt(fields[2] * fields[2] + fields[3] * fields[3] + speed_floor)
    press_one = buoyancy * (fields[0] + fields[1])
    rubbing = load_factor * drag_coefficient * flow_speed
    return jnp.stack([rubbing * fields[2], rubbing * fields[3], -load_factor * press_one])


def weights_cube():
    cube = (
        gll_weights.reshape(5, 1, 1) * gll_weights.reshape(1, 5, 1) * gll_weights.reshape(1, 1, 5)
    )
    return jnp.asarray(cube.reshape(5, 5, 5, 1, 1, 1), jnp.float32)


def load_kernel(trac_ref, row_ref, col_ref, out_ref):
    slots = out_ref.shape[0]

    @pl.when(pl.program_id(0) == 0)
    def _():
        out_ref[...] = jnp.zeros(out_ref.shape, out_ref.dtype)

    def row_body(r, carry):
        for c0 in range(0, row_ref.shape[1], CHUNK):
            point_row = row_ref[pl.ds(r, 1), pl.ds(c0, CHUNK)]
            point_col = col_ref[pl.ds(r, 1), pl.ds(c0, CHUNK)]
            hit = lax.broadcasted_iota(jnp.int32, (ROW_PAD, CHUNK), 0) == point_row
            pieces = []
            for k in range(3):
                value = trac_ref[k, pl.ds(r, 1), pl.ds(c0, CHUNK)]
                high = value.astype(jnp.bfloat16).astype(jnp.float32)
                low = value - high
                pieces.append(jnp.where(hit, high, 0.0))
                pieces.append(jnp.where(hit, low, 0.0))
            weighted = jnp.concatenate(pieces, axis=0).astype(jnp.bfloat16)
            onehot = (
                lax.broadcasted_iota(jnp.int32, (slots, CHUNK), 0) == point_col
            ).astype(jnp.bfloat16)
            out_ref[...] += lax.dot_general(
                onehot,
                weighted,
                (((1,), (1,)), ((), ())),
                preferred_element_type=jnp.float32,
            )
        return carry

    lax.fori_loop(0, ROW_BLOCK, row_body, 0, unroll=4)


def load_table(trac, point_row, point_col, slots):
    rows, cols = point_row.shape
    return pl.pallas_call(
        load_kernel,
        grid=(rows // ROW_BLOCK,),
        in_specs=[
            pl.BlockSpec((3, ROW_BLOCK, cols), lambda g: (0, g, 0)),
            pl.BlockSpec((ROW_BLOCK, cols), lambda g: (g, 0)),
            pl.BlockSpec((ROW_BLOCK, cols), lambda g: (g, 0)),
        ],
        out_specs=pl.BlockSpec((slots, 6 * ROW_PAD), lambda g: (0, 0)),
        out_shape=jax.ShapeDtypeStruct((slots, 6 * ROW_PAD), jnp.float32),
        compiler_params=pltpu.CompilerParams(dimension_semantics=("arbitrary",)),
    )(trac, point_row, point_col)


def along(x, axis, transpose):
    table = TABLE.T if transpose else TABLE
    shape = [1] * (x.ndim + 1)
    shape[axis] = 5
    shape[axis + 1] = 5
    coefs = jnp.asarray(table.reshape(shape))
    return jnp.sum(coefs * jnp.expand_dims(x, axis), axis=axis + 1)


def internal_force(values, lame_first, shear_modulus):
    shape = values.shape
    merged = shape[:4] + (shape[4] * shape[5], shape[6])
    values = values.reshape(merged)
    lame_first = lame_first.reshape(merged[4:])
    shear_modulus = shear_modulus.reshape(merged[4:])
    weights_3d = weights_cube().reshape(5, 5, 5, 1, 1)
    gradients = [[along(values[i], j, False) for i in range(3)] for j in range(3)]
    divergence = gradients[0][0] + gradients[1][1] + gradients[2][2]
    forces = []
    for i in range(3):
        pulled = None
        for j in range(3):
            stress = shear_modulus * (gradients[j][i] + gradients[i][j])
            if i == j:
                stress = stress + lame_first * divergence
            term = along(weights_3d * stress, j, True)
            pulled = term if pulled is None else pulled + term
        forces.append(-pulled)
    return jnp.stack(forces).reshape(shape)


def shift_block(block, axis, forward):
    count = lax.axis_size(axis)
    pairs = [(i, i + 1) for i in range(count - 1)]
    if not forward:
        pairs = [(target, source) for source, target in pairs]
    return lax.ppermute(block, axis, pairs)


def shift_faces(low_face, high_face, dim, axis):
    count = lax.axis_size(axis)
    forward = [(i, i + 1) for i in range(count - 1)]
    backward = [(target, source) for source, target in forward]
    size = low_face.shape[dim]
    from_prev = lax.ppermute(lax.slice_in_dim(high_face, size - 1, size, axis=dim), axis, forward)
    from_next = lax.ppermute(lax.slice_in_dim(low_face, 0, 1, axis=dim), axis, backward)
    before = jnp.concatenate([from_prev, lax.slice_in_dim(high_face, 0, size - 1, axis=dim)], axis=dim)
    after = jnp.concatenate([lax.slice_in_dim(low_face, 1, size, axis=dim), from_next], axis=dim)
    return before, after


def assemble_dim(values, node_dim, elem_dim, axis):
    low_face = lax.index_in_dim(values, 0, node_dim, keepdims=False)
    high_face = lax.index_in_dim(values, 4, node_dim, keepdims=False)
    face_elem_dim = elem_dim - 1
    if axis is None:
        size = low_face.shape[face_elem_dim]
        zero = jnp.zeros_like(lax.slice_in_dim(low_face, 0, 1, axis=face_elem_dim))
        before = jnp.concatenate(
            [zero, lax.slice_in_dim(high_face, 0, size - 1, axis=face_elem_dim)], axis=face_elem_dim
        )
        after = jnp.concatenate(
            [lax.slice_in_dim(low_face, 1, size, axis=face_elem_dim), zero], axis=face_elem_dim
        )
    else:
        before, after = shift_faces(low_face, high_face, face_elem_dim, axis)
    new_low = jnp.expand_dims(low_face + before, node_dim)
    new_high = jnp.expand_dims(high_face + after, node_dim)
    middle = lax.slice_in_dim(values, 1, 4, axis=node_dim)
    return jnp.concatenate([new_low, middle, new_high], axis=node_dim)


def assemble(values):
    values = assemble_dim(values, 1, 5, "gx")
    values = assemble_dim(values, 2, 6, "gy")
    values = assemble_dim(values, 3, 4, None)
    return values


def per_device(
    flow_state,
    drag_coefficient,
    wet_mask,
    target_elem,
    target_node,
    displacement,
    previous,
    density,
    lame_first,
    shear_modulus,
):
    buoyancy = 1.0 - 0.6 * wet_mask.astype(jnp.float32)
    fields = flow_state
    depth = FLOW_STEPS
    cell_rows = fields.shape[1]
    cell_cols = fields.shape[2]
    bundle = jnp.concatenate([fields, buoyancy[None], drag_coefficient[None]], axis=0)
    first_force = internal_force(displacement, lame_first, shear_modulus)
    rows_widened = extended(bundle, (("gx", 1),), depth)
    rows_widened, first_force = lax.optimization_barrier((rows_widened, first_force))
    widened = extended(rows_widened, (("gy", 2),), depth)
    row_ids = lax.axis_index("gx") * cell_rows + jnp.arange(cell_rows + 2 * depth) - depth
    col_ids = lax.axis_index("gy") * cell_cols + jnp.arange(cell_cols + 2 * depth) - depth
    row_inside = (row_ids >= 0) & (row_ids < cell_rows * lax.axis_size("gx"))
    col_inside = (col_ids >= 0) & (col_ids < cell_cols * lax.axis_size("gy"))
    inside = (row_inside[:, None] & col_inside[None, :]).astype(jnp.float32)
    wide_fields = widened[:6]
    wide_buoyancy = widened[6]
    wide_drag = widened[7]
    for counter in range(FLOW_STEPS):
        stacked = pressures(wide_fields, wide_buoyancy)
        padded = jnp.pad(stacked, ((0, 0), (1, 1), (1, 1)))
        wide_fields = advance(stacked, padded, wide_drag) * inside[None]
    fields = wide_fields[:, depth : depth + cell_rows, depth : depth + cell_cols]
    traction = basal_traction(fields, buoyancy, drag_coefficient)
    mass_parts = density[None, None, None, None] * weights_cube()[None]
    joined = assemble_dim(jnp.concatenate([first_force, mass_parts], axis=0), 1, 5, "gx")
    traction, joined = lax.optimization_barrier((traction, joined))
    joined = assemble_dim(assemble_dim(joined, 2, 6, "gy"), 3, 4, None)
    block_rows = displacement.shape[5]
    block_cols = displacement.shape[6]
    devices_y = lax.axis_size("gy")
    surface_cols = block_cols * devices_y
    elem_row = target_elem // surface_cols
    elem_col = target_elem % surface_cols
    local_x = elem_row - block_rows * lax.axis_index("gx") + 1
    local_y = elem_col - block_cols * lax.axis_index("gy") + 1
    point_rows = 4 * (block_rows + 2) + 1
    point_cols = 4 * (block_cols + 2) + 1
    span_x = 4 * block_rows
    span_y = 4 * block_cols
    point_row = 4 * local_x + target_node // 5
    point_col = 4 * local_y + target_node % 5
    slots = -(-point_cols // 16) * 16
    grid = load_table(traction, point_row, point_col, slots)
    grid, joined = lax.optimization_barrier((grid, joined))
    grid = grid.reshape(slots, 3, 2, ROW_PAD)
    grid = grid[:, :, 0] + grid[:, :, 1]
    overlap_x = point_rows - span_x
    overlap_y = point_cols - span_y
    from_next = shift_block(grid[:, :, :overlap_x], "gx", False)
    from_prev = shift_block(grid[:, :, span_x:point_rows], "gx", True)
    grid = (
        grid
        + jnp.pad(from_next, ((0, 0), (0, 0), (span_x, ROW_PAD - point_rows)))
        + jnp.pad(from_prev, ((0, 0), (0, 0), (0, ROW_PAD - overlap_x)))
    )
    from_next = shift_block(grid[:overlap_y], "gy", False)
    from_prev = shift_block(grid[span_y:point_cols], "gy", True)
    grid = (
        grid
        + jnp.pad(from_next, ((span_y, slots - point_cols), (0, 0), (0, 0)))
        + jnp.pad(from_prev, ((0, slots - overlap_y), (0, 0), (0, 0)))
    )
    by_col = jnp.concatenate(
        [
            grid[4 : 4 + span_y].reshape(block_cols, 4, 3, ROW_PAD),
            grid[8 : 8 + span_y].reshape(block_cols, 4, 3, ROW_PAD)[:, 0:1],
        ],
        axis=1,
    )
    by_row = jnp.concatenate(
        [
            by_col[..., 4 : 4 + span_x].reshape(block_cols, 5, 3, block_rows, 4),
            by_col[..., 8 : 8 + span_x].reshape(block_cols, 5, 3, block_rows, 4)[..., 0:1],
        ],
        axis=-1,
    )
    surface_load = jnp.transpose(by_row, (2, 4, 1, 3, 0))
    surface_load = surface_load.reshape(3, 5, 5, 1, 1, block_rows, block_cols)
    layers = displacement.shape[4]
    load_padded = jnp.pad(
        surface_load,
        ((0, 0), (0, 0), (0, 0), (0, 4), (0, layers - 1), (0, 0), (0, 0)),
    )
    masses = joined[3:]
    current = displacement
    for counter in range(SOLID_STEPS):
        if counter == 0:
            force = joined[:3]
        else:
            force = assemble(internal_force(current, lame_first, shear_modulus))
        acceleration = (force + load_padded) / masses
        advanced = 2.0 * current - previous + solid_dt * solid_dt * acceleration
        previous = current
        current = advanced
    return (fields, current, previous)


def solution(mesh):
    return jax.shard_map(
        per_device,
        mesh=mesh,
        in_specs=(
            P(None, "gx", "gy"),
            P("gx", "gy"),
            P("gx", "gy"),
            P("gx", "gy"),
            P("gx", "gy"),
            P(None, None, None, None, None, "gx", "gy"),
            P(None, None, None, None, None, "gx", "gy"),
            P(None, "gx", "gy"),
            P(None, "gx", "gy"),
            P(None, "gx", "gy"),
        ),
        out_specs=(
            P(None, "gx", "gy"),
            P(None, None, None, None, None, "gx", "gy"),
            P(None, None, None, None, None, "gx", "gy"),
        ),
        check_vma=False,
    )
```

```python
import jax
import jax.numpy as jnp
import numpy as np
from jax import lax
from jax.experimental import pallas as pl
from jax.experimental.pallas import tpu as pltpu
from jax.sharding import PartitionSpec as P

FLOW_STEPS = 4
SOLID_STEPS = 2


gll_points = np.array([-1.0, -np.sqrt(3.0 / 7.0), 0.0, np.sqrt(3.0 / 7.0), 1.0])
gll_weights = np.array([0.1, 49.0 / 90.0, 32.0 / 45.0, 49.0 / 90.0, 0.1])
flow_dt = 0.4
diffusion = 0.2
coupling = 0.5
upper_gravity = 0.8
density_ratio = 0.7
speed_floor = 0.0001
load_factor = 4.0
solid_dt = 0.04

ROW_PAD = 24
CHUNK = 2048
ROW_BLOCK = 8


def extended(block, sides, width):
    for axis, dim in sides:
        count = lax.axis_size(axis)
        forward = [(i, i + 1) for i in range(count - 1)]
        backward = [(target, source) for source, target in forward]
        low = lax.ppermute(
            lax.slice_in_dim(block, block.shape[dim] - width, None, axis=dim), axis, forward
        )
        high = lax.ppermute(lax.slice_in_dim(block, 0, width, axis=dim), axis, backward)
        block = jnp.concatenate([low, block, high], axis=dim)
    return block


def legendre_four(x):
    return (35.0 * x**4 - 30.0 * x**2 + 3.0) / 8.0


def derivative_table():
    result = np.zeros((5, 5))
    for i in range(5):
        for j in range(5):
            if i != j:
                result[i, j] = (
                    legendre_four(gll_points[i])
                    / legendre_four(gll_points[j])
                    / (gll_points[i] - gll_points[j])
                )
    result[0, 0] = -5.0
    result[4, 4] = 5.0
    return result


TABLE = derivative_table().astype(np.float32)


def pressures(fields, buoyancy):
    press_one = buoyancy * (fields[0] + fields[1])
    press_two = upper_gravity * (density_ratio * fields[0] + fields[1])
    return jnp.concatenate([fields, press_one[None], press_two[None]], axis=0)


def advance(center, padded, drag_coefficient):
    ahead_x = padded[:, 2:, 1:-1]
    behind_x = padded[:, :-2, 1:-1]
    ahead_y = padded[:, 1:-1, 2:]
    behind_y = padded[:, 1:-1, :-2]
    slope_x = 0.5 * (ahead_x - behind_x)
    slope_y = 0.5 * (ahead_y - behind_y)
    spread = ahead_x + behind_x + ahead_y + behind_y - 4.0 * center
    flow_speed = jnp.sqrt(center[2] * center[2] + center[3] * center[3] + speed_floor)
    dense_depth = center[0] - flow_dt * (slope_x[2] + slope_y[3]) + diffusion * spread[0]
    light_depth = center[1] - flow_dt * (slope_x[4] + slope_y[5]) + diffusion * spread[1]
    dense_xmom = (
        center[2]
        - flow_dt
        * (
            slope_x[6]
            + drag_coefficient * flow_speed * center[2]
            + coupling * (center[2] - center[4])
        )
        + diffusion * spread[2]
    )
    dense_ymom = (
        center[3]
        - flow_dt
        * (
            slope_y[6]
            + drag_coefficient * flow_speed * center[3]
            + coupling * (center[3] - center[5])
        )
        + diffusion * spread[3]
    )
    light_xmom = (
        center[4]
        - flow_dt * (slope_x[7] + coupling * (center[4] - center[2]))
        + diffusion * spread[4]
    )
    light_ymom = (
        center[5]
        - flow_dt * (slope_y[7] + coupling * (center[5] - center[3]))
        + diffusion * spread[5]
    )
    return jnp.stack([dense_depth, light_depth, dense_xmom, dense_ymom, light_xmom, light_ymom])


def basal_traction(fields, buoyancy, drag_coefficient):
    flow_speed = jnp.sqrt(fields[2] * fields[2] + fields[3] * fields[3] + speed_floor)
    press_one = buoyancy * (fields[0] + fields[1])
    rubbing = load_factor * drag_coefficient * flow_speed
    return jnp.stack([rubbing * fields[2], rubbing * fields[3], -load_factor * press_one])


def weights_cube():
    cube = (
        gll_weights.reshape(5, 1, 1) * gll_weights.reshape(1, 5, 1) * gll_weights.reshape(1, 1, 5)
    )
    return jnp.asarray(cube.reshape(5, 5, 5, 1, 1, 1), jnp.float32)


def load_kernel(trac_ref, row_ref, col_ref, out_ref):
    slots = out_ref.shape[0]

    @pl.when(pl.program_id(0) == 0)
    def _():
        out_ref[...] = jnp.zeros(out_ref.shape, out_ref.dtype)

    def row_body(r, carry):
        for c0 in range(0, row_ref.shape[1], CHUNK):
            point_row = row_ref[pl.ds(r, 1), pl.ds(c0, CHUNK)]
            point_col = col_ref[pl.ds(r, 1), pl.ds(c0, CHUNK)]
            hit = lax.broadcasted_iota(jnp.int32, (ROW_PAD, CHUNK), 0) == point_row
            pieces = []
            for k in range(3):
                value = trac_ref[k, pl.ds(r, 1), pl.ds(c0, CHUNK)]
                high = value.astype(jnp.bfloat16).astype(jnp.float32)
                low = value - high
                pieces.append(jnp.where(hit, high, 0.0))
                pieces.append(jnp.where(hit, low, 0.0))
            weighted = jnp.concatenate(pieces, axis=0).astype(jnp.bfloat16)
            onehot = (
                lax.broadcasted_iota(jnp.int32, (slots, CHUNK), 0) == point_col
            ).astype(jnp.bfloat16)
            out_ref[...] += lax.dot_general(
                onehot,
                weighted,
                (((1,), (1,)), ((), ())),
                preferred_element_type=jnp.float32,
            )
        return carry

    lax.fori_loop(0, ROW_BLOCK, row_body, 0, unroll=True)


def load_table(trac, point_row, point_col, slots):
    rows, cols = point_row.shape
    return pl.pallas_call(
        load_kernel,
        grid=(rows // ROW_BLOCK,),
        in_specs=[
            pl.BlockSpec((3, ROW_BLOCK, cols), lambda g: (0, g, 0)),
            pl.BlockSpec((ROW_BLOCK, cols), lambda g: (g, 0)),
            pl.BlockSpec((ROW_BLOCK, cols), lambda g: (g, 0)),
        ],
        out_specs=pl.BlockSpec((slots, 6 * ROW_PAD), lambda g: (0, 0)),
        out_shape=jax.ShapeDtypeStruct((slots, 6 * ROW_PAD), jnp.float32),
        compiler_params=pltpu.CompilerParams(dimension_semantics=("arbitrary",)),
    )(trac, point_row, point_col)


def along(x, axis, transpose):
    table = TABLE.T if transpose else TABLE
    shape = [1] * (x.ndim + 1)
    shape[axis] = 5
    shape[axis + 1] = 5
    coefs = jnp.asarray(table.reshape(shape))
    return jnp.sum(coefs * jnp.expand_dims(x, axis), axis=axis + 1)


def internal_force(values, lame_first, shear_modulus):
    shape = values.shape
    merged = shape[:4] + (shape[4] * shape[5], shape[6])
    values = values.reshape(merged)
    lame_first = lame_first.reshape(merged[4:])
    shear_modulus = shear_modulus.reshape(merged[4:])
    weights_3d = weights_cube().reshape(5, 5, 5, 1, 1)
    gradients = [[along(values[i], j, False) for i in range(3)] for j in range(3)]
    divergence = gradients[0][0] + gradients[1][1] + gradients[2][2]
    forces = []
    for i in range(3):
        pulled = None
        for j in range(3):
            stress = shear_modulus * (gradients[j][i] + gradients[i][j])
            if i == j:
                stress = stress + lame_first * divergence
            term = along(weights_3d * stress, j, True)
            pulled = term if pulled is None else pulled + term
        forces.append(-pulled)
    return jnp.stack(forces).reshape(shape)


def shift_block(block, axis, forward):
    count = lax.axis_size(axis)
    pairs = [(i, i + 1) for i in range(count - 1)]
    if not forward:
        pairs = [(target, source) for source, target in pairs]
    return lax.ppermute(block, axis, pairs)


def shift_faces(low_face, high_face, dim, axis):
    count = lax.axis_size(axis)
    forward = [(i, i + 1) for i in range(count - 1)]
    backward = [(target, source) for source, target in forward]
    size = low_face.shape[dim]
    from_prev = lax.ppermute(lax.slice_in_dim(high_face, size - 1, size, axis=dim), axis, forward)
    from_next = lax.ppermute(lax.slice_in_dim(low_face, 0, 1, axis=dim), axis, backward)
    before = jnp.concatenate([from_prev, lax.slice_in_dim(high_face, 0, size - 1, axis=dim)], axis=dim)
    after = jnp.concatenate([lax.slice_in_dim(low_face, 1, size, axis=dim), from_next], axis=dim)
    return before, after


def assemble_dim(values, node_dim, elem_dim, axis):
    low_face = lax.index_in_dim(values, 0, node_dim, keepdims=False)
    high_face = lax.index_in_dim(values, 4, node_dim, keepdims=False)
    face_elem_dim = elem_dim - 1
    if axis is None:
        size = low_face.shape[face_elem_dim]
        zero = jnp.zeros_like(lax.slice_in_dim(low_face, 0, 1, axis=face_elem_dim))
        before = jnp.concatenate(
            [zero, lax.slice_in_dim(high_face, 0, size - 1, axis=face_elem_dim)], axis=face_elem_dim
        )
        after = jnp.concatenate(
            [lax.slice_in_dim(low_face, 1, size, axis=face_elem_dim), zero], axis=face_elem_dim
        )
    else:
        before, after = shift_faces(low_face, high_face, face_elem_dim, axis)
    new_low = jnp.expand_dims(low_face + before, node_dim)
    new_high = jnp.expand_dims(high_face + after, node_dim)
    middle = lax.slice_in_dim(values, 1, 4, axis=node_dim)
    return jnp.concatenate([new_low, middle, new_high], axis=node_dim)


def assemble(values):
    values = assemble_dim(values, 1, 5, "gx")
    values = assemble_dim(values, 2, 6, "gy")
    values = assemble_dim(values, 3, 4, None)
    return values


def per_device(
    flow_state,
    drag_coefficient,
    wet_mask,
    target_elem,
    target_node,
    displacement,
    previous,
    density,
    lame_first,
    shear_modulus,
):
    buoyancy = 1.0 - 0.6 * wet_mask.astype(jnp.float32)
    fields = flow_state
    depth = FLOW_STEPS
    cell_rows = fields.shape[1]
    cell_cols = fields.shape[2]
    bundle = jnp.concatenate([fields, buoyancy[None], drag_coefficient[None]], axis=0)
    first_force = internal_force(displacement, lame_first, shear_modulus)
    rows_widened = extended(bundle, (("gx", 1),), depth)
    rows_widened, first_force = lax.optimization_barrier((rows_widened, first_force))
    widened = extended(rows_widened, (("gy", 2),), depth)
    row_ids = lax.axis_index("gx") * cell_rows + jnp.arange(cell_rows + 2 * depth) - depth
    col_ids = lax.axis_index("gy") * cell_cols + jnp.arange(cell_cols + 2 * depth) - depth
    row_inside = (row_ids >= 0) & (row_ids < cell_rows * lax.axis_size("gx"))
    col_inside = (col_ids >= 0) & (col_ids < cell_cols * lax.axis_size("gy"))
    inside = (row_inside[:, None] & col_inside[None, :]).astype(jnp.float32)
    wide_fields = widened[:6]
    wide_buoyancy = widened[6]
    wide_drag = widened[7]
    for counter in range(FLOW_STEPS):
        stacked = pressures(wide_fields, wide_buoyancy)
        padded = jnp.pad(stacked, ((0, 0), (1, 1), (1, 1)))
        wide_fields = advance(stacked, padded, wide_drag) * inside[None]
    fields = wide_fields[:, depth : depth + cell_rows, depth : depth + cell_cols]
    traction = basal_traction(fields, buoyancy, drag_coefficient)
    mass_parts = density[None, None, None, None] * weights_cube()[None]
    joined = assemble_dim(jnp.concatenate([first_force, mass_parts], axis=0), 1, 5, "gx")
    traction, joined = lax.optimization_barrier((traction, joined))
    joined = assemble_dim(assemble_dim(joined, 2, 6, "gy"), 3, 4, None)
    block_rows = displacement.shape[5]
    block_cols = displacement.shape[6]
    devices_y = lax.axis_size("gy")
    surface_cols = block_cols * devices_y
    elem_row = target_elem // surface_cols
    elem_col = target_elem % surface_cols
    local_x = elem_row - block_rows * lax.axis_index("gx") + 1
    local_y = elem_col - block_cols * lax.axis_index("gy") + 1
    point_rows = 4 * (block_rows + 2) + 1
    point_cols = 4 * (block_cols + 2) + 1
    span_x = 4 * block_rows
    span_y = 4 * block_cols
    point_row = 4 * local_x + target_node // 5
    point_col = 4 * local_y + target_node % 5
    slots = -(-point_cols // 16) * 16
    grid = load_table(traction, point_row, point_col, slots)
    grid, joined = lax.optimization_barrier((grid, joined))
    grid = grid.reshape(slots, 3, 2, ROW_PAD)
    grid = grid[:, :, 0] + grid[:, :, 1]
    overlap_x = point_rows - span_x
    overlap_y = point_cols - span_y
    from_next = shift_block(grid[:, :, :overlap_x], "gx", False)
    from_prev = shift_block(grid[:, :, span_x:point_rows], "gx", True)
    grid = (
        grid
        + jnp.pad(from_next, ((0, 0), (0, 0), (span_x, ROW_PAD - point_rows)))
        + jnp.pad(from_prev, ((0, 0), (0, 0), (0, ROW_PAD - overlap_x)))
    )
    from_next = shift_block(grid[:overlap_y], "gy", False)
    from_prev = shift_block(grid[span_y:point_cols], "gy", True)
    grid = (
        grid
        + jnp.pad(from_next, ((span_y, slots - point_cols), (0, 0), (0, 0)))
        + jnp.pad(from_prev, ((0, slots - overlap_y), (0, 0), (0, 0)))
    )
    by_col = jnp.concatenate(
        [
            grid[4 : 4 + span_y].reshape(block_cols, 4, 3, ROW_PAD),
            grid[8 : 8 + span_y].reshape(block_cols, 4, 3, ROW_PAD)[:, 0:1],
        ],
        axis=1,
    )
    by_row = jnp.concatenate(
        [
            by_col[..., 4 : 4 + span_x].reshape(block_cols, 5, 3, block_rows, 4),
            by_col[..., 8 : 8 + span_x].reshape(block_cols, 5, 3, block_rows, 4)[..., 0:1],
        ],
        axis=-1,
    )
    surface_load = jnp.transpose(by_row, (2, 4, 1, 3, 0))
    surface_load = surface_load.reshape(3, 5, 5, 1, 1, block_rows, block_cols)
    layers = displacement.shape[4]
    load_padded = jnp.pad(
        surface_load,
        ((0, 0), (0, 0), (0, 0), (0, 4), (0, layers - 1), (0, 0), (0, 0)),
    )
    masses = joined[3:]
    current = displacement
    for counter in range(SOLID_STEPS):
        if counter == 0:
            force = joined[:3]
        else:
            force = assemble(internal_force(current, lame_first, shear_modulus))
        acceleration = (force + load_padded) / masses
        advanced = 2.0 * current - previous + solid_dt * solid_dt * acceleration
        previous = current
        current = advanced
    return (fields, current, previous)


def solution(mesh):
    return jax.shard_map(
        per_device,
        mesh=mesh,
        in_specs=(
            P(None, "gx", "gy"),
            P("gx", "gy"),
            P("gx", "gy"),
            P("gx", "gy"),
            P("gx", "gy"),
            P(None, None, None, None, None, "gx", "gy"),
            P(None, None, None, None, None, "gx", "gy"),
            P(None, "gx", "gy"),
            P(None, "gx", "gy"),
            P(None, "gx", "gy"),
        ),
        out_specs=(
            P(None, "gx", "gy"),
            P(None, None, None, None, None, "gx", "gy"),
            P(None, None, None, None, None, "gx", "gy"),
        ),
        check_vma=False,
    )
```

```python
import jax
import jax.numpy as jnp
import numpy as np
from jax import lax
from jax.experimental import pallas as pl
from jax.experimental.pallas import tpu as pltpu
from jax.sharding import PartitionSpec as P

FLOW_STEPS = 4
SOLID_STEPS = 2


gll_points = np.array([-1.0, -np.sqrt(3.0 / 7.0), 0.0, np.sqrt(3.0 / 7.0), 1.0])
gll_weights = np.array([0.1, 49.0 / 90.0, 32.0 / 45.0, 49.0 / 90.0, 0.1])
flow_dt = 0.4
diffusion = 0.2
coupling = 0.5
upper_gravity = 0.8
density_ratio = 0.7
speed_floor = 0.0001
load_factor = 4.0
solid_dt = 0.04

ROW_PAD = 24
CHUNK = 2048
ROW_BLOCK = 16


def extended(block, sides, width):
    for axis, dim in sides:
        count = lax.axis_size(axis)
        forward = [(i, i + 1) for i in range(count - 1)]
        backward = [(target, source) for source, target in forward]
        low = lax.ppermute(
            lax.slice_in_dim(block, block.shape[dim] - width, None, axis=dim), axis, forward
        )
        high = lax.ppermute(lax.slice_in_dim(block, 0, width, axis=dim), axis, backward)
        block = jnp.concatenate([low, block, high], axis=dim)
    return block


def legendre_four(x):
    return (35.0 * x**4 - 30.0 * x**2 + 3.0) / 8.0


def derivative_table():
    result = np.zeros((5, 5))
    for i in range(5):
        for j in range(5):
            if i != j:
                result[i, j] = (
                    legendre_four(gll_points[i])
                    / legendre_four(gll_points[j])
                    / (gll_points[i] - gll_points[j])
                )
    result[0, 0] = -5.0
    result[4, 4] = 5.0
    return result


TABLE = derivative_table().astype(np.float32)


def pressures(fields, buoyancy):
    press_one = buoyancy * (fields[0] + fields[1])
    press_two = upper_gravity * (density_ratio * fields[0] + fields[1])
    return jnp.concatenate([fields, press_one[None], press_two[None]], axis=0)


def advance(center, padded, drag_coefficient):
    ahead_x = padded[:, 2:, 1:-1]
    behind_x = padded[:, :-2, 1:-1]
    ahead_y = padded[:, 1:-1, 2:]
    behind_y = padded[:, 1:-1, :-2]
    slope_x = 0.5 * (ahead_x - behind_x)
    slope_y = 0.5 * (ahead_y - behind_y)
    spread = ahead_x + behind_x + ahead_y + behind_y - 4.0 * center
    flow_speed = jnp.sqrt(center[2] * center[2] + center[3] * center[3] + speed_floor)
    dense_depth = center[0] - flow_dt * (slope_x[2] + slope_y[3]) + diffusion * spread[0]
    light_depth = center[1] - flow_dt * (slope_x[4] + slope_y[5]) + diffusion * spread[1]
    dense_xmom = (
        center[2]
        - flow_dt
        * (
            slope_x[6]
            + drag_coefficient * flow_speed * center[2]
            + coupling * (center[2] - center[4])
        )
        + diffusion * spread[2]
    )
    dense_ymom = (
        center[3]
        - flow_dt
        * (
            slope_y[6]
            + drag_coefficient * flow_speed * center[3]
            + coupling * (center[3] - center[5])
        )
        + diffusion * spread[3]
    )
    light_xmom = (
        center[4]
        - flow_dt * (slope_x[7] + coupling * (center[4] - center[2]))
        + diffusion * spread[4]
    )
    light_ymom = (
        center[5]
        - flow_dt * (slope_y[7] + coupling * (center[5] - center[3]))
        + diffusion * spread[5]
    )
    return jnp.stack([dense_depth, light_depth, dense_xmom, dense_ymom, light_xmom, light_ymom])


def basal_traction(fields, buoyancy, drag_coefficient):
    flow_speed = jnp.sqrt(fields[2] * fields[2] + fields[3] * fields[3] + speed_floor)
    press_one = buoyancy * (fields[0] + fields[1])
    rubbing = load_factor * drag_coefficient * flow_speed
    return jnp.stack([rubbing * fields[2], rubbing * fields[3], -load_factor * press_one])


def weights_cube():
    cube = (
        gll_weights.reshape(5, 1, 1) * gll_weights.reshape(1, 5, 1) * gll_weights.reshape(1, 1, 5)
    )
    return jnp.asarray(cube.reshape(5, 5, 5, 1, 1, 1), jnp.float32)


def load_kernel(trac_ref, row_ref, col_ref, out_ref):
    slots = out_ref.shape[0]

    @pl.when(pl.program_id(0) == 0)
    def _():
        out_ref[...] = jnp.zeros(out_ref.shape, out_ref.dtype)

    def row_body(r, carry):
        for c0 in range(0, row_ref.shape[1], CHUNK):
            point_row = row_ref[pl.ds(r, 1), pl.ds(c0, CHUNK)]
            point_col = col_ref[pl.ds(r, 1), pl.ds(c0, CHUNK)]
            hit = lax.broadcasted_iota(jnp.int32, (ROW_PAD, CHUNK), 0) == point_row
            pieces = []
            for k in range(3):
                value = trac_ref[k, pl.ds(r, 1), pl.ds(c0, CHUNK)]
                high = value.astype(jnp.bfloat16).astype(jnp.float32)
                low = value - high
                pieces.append(jnp.where(hit, high, 0.0))
                pieces.append(jnp.where(hit, low, 0.0))
            weighted = jnp.concatenate(pieces, axis=0).astype(jnp.bfloat16)
            onehot = (
                lax.broadcasted_iota(jnp.int32, (slots, CHUNK), 0) == point_col
            ).astype(jnp.bfloat16)
            out_ref[...] += lax.dot_general(
                onehot,
                weighted,
                (((1,), (1,)), ((), ())),
                preferred_element_type=jnp.float32,
            )
        return carry

    lax.fori_loop(0, ROW_BLOCK, row_body, 0, unroll=True)


def load_table(trac, point_row, point_col, slots):
    rows, cols = point_row.shape
    return pl.pallas_call(
        load_kernel,
        grid=(rows // ROW_BLOCK,),
        in_specs=[
            pl.BlockSpec((3, ROW_BLOCK, cols), lambda g: (0, g, 0)),
            pl.BlockSpec((ROW_BLOCK, cols), lambda g: (g, 0)),
            pl.BlockSpec((ROW_BLOCK, cols), lambda g: (g, 0)),
        ],
        out_specs=pl.BlockSpec((slots, 6 * ROW_PAD), lambda g: (0, 0)),
        out_shape=jax.ShapeDtypeStruct((slots, 6 * ROW_PAD), jnp.float32),
        compiler_params=pltpu.CompilerParams(dimension_semantics=("arbitrary",)),
    )(trac, point_row, point_col)


def along(x, axis, transpose):
    table = TABLE.T if transpose else TABLE
    shape = [1] * (x.ndim + 1)
    shape[axis] = 5
    shape[axis + 1] = 5
    coefs = jnp.asarray(table.reshape(shape))
    return jnp.sum(coefs * jnp.expand_dims(x, axis), axis=axis + 1)


def internal_force(values, lame_first, shear_modulus):
    shape = values.shape
    merged = shape[:4] + (shape[4] * shape[5], shape[6])
    values = values.reshape(merged)
    lame_first = lame_first.reshape(merged[4:])
    shear_modulus = shear_modulus.reshape(merged[4:])
    weights_3d = weights_cube().reshape(5, 5, 5, 1, 1)
    gradients = [[along(values[i], j, False) for i in range(3)] for j in range(3)]
    divergence = gradients[0][0] + gradients[1][1] + gradients[2][2]
    forces = []
    for i in range(3):
        pulled = None
        for j in range(3):
            stress = shear_modulus * (gradients[j][i] + gradients[i][j])
            if i == j:
                stress = stress + lame_first * divergence
            term = along(weights_3d * stress, j, True)
            pulled = term if pulled is None else pulled + term
        forces.append(-pulled)
    return jnp.stack(forces).reshape(shape)


def shift_block(block, axis, forward):
    count = lax.axis_size(axis)
    pairs = [(i, i + 1) for i in range(count - 1)]
    if not forward:
        pairs = [(target, source) for source, target in pairs]
    return lax.ppermute(block, axis, pairs)


def shift_faces(low_face, high_face, dim, axis):
    count = lax.axis_size(axis)
    forward = [(i, i + 1) for i in range(count - 1)]
    backward = [(target, source) for source, target in forward]
    size = low_face.shape[dim]
    from_prev = lax.ppermute(lax.slice_in_dim(high_face, size - 1, size, axis=dim), axis, forward)
    from_next = lax.ppermute(lax.slice_in_dim(low_face, 0, 1, axis=dim), axis, backward)
    before = jnp.concatenate([from_prev, lax.slice_in_dim(high_face, 0, size - 1, axis=dim)], axis=dim)
    after = jnp.concatenate([lax.slice_in_dim(low_face, 1, size, axis=dim), from_next], axis=dim)
    return before, after


def assemble_dim(values, node_dim, elem_dim, axis):
    low_face = lax.index_in_dim(values, 0, node_dim, keepdims=False)
    high_face = lax.index_in_dim(values, 4, node_dim, keepdims=False)
    face_elem_dim = elem_dim - 1
    if axis is None:
        size = low_face.shape[face_elem_dim]
        zero = jnp.zeros_like(lax.slice_in_dim(low_face, 0, 1, axis=face_elem_dim))
        before = jnp.concatenate(
            [zero, lax.slice_in_dim(high_face, 0, size - 1, axis=face_elem_dim)], axis=face_elem_dim
        )
        after = jnp.concatenate(
            [lax.slice_in_dim(low_face, 1, size, axis=face_elem_dim), zero], axis=face_elem_dim
        )
    else:
        before, after = shift_faces(low_face, high_face, face_elem_dim, axis)
    new_low = jnp.expand_dims(low_face + before, node_dim)
    new_high = jnp.expand_dims(high_face + after, node_dim)
    middle = lax.slice_in_dim(values, 1, 4, axis=node_dim)
    return jnp.concatenate([new_low, middle, new_high], axis=node_dim)


def assemble(values):
    values = assemble_dim(values, 1, 5, "gx")
    values = assemble_dim(values, 2, 6, "gy")
    values = assemble_dim(values, 3, 4, None)
    return values


def per_device(
    flow_state,
    drag_coefficient,
    wet_mask,
    target_elem,
    target_node,
    displacement,
    previous,
    density,
    lame_first,
    shear_modulus,
):
    buoyancy = 1.0 - 0.6 * wet_mask.astype(jnp.float32)
    fields = flow_state
    depth = FLOW_STEPS
    cell_rows = fields.shape[1]
    cell_cols = fields.shape[2]
    bundle = jnp.concatenate([fields, buoyancy[None], drag_coefficient[None]], axis=0)
    first_force = internal_force(displacement, lame_first, shear_modulus)
    rows_widened = extended(bundle, (("gx", 1),), depth)
    rows_widened, first_force = lax.optimization_barrier((rows_widened, first_force))
    widened = extended(rows_widened, (("gy", 2),), depth)
    row_ids = lax.axis_index("gx") * cell_rows + jnp.arange(cell_rows + 2 * depth) - depth
    col_ids = lax.axis_index("gy") * cell_cols + jnp.arange(cell_cols + 2 * depth) - depth
    row_inside = (row_ids >= 0) & (row_ids < cell_rows * lax.axis_size("gx"))
    col_inside = (col_ids >= 0) & (col_ids < cell_cols * lax.axis_size("gy"))
    inside = (row_inside[:, None] & col_inside[None, :]).astype(jnp.float32)
    wide_fields = widened[:6]
    wide_buoyancy = widened[6]
    wide_drag = widened[7]
    for counter in range(FLOW_STEPS):
        stacked = pressures(wide_fields, wide_buoyancy)
        padded = jnp.pad(stacked, ((0, 0), (1, 1), (1, 1)))
        wide_fields = advance(stacked, padded, wide_drag) * inside[None]
    fields = wide_fields[:, depth : depth + cell_rows, depth : depth + cell_cols]
    traction = basal_traction(fields, buoyancy, drag_coefficient)
    mass_parts = density[None, None, None, None] * weights_cube()[None]
    joined = assemble_dim(jnp.concatenate([first_force, mass_parts], axis=0), 1, 5, "gx")
    traction, joined = lax.optimization_barrier((traction, joined))
    joined = assemble_dim(assemble_dim(joined, 2, 6, "gy"), 3, 4, None)
    block_rows = displacement.shape[5]
    block_cols = displacement.shape[6]
    devices_y = lax.axis_size("gy")
    surface_cols = block_cols * devices_y
    elem_row = target_elem // surface_cols
    elem_col = target_elem % surface_cols
    local_x = elem_row - block_rows * lax.axis_index("gx") + 1
    local_y = elem_col - block_cols * lax.axis_index("gy") + 1
    point_rows = 4 * (block_rows + 2) + 1
    point_cols = 4 * (block_cols + 2) + 1
    span_x = 4 * block_rows
    span_y = 4 * block_cols
    point_row = 4 * local_x + target_node // 5
    point_col = 4 * local_y + target_node % 5
    slots = -(-point_cols // 16) * 16
    grid = load_table(traction, point_row, point_col, slots)
    grid, joined = lax.optimization_barrier((grid, joined))
    grid = grid.reshape(slots, 3, 2, ROW_PAD)
    grid = grid[:, :, 0] + grid[:, :, 1]
    overlap_x = point_rows - span_x
    overlap_y = point_cols - span_y
    from_next = shift_block(grid[:, :, :overlap_x], "gx", False)
    from_prev = shift_block(grid[:, :, span_x:point_rows], "gx", True)
    grid = (
        grid
        + jnp.pad(from_next, ((0, 0), (0, 0), (span_x, ROW_PAD - point_rows)))
        + jnp.pad(from_prev, ((0, 0), (0, 0), (0, ROW_PAD - overlap_x)))
    )
    from_next = shift_block(grid[:overlap_y], "gy", False)
    from_prev = shift_block(grid[span_y:point_cols], "gy", True)
    grid = (
        grid
        + jnp.pad(from_next, ((span_y, slots - point_cols), (0, 0), (0, 0)))
        + jnp.pad(from_prev, ((0, slots - overlap_y), (0, 0), (0, 0)))
    )
    by_col = jnp.concatenate(
        [
            grid[4 : 4 + span_y].reshape(block_cols, 4, 3, ROW_PAD),
            grid[8 : 8 + span_y].reshape(block_cols, 4, 3, ROW_PAD)[:, 0:1],
        ],
        axis=1,
    )
    by_row = jnp.concatenate(
        [
            by_col[..., 4 : 4 + span_x].reshape(block_cols, 5, 3, block_rows, 4),
            by_col[..., 8 : 8 + span_x].reshape(block_cols, 5, 3, block_rows, 4)[..., 0:1],
        ],
        axis=-1,
    )
    surface_load = jnp.transpose(by_row, (2, 4, 1, 3, 0))
    surface_load = surface_load.reshape(3, 5, 5, 1, 1, block_rows, block_cols)
    layers = displacement.shape[4]
    load_padded = jnp.pad(
        surface_load,
        ((0, 0), (0, 0), (0, 0), (0, 4), (0, layers - 1), (0, 0), (0, 0)),
    )
    masses = joined[3:]
    current = displacement
    for counter in range(SOLID_STEPS):
        if counter == 0:
            force = joined[:3]
        else:
            force = assemble(internal_force(current, lame_first, shear_modulus))
        acceleration = (force + load_padded) / masses
        advanced = 2.0 * current - previous + solid_dt * solid_dt * acceleration
        previous = current
        current = advanced
    return (fields, current, previous)


def solution(mesh):
    return jax.shard_map(
        per_device,
        mesh=mesh,
        in_specs=(
            P(None, "gx", "gy"),
            P("gx", "gy"),
            P("gx", "gy"),
            P("gx", "gy"),
            P("gx", "gy"),
            P(None, None, None, None, None, "gx", "gy"),
            P(None, None, None, None, None, "gx", "gy"),
            P(None, "gx", "gy"),
            P(None, "gx", "gy"),
            P(None, "gx", "gy"),
        ),
        out_specs=(
            P(None, "gx", "gy"),
            P(None, None, None, None, None, "gx", "gy"),
            P(None, None, None, None, None, "gx", "gy"),
        ),
        check_vma=False,
    )
```
